32 devices in a mesh: groups: 2 (over x), blk: 8 (over z, y), inner: 2 (over core).
Axes of the slice: x: 2, y: 2, z: 4, core: 2. Of those that a mesh axis runs over, the one named last changes fastest.
Arguments:
- patch_rows: bfloat16 [24576, 1536], P(('groups', 'blk', 'inner')), parts along dimension 0, may hold values from -6 to 6
- owner_ids: int32 [24576, 1], P(('groups', 'blk', 'inner')), parts along dimension 0, may hold values from 0 to 7; in each aligned block of 768 rows (0 to 767, 768 to 1535, ...) at most 192 rows name the same one
- page_ids: int32 [24576], P(('groups', 'blk', 'inner')), parts along dimension 0, may hold values from 0 to 7
- proj_weight: bfloat16 [1536, 128], replicated, may hold values from -0.15625 to 0.15625
- proj_bias: float32 [128], replicated, may hold values from -1.8 to 1.8
- query_tokens: bfloat16 [128, 32, 128], P(('groups', 'blk')), parts along dimension 0, may hold values from -0.5 to 0.5
- query_counts: int32 [128], P(('groups', 'blk')), parts along dimension 0, may hold values from 1 to 32, as said below
Outputs:
- page_scores: float32 [256, 64], P(('groups', 'blk', 'inner')), parts along dimension 0
The draws below stay inside these ranges and needn't reach their ends.
There are 2 independent parts, one for each index of `groups`. The reference program is written for one: setup_inputs(seed, part) draws one part's arguments, and reference() takes and returns one part's arrays. A program takes and returns all parts, laid end to end along the dimension named above; an argument that names none is the same for every part. Nothing has to cross between parts.
Inputs may be any that keep to these rules, and one draw needn't show every extreme that they name: `owner_ids`: among the rows of one device, at most 192 name the same owner, a bound that some block reaches of them. `query_counts`: the first query of each part has all 32 tokens live.
All inputs are finite; a program needn't handle non-finite values.
Results may differ from the reference program's by a relative error of at most 0.00031.
Values may be sent and summed in bfloat16 or wider, within the bound.
No kernel may reach another device: no remote copies, remote signals or barrier semaphores. Data moves between devices by JAX's collectives and lax.ppermute only.
A program may use at most 64 MiB of HBM per device.

```python
import math
import jax
import jax.numpy as jnp
import numpy as np
from jax import lax

F = 1536
E = 128
PATCH_DEV = 768
QTOK = 32
PAGES_DEV = 8
CAP = 192
PATCHES = 12288
QUERIES = 64
N_BLK = 8
N_INNER = 2


def draw_query_counts(key, part):
    counts = jax.random.randint(key, (QUERIES,), 1, QTOK + 1, dtype=jnp.int32)
    return counts.at[0].set(QTOK)


def touch_ends(array, stream_key, least, high):
    dims = array.shape
    spot = [jax.random.randint(jax.random.fold_in(stream_key, axis), (), 0, dims[axis]) for axis in range(len(dims))]
    array = array.at[tuple(spot)].set(least)
    longest = dims.index(max(dims))
    spot[longest] = (spot[longest] + 1) % dims[longest]
    return array.at[tuple(spot)].set(high)


def steps_of(own_key, shape, split, least, largest):
    level = 1.0
    for position, shards_of in split:
        heights = jax.random.uniform(jax.random.fold_in(jax.random.fold_in(own_key, 6), position), (shards_of,), jnp.float32, least / len(split), largest / len(split))
        level = level * jnp.repeat(jnp.exp(heights), shape[position] // shards_of).reshape((-1,) + (1,) * (len(shape) - 1 - position))
    return level


def assign_block(rng, own, number, rows, number_of, top, reach, lean):
    order = jax.random.permutation(rng, number_of)
    packed, ordinary = load_shares(number_of, rows * top, reach, lean, True), load_shares(number_of, rows * top, reach, lean, False)
    places = jnp.arange(number_of)

    def named(tallies, turn):
        used = int((tallies > 0).sum())
        fixed = max(1, used // 4)
        moved = fixed + (places - fixed + turn * (used - fixed)) % max(1, number_of - fixed)
        return jnp.zeros((number_of,), jnp.int32).at[order[jnp.where(places < fixed, places, moved)]].set(jnp.asarray(tallies, jnp.int32))

    tallies = jnp.where(number % 4 == 0, named(packed, number // 4), named(ordinary, number - number // 4 - 1))
    mixed = jax.random.permutation(jax.random.fold_in(own, 3), number_of)
    giver, sink = mixed[0:number_of // 2 * 2:2], mixed[1:number_of // 2 * 2:2]
    slack = jnp.minimum(tallies[giver] - 1, reach - tallies[sink]) // 2
    slack = jnp.where((giver == order[0]) | (sink == order[0]) | (tallies[sink] == 0), 0, jnp.maximum(slack, 0))
    moved = jax.random.randint(jax.random.fold_in(own, 4), (number_of // 2,), 0, 1 << 20) % (slack + 1)
    tallies = tallies.at[giver].add(-moved).at[sink].add(moved)
    labels = jnp.searchsorted(jnp.cumsum(tallies), jnp.arange(rows * top), side="right").astype(jnp.int32)
    listing = labels.reshape(top, rows).T
    listing = listing[jax.random.permutation(jax.random.fold_in(own, 1), rows)]
    turn = jax.random.randint(jax.random.fold_in(own, 2), (rows, 1), 0, top)
    return jnp.take_along_axis(listing, (jnp.arange(top)[None, :] + turn) % top, axis=1)


def load_shares(number_of, total, bound, lean, full):
    weights = [(1 << 20) // math.isqrt(rank ** lean) + 1 for rank in range(1, number_of + 1)]
    largest = bound if full else min(bound, max(-(-total // number_of), total * weights[0] // sum(weights)))
    least = 1 if total - largest >= number_of - 1 else 0
    given, spare = [largest] + [least] * (number_of - 1), total - largest - least * (number_of - 1)
    while spare > 0:
        free = [i for i in range(1, number_of) if given[i] < largest] or [i for i in range(1, number_of) if given[i] < bound]
        whole, remaining = sum([weights[i] for i in free]), spare
        for i in free:
            more = min(bound - given[i], max(1, remaining * weights[i] // whole), spare)
            given[i] = given[i] + more
            spare = spare - more
    return np.array(given)


def gaussian(rng, extent, deviation, reach, shards=(), kind=jnp.bfloat16):
    values = jax.random.normal(rng, extent, jnp.float32) * deviation
    if len(shards) > 0:
        values = steps_of(rng, extent, shards, -0.22, 0.18) * values
    return jnp.clip(values, min=-reach, max=reach).astype(kind)


def setup_inputs(seed: int = 0, part: int = 0) -> dict:
    splits = jax.random.split(jax.random.key(seed), 8)
    part_splits = jax.random.split(jax.random.fold_in(splits[7], part), 8)
    patch_rows = gaussian(part_splits[0], (PATCHES, F), 1.0, 6.0, ((0, 16),))
    owner_ids_keys = jax.random.split(jax.random.fold_in(part_splits[1], 1), PATCHES // PATCH_DEV)
    owner_ids_turns = jax.random.permutation(jax.random.fold_in(part_splits[1], 3), PATCHES // PATCH_DEV)
    owner_ids = jax.vmap(lambda own, number: assign_block(jax.random.fold_in(part_splits[1], 2), own, number, PATCH_DEV, N_BLK, 1, CAP, 2))(owner_ids_keys, owner_ids_turns).reshape((PATCHES, 1))
    page_ids = touch_ends(jax.random.randint(part_splits[2], (PATCHES,), 0, PAGES_DEV), jax.random.fold_in(part_splits[2], 1), 0, PAGES_DEV - 1).astype(jnp.int32)
    proj_weight = gaussian(splits[3], (F, E), F ** -0.5, 0.15625)
    proj_bias = gaussian(splits[4], (E,), 0.3, 1.8, (), jnp.float32)
    query_tokens = gaussian(part_splits[5], (QUERIES, QTOK, E), 0.08, 0.5, ((0, 8),))
    query_counts = draw_query_counts(jax.random.fold_in(jax.random.fold_in(splits[7], part), 71), part)
    return dict(patch_rows=patch_rows, owner_ids=owner_ids, page_ids=page_ids, proj_weight=proj_weight, proj_bias=proj_bias, query_tokens=query_tokens, query_counts=query_counts)


def embed(rows, weight, bias):
    proj = jnp.dot(rows, weight, preferred_element_type=jnp.float32) + bias[None, :]
    scale = lax.rsqrt(lax.optimization_barrier(jnp.sum(proj * proj, axis=1, keepdims=True)) + 1e-06)
    return (proj * scale).astype(jnp.bfloat16)

def reference(patch_rows, owner_ids, page_ids, proj_weight, proj_bias, query_tokens, query_counts):
    devices_all = N_BLK * N_INNER
    slot_total = N_BLK * CAP
    embedded = embed(patch_rows, proj_weight, proj_bias)
    target = owner_ids[:, 0].reshape(devices_all, PATCH_DEV)
    onehot = (target[:, :, None] == jnp.arange(N_BLK, dtype=jnp.int32)[None, None, :]).astype(jnp.int32)
    before = lax.optimization_barrier(jnp.sum((jnp.cumsum(onehot, axis=1) - onehot) * onehot, axis=2))
    source = jnp.arange(devices_all, dtype=jnp.int32)[:, None]
    dest_dev = target * N_INNER + source % N_INNER
    flat = (dest_dev * slot_total + source // N_INNER * CAP + before).reshape(-1).astype(jnp.int32)
    boxes = jnp.zeros((devices_all * slot_total, E), jnp.bfloat16).at[flat].set(embedded)
    boxes = boxes.reshape(devices_all, slot_total, E)
    box_pages = jnp.full((devices_all * slot_total,), -1, jnp.int32).at[flat].set(page_ids.astype(jnp.int32))
    box_pages = box_pages.reshape(devices_all, slot_total)
    tokens = query_tokens.reshape(QUERIES * QTOK, E)
    live = (jnp.arange(QTOK, dtype=jnp.int32)[None, :] < query_counts[:, None]).astype(jnp.float32)

    def per_device(args):
        box, pages = args
        sims = jnp.dot(tokens, box.T, preferred_element_type=jnp.float32)
        best = jnp.stack([lax.optimization_barrier(jnp.max(jnp.where(pages[None, :] == page, sims, jnp.float32(-2.0)), axis=1)) for page in range(PAGES_DEV)], axis=0)
        best = best.reshape(PAGES_DEV, QUERIES, QTOK)
        return lax.optimization_barrier(jnp.sum(best * live[None, :, :], axis=2))
    scores = lax.map(per_device, (boxes, box_pages))
    return scores.reshape(devices_all * PAGES_DEV, QUERIES)
```

```python
import functools
import math

import jax
import jax.numpy as jnp
from jax import lax
from jax.experimental import pallas as pl
from jax.experimental.pallas import tpu as pltpu
from jax.sharding import PartitionSpec as P

PAGES_DEV = 8


def embed(rows, weight, bias):
    proj = jnp.dot(rows, weight, preferred_element_type=jnp.float32) + bias[None, :]
    scale = lax.rsqrt(jnp.sum(proj * proj, axis=1, keepdims=True) + 1e-06)
    return (proj * scale).astype(jnp.bfloat16)


def page_order(embedded, slot_pages, page_total):
    slots = slot_pages.shape[0]
    lane = 128
    blocks = slots // lane
    onehot = slot_pages[:, None] == jnp.arange(page_total, dtype=jnp.int32)[None, :]
    tiles = onehot.astype(jnp.bfloat16).reshape(blocks, lane, page_total)
    earlier = (jnp.arange(lane)[None, :] < jnp.arange(lane)[:, None]).astype(jnp.bfloat16)
    within = jnp.einsum("ij,bjp->bip", earlier, tiles, preferred_element_type=jnp.float32)
    block_total = jnp.sum(tiles.astype(jnp.float32), axis=1)
    block_start = jnp.cumsum(block_total, axis=0) - block_total
    rank_all = (within + block_start[:, None, :]).reshape(slots, page_total)
    flags = onehot.astype(jnp.float32)
    rank = jnp.sum(rank_all * flags, axis=1).astype(jnp.int32)
    counts = jnp.sum(onehot.astype(jnp.int32), axis=0)
    groups = (counts + 7) // 8
    group_start = jnp.cumsum(groups) - groups
    row_start = jnp.sum(flags * (group_start * 8).astype(jnp.float32)[None, :], axis=1).astype(jnp.int32)
    position = jnp.where(slot_pages >= 0, row_start + rank, -1)
    ordered_rows = slots + 8 * page_total
    place = (position[:, None] == jnp.arange(ordered_rows, dtype=jnp.int32)[None, :]).astype(jnp.bfloat16)
    ordered = lax.dot_general(place, embedded, (((0,), (0,)), ((), ())), preferred_element_type=jnp.float32)
    table = jnp.concatenate([group_start, counts // 8, counts % 8]).astype(jnp.int32)
    return ordered.astype(jnp.bfloat16), table


def best_kernel(page_total, table_ref, rows_ref, tokens_ref, best_ref, sims_ref):
    sims_ref[...] = lax.dot_general(
        rows_ref[...], tokens_ref[...], (((1,), (1,)), ((), ())), preferred_element_type=jnp.float32
    )
    width = sims_ref.shape[1]
    sub = lax.broadcasted_iota(jnp.int32, (8, width), 0)
    for page in range(page_total):
        first = table_ref[page]
        full = table_ref[page_total + page]
        tail = table_ref[2 * page_total + page]

        def step(group, carry):
            start = pl.multiple_of((first + group) * 8, 8)
            return jnp.maximum(carry, sims_ref[pl.ds(start, 8), :])

        carry = lax.fori_loop(0, full, step, jnp.full((8, width), -2.0, jnp.float32))
        last = sims_ref[pl.ds(pl.multiple_of((first + full) * 8, 8), 8), :]
        carry = jnp.maximum(carry, jnp.where(sub < tail, last, jnp.float32(-2.0)))
        best_ref[page : page + 1, :] = jnp.max(carry, axis=0, keepdims=True)


def page_best(ordered, table, tokens, page_total):
    ordered_rows, width = ordered.shape
    token_total = tokens.shape[0]
    token_block = min(token_total, 1024)
    return pl.pallas_call(
        functools.partial(best_kernel, page_total),
        out_shape=jax.ShapeDtypeStruct((page_total, token_total), jnp.float32),
        grid_spec=pltpu.PrefetchScalarGridSpec(
            num_scalar_prefetch=1,
            grid=(token_total // token_block,),
            in_specs=[
                pl.BlockSpec((ordered_rows, width), lambda i, table: (0, 0)),
                pl.BlockSpec((token_block, width), lambda i, table: (i, 0)),
            ],
            out_specs=pl.BlockSpec((page_total, token_block), lambda i, table: (0, i)),
            scratch_shapes=[pltpu.VMEM((ordered_rows, token_block), jnp.float32)],
        ),
        cost_estimate=pl.CostEstimate(
            flops=2 * ordered_rows * token_total * width,
            bytes_accessed=2 * (ordered_rows + token_total) * width + 4 * page_total * token_total,
            transcendentals=0,
        ),
    )(table, ordered, tokens)


def dispatch(target, page_ids, local, owners, capacity):
    rows = target.shape[0]
    slot_count = owners * capacity
    onehot = (target[:, None] == jnp.arange(owners, dtype=jnp.int32)[None, :]).astype(jnp.bfloat16)
    earlier = (jnp.arange(rows)[None, :] < jnp.arange(rows)[:, None]).astype(jnp.bfloat16)
    seen = jnp.dot(earlier, onehot, preferred_element_type=jnp.float32)
    before = jnp.sum(seen * onehot.astype(jnp.float32), axis=1).astype(jnp.int32)
    slot_index = target * capacity + before
    placed = (slot_index[:, None] == jnp.arange(slot_count, dtype=jnp.int32)[None, :]).astype(jnp.bfloat16)
    packed = lax.dot_general(placed, local, (((0,), (0,)), ((), ())), preferred_element_type=jnp.float32)
    page_column = jnp.broadcast_to((page_ids + 1).astype(jnp.bfloat16)[:, None], (rows, 128))
    paged = lax.dot_general(placed, page_column, (((0,), (0,)), ((), ())), preferred_element_type=jnp.float32)
    slot_pages = paged[:, 0].astype(jnp.int32) - 1
    return packed.astype(jnp.bfloat16), slot_pages


def shards(patch_rows, owner_ids, page_ids, proj_weight, proj_bias, query_tokens, query_counts):
    owners = lax.axis_size("blk")
    halves = lax.axis_size("inner")
    rows = patch_rows.shape[0]
    capacity = 2 * rows // owners
    slot_count = owners * capacity
    local = embed(patch_rows, proj_weight, proj_bias)
    packed, outgoing_pages = dispatch(owner_ids[:, 0], page_ids, local, owners, capacity)
    per_block = query_tokens.shape[0]
    token_slots = query_tokens.shape[1]
    width = query_tokens.shape[2]
    total_queries = per_block * owners
    half_queries = per_block // halves
    query_rows = half_queries * token_slots
    page_rows = -(-capacity // width)
    count_rows = -(-per_block // width)
    used = query_rows + capacity + page_rows + count_rows
    message_rows = -(-used // 16) * 16
    own_half = lax.dynamic_slice_in_dim(query_tokens, lax.axis_index("inner") * half_queries, half_queries, axis=0)
    pages_part = jnp.pad(
        outgoing_pages.reshape(owners, capacity), ((0, 0), (0, page_rows * width - capacity)), constant_values=-1
    ).astype(jnp.bfloat16)
    counts_part = jnp.pad(query_counts, (0, count_rows * width - per_block)).astype(jnp.bfloat16)
    message = jnp.concatenate(
        [
            jnp.broadcast_to(own_half.reshape(1, query_rows, width), (owners, query_rows, width)),
            packed.reshape(owners, capacity, width),
            pages_part.reshape(owners, page_rows, width),
            jnp.broadcast_to(counts_part.reshape(1, count_rows, width), (owners, count_rows, width)),
            jnp.zeros((owners, message_rows - used, width), jnp.bfloat16),
        ],
        axis=1,
    )
    received = lax.all_to_all(message, "blk", split_axis=0, concat_axis=0, tiled=True)
    halves_in = lax.all_gather(received[:, :query_rows], "inner", axis=1, tiled=True)
    tokens = halves_in.reshape(total_queries, token_slots, width)
    embedded = received[:, query_rows : query_rows + capacity].reshape(slot_count, width)
    at = query_rows + capacity
    slot_pages = (
        received[:, at : at + page_rows].reshape(owners, page_rows * width)[:, :capacity].astype(jnp.int32)
    ).reshape(slot_count)
    at = at + page_rows
    counts = (
        received[:, at : at + count_rows].reshape(owners, count_rows * width)[:, :per_block].astype(jnp.int32)
    ).reshape(total_queries)
    ordered, table = page_order(embedded, slot_pages, PAGES_DEV)
    best = page_best(ordered, table, tokens.reshape(total_queries * token_slots, width), PAGES_DEV)
    live = (jnp.arange(token_slots, dtype=jnp.int32)[None, :] < counts[:, None]).astype(jnp.float32)
    return jnp.sum(best.reshape(PAGES_DEV, total_queries, token_slots) * live[None, :, :], axis=2)


def solution(mesh):
    in_specs = (
        P(("groups", "blk", "inner"), None),
        P(("groups", "blk", "inner"), None),
        P(("groups", "blk", "inner")),
        P(),
        P(),
        P(("groups", "blk"), None, None),
        P(("groups", "blk")),
    )
    out_specs = P(("groups", "blk", "inner"), None)
    return jax.shard_map(shards, mesh=mesh, in_specs=in_specs, out_specs=out_specs, check_vma=False)
```

```python
import functools
import math

import jax
import jax.numpy as jnp
from jax import lax
from jax.experimental import pallas as pl
from jax.experimental.pallas import tpu as pltpu
from jax.sharding import PartitionSpec as P

PAGES_DEV = 8


def embed(rows, weight, bias):
    proj = jnp.dot(rows, weight, preferred_element_type=jnp.float32) + bias[None, :]
    scale = lax.rsqrt(jnp.sum(proj * proj, axis=1, keepdims=True) + 1e-06)
    return (proj * scale).astype(jnp.bfloat16)


def page_positions(slot_pages, page_total, run):
    slots = slot_pages.shape[0]
    lane = 128
    blocks = slots // lane
    onehot = slot_pages[:, None] == jnp.arange(page_total, dtype=jnp.int32)[None, :]
    tiles = onehot.astype(jnp.bfloat16).reshape(blocks, lane, page_total)
    earlier = (jnp.arange(lane)[None, :] < jnp.arange(lane)[:, None]).astype(jnp.bfloat16)
    within = jnp.einsum("ij,bjp->bip", earlier, tiles, preferred_element_type=jnp.float32)
    block_total = jnp.sum(tiles.astype(jnp.float32), axis=1)
    block_start = jnp.cumsum(block_total, axis=0) - block_total
    rank_all = (within + block_start[:, None, :]).reshape(slots, page_total)
    flags = onehot.astype(jnp.float32)
    rank = jnp.sum(rank_all * flags, axis=1).astype(jnp.int32)
    counts = jnp.sum(onehot.astype(jnp.int32), axis=0)
    padded = (counts + run - 1) // run * run
    first = jnp.cumsum(padded) - padded
    row_start = jnp.sum(flags * first.astype(jnp.float32)[None, :], axis=1).astype(jnp.int32)
    position = jnp.where(slot_pages >= 0, row_start + rank, -1)
    table = jnp.concatenate([first, counts // run, counts % run]).astype(jnp.int32)
    return position, table


def score_kernel(page_total, token_slots, query_rows, token_block, table_ref, received_ref, tokens_ref, position_ref,
                 counts_ref, out_ref, ordered_ref, sims_ref):
    owners, chunk_rows = position_ref.shape
    ordered_rows, width = ordered_ref.shape
    total_queries = out_ref.shape[1]
    target = lax.broadcasted_iota(jnp.int32, (ordered_rows, chunk_rows), 0)
    ordered = jnp.zeros((ordered_rows, width), jnp.float32)
    for chunk in range(owners):
        place = (position_ref[chunk : chunk + 1, :] == target).astype(jnp.bfloat16)
        rows = received_ref[chunk, query_rows : query_rows + chunk_rows, :]
        ordered = ordered + jnp.dot(place, rows, preferred_element_type=jnp.float32)
    ordered_ref[...] = ordered.astype(jnp.bfloat16)
    sources = token_block // tokens_ref.shape[1]
    sub = lax.broadcasted_iota(jnp.int32, (8, token_block), 0)
    token_id = lax.broadcasted_iota(jnp.int32, (token_block, total_queries), 0)
    query_id = lax.broadcasted_iota(jnp.int32, (token_block, total_queries), 1)

    def block_scores(block, total):
        tokens = tokens_ref[pl.ds(block * sources, sources)].reshape(token_block, width)
        sims_ref[...] = lax.dot_general(
            ordered_ref[...], tokens, (((1,), (1,)), ((), ())), preferred_element_type=jnp.float32
        )
        best_rows = []
        for page in range(page_total):
            first = table_ref[page]
            whole = table_ref[page_total + page]
            rest = table_ref[2 * page_total + page]

            def step(i, carry):
                start = pl.multiple_of(first + i * 16, 16)
                return (
                    jnp.maximum(carry[0], sims_ref[pl.ds(start, 8), :]),
                    jnp.maximum(carry[1], sims_ref[pl.ds(start + 8, 8), :]),
                )

            floor = jnp.full((8, token_block), -2.0, jnp.float32)
            low, high = lax.fori_loop(0, whole, step, (floor, floor))
            start = pl.multiple_of(first + whole * 16, 16)
            low = jnp.maximum(low, jnp.where(sub < rest, sims_ref[pl.ds(start, 8), :], jnp.float32(-2.0)))
            high = jnp.maximum(high, jnp.where(sub + 8 < rest, sims_ref[pl.ds(start + 8, 8), :], jnp.float32(-2.0)))
            best_rows.append(jnp.max(jnp.maximum(low, high), axis=0, keepdims=True))
        best = jnp.concatenate(best_rows, axis=0)
        token = token_id + block * token_block
        live = ((token // token_slots) == query_id) & ((token % token_slots) < counts_ref[...])
        return total + jnp.dot(
            best, live.astype(jnp.float32), precision=lax.Precision.HIGHEST, preferred_element_type=jnp.float32
        )

    blocks = tokens_ref.shape[0] * tokens_ref.shape[1] // token_block
    out_ref[...] = lax.fori_loop(
        0, blocks, block_scores, jnp.zeros((page_total, total_queries), jnp.float32)
    )


def page_scores(received, tokens, position, table, counts, page_total, token_slots, query_rows):
    owners, chunk_rows = position.shape
    width = received.shape[2]
    ordered_rows = owners * chunk_rows + 16 * page_total + 16
    token_total = tokens.shape[0] * tokens.shape[1]
    total_queries = counts.shape[1]
    token_block = min(token_total, 1024)
    vmem = pl.BlockSpec(memory_space=pltpu.VMEM)
    return pl.pallas_call(
        functools.partial(score_kernel, page_total, token_slots, query_rows, token_block),
        out_shape=jax.ShapeDtypeStruct((page_total, total_queries), jnp.float32),
        in_specs=[pl.BlockSpec(memory_space=pltpu.SMEM), vmem, vmem, vmem, vmem],
        out_specs=vmem,
        scratch_shapes=[
            pltpu.VMEM((ordered_rows, width), jnp.bfloat16),
            pltpu.VMEM((ordered_rows, token_block), jnp.float32),
        ],
        cost_estimate=pl.CostEstimate(
            flops=2 * ordered_rows * width * (owners * chunk_rows + token_total),
            bytes_accessed=2 * received.size + 2 * tokens.size + 4 * page_total * total_queries,
            transcendentals=0,
        ),
    )(table, received, tokens, position, counts)


def dispatch(target, page_ids, local, owners, capacity):
    rows = target.shape[0]
    slot_count = owners * capacity
    onehot = (target[:, None] == jnp.arange(owners, dtype=jnp.int32)[None, :]).astype(jnp.bfloat16)
    earlier = (jnp.arange(rows)[None, :] < jnp.arange(rows)[:, None]).astype(jnp.bfloat16)
    seen = jnp.dot(earlier, onehot, preferred_element_type=jnp.float32)
    before = jnp.sum(seen * onehot.astype(jnp.float32), axis=1).astype(jnp.int32)
    slot_index = target * capacity + before
    placed = (slot_index[:, None] == jnp.arange(slot_count, dtype=jnp.int32)[None, :]).astype(jnp.bfloat16)
    packed = lax.dot_general(placed, local, (((0,), (0,)), ((), ())), preferred_element_type=jnp.float32)
    page_column = jnp.broadcast_to((page_ids + 1).astype(jnp.bfloat16)[:, None], (rows, 128))
    paged = lax.dot_general(placed, page_column, (((0,), (0,)), ((), ())), preferred_element_type=jnp.float32)
    slot_pages = paged[:, 0].astype(jnp.int32) - 1
    return packed.astype(jnp.bfloat16), slot_pages


def shards(patch_rows, owner_ids, page_ids, proj_weight, proj_bias, query_tokens, query_counts):
    owners = lax.axis_size("blk")
    halves = lax.axis_size("inner")
    rows = patch_rows.shape[0]
    capacity = 2 * rows // owners
    slot_count = owners * capacity
    local = embed(patch_rows, proj_weight, proj_bias)
    packed, outgoing_pages = dispatch(owner_ids[:, 0], page_ids, local, owners, capacity)
    per_block = query_tokens.shape[0]
    token_slots = query_tokens.shape[1]
    width = query_tokens.shape[2]
    total_queries = per_block * owners
    half_queries = per_block // halves
    query_rows = half_queries * token_slots
    page_rows = -(-capacity // width)
    count_rows = -(-per_block // width)
    used = query_rows + capacity + page_rows + count_rows
    message_rows = -(-used // 16) * 16
    own_half = lax.dynamic_slice_in_dim(query_tokens, lax.axis_index("inner") * half_queries, half_queries, axis=0)
    pages_part = jnp.pad(
        outgoing_pages.reshape(owners, capacity), ((0, 0), (0, page_rows * width - capacity)), constant_values=-1
    ).astype(jnp.bfloat16)
    counts_part = jnp.pad(query_counts, (0, count_rows * width - per_block)).astype(jnp.bfloat16)
    message = jnp.concatenate(
        [
            jnp.broadcast_to(own_half.reshape(1, query_rows, width), (owners, query_rows, width)),
            packed.reshape(owners, capacity, width),
            pages_part.reshape(owners, page_rows, width),
            jnp.broadcast_to(counts_part.reshape(1, count_rows, width), (owners, count_rows, width)),
            jnp.zeros((owners, message_rows - used, width), jnp.bfloat16),
        ],
        axis=1,
    )
    received = lax.all_to_all(message, "blk", split_axis=0, concat_axis=0, tiled=True)
    halves_in = lax.all_gather(received[:, :query_rows], "inner", axis=1, tiled=True)
    at = query_rows + capacity
    slot_pages = (
        received[:, at : at + page_rows].reshape(owners, page_rows * width)[:, :capacity].astype(jnp.int32)
    ).reshape(slot_count)
    at = at + page_rows
    counts = (
        received[:, at : at + count_rows].reshape(owners, count_rows * width)[:, :per_block].astype(jnp.int32)
    ).reshape(1, total_queries)
    position, table = page_positions(slot_pages, PAGES_DEV, 16)
    return page_scores(
        received, halves_in, position.reshape(owners, capacity), table, counts, PAGES_DEV, token_slots, query_rows
    )


def solution(mesh):
    in_specs = (
        P(("groups", "blk", "inner"), None),
        P(("groups", "blk", "inner"), None),
        P(("groups", "blk", "inner")),
        P(),
        P(),
        P(("groups", "blk"), None, None),
        P(("groups", "blk")),
    )
    out_specs = P(("groups", "blk", "inner"), None)
    return jax.shard_map(shards, mesh=mesh, in_specs=in_specs, out_specs=out_specs, check_vma=False)
```

```python
import functools
import math

import jax
import jax.numpy as jnp
from jax import lax
from jax.experimental import pallas as pl
from jax.experimental.pallas import tpu as pltpu
from jax.sharding import PartitionSpec as P

PAGES_DEV = 8


def embed(rows, weight, bias):
    proj = jnp.dot(rows, weight, preferred_element_type=jnp.float32) + bias[None, :]
    scale = lax.rsqrt(jnp.sum(proj * proj, axis=1, keepdims=True) + 1e-06)
    return (proj * scale).astype(jnp.bfloat16)


def send_kernel(page_total, capacity, query_rows, block_at, meta_ref, rows_ref, weight_ref, bias_ref, half_ref,
                message_ref):
    owners = message_ref.shape[0]
    rows = rows_ref.shape[0]
    proj = jnp.dot(rows_ref[...], weight_ref[...], preferred_element_type=jnp.float32) + bias_ref[...]
    scale = lax.rsqrt(jnp.sum(proj * proj, axis=1, keepdims=True) + 1e-06)
    local = (proj * scale).astype(jnp.bfloat16)
    combo = meta_ref[0:1, :] * page_total + meta_ref[1:2, :]
    combos = -(-owners * page_total // 128) * 128
    combo_id = lax.broadcasted_iota(jnp.int32, (combos, rows), 0)
    onehot = (combo == combo_id).astype(jnp.bfloat16)
    earlier = (
        lax.broadcasted_iota(jnp.int32, (rows, rows), 0) < lax.broadcasted_iota(jnp.int32, (rows, rows), 1)
    ).astype(jnp.bfloat16)
    seen = jnp.dot(onehot, earlier, preferred_element_type=jnp.float32)
    count = jnp.sum(onehot.astype(jnp.float32), axis=1, keepdims=True)
    row_id = lax.broadcasted_iota(jnp.int32, (combos, combos), 0)
    col_id = lax.broadcasted_iota(jnp.int32, (combos, combos), 1)
    same_owner_lower = (row_id // page_total == col_id // page_total) & (col_id % page_total < row_id % page_total)
    offset = jnp.dot(same_owner_lower.astype(jnp.bfloat16), count.astype(jnp.bfloat16),
                     preferred_element_type=jnp.float32)
    base = (lax.broadcasted_iota(jnp.int32, (combos, 1), 0) // page_total * capacity).astype(jnp.float32) + offset
    slot = jnp.sum(onehot.astype(jnp.float32) * (base + seen), axis=0, keepdims=True).astype(jnp.int32)
    count_rows = [
        lax.dot_general(
            jnp.ones((1, rows), jnp.bfloat16), onehot[group * 128 : (group + 1) * 128],
            (((1,), (1,)), ((), ())), preferred_element_type=jnp.float32,
        )
        for group in range(combos // 128)
    ]
    block_rows = message_ref.shape[1] - block_at
    block = jnp.concatenate(
        count_rows
        + [meta_ref[2:3, 0:128].astype(jnp.float32), jnp.zeros((block_rows - len(count_rows) - 1, 128), jnp.float32)],
        axis=0,
    ).astype(jnp.bfloat16)
    slot_id = lax.broadcasted_iota(jnp.int32, (capacity, rows), 0)
    for owner in range(owners):
        placed = (slot == slot_id + owner * capacity).astype(jnp.bfloat16)
        message_ref[owner, 0:query_rows, :] = half_ref[...]
        message_ref[owner, query_rows : query_rows + capacity, :] = jnp.dot(
            placed, local, preferred_element_type=jnp.float32
        ).astype(jnp.bfloat16)
        message_ref[owner, block_at:, :] = block


def send_message(patch_rows, owner_ids, page_ids, proj_weight, proj_bias, own_half, query_counts, owners, capacity):
    rows, features = patch_rows.shape
    query_rows, width = own_half.shape
    block_at = -(-(query_rows + capacity) // 16) * 16
    meta = jnp.concatenate(
        [owner_ids.reshape(1, rows), page_ids.reshape(1, rows), jnp.pad(query_counts, (0, rows - query_counts.shape[0])).reshape(1, rows)],
        axis=0,
    )
    vmem = pl.BlockSpec(memory_space=pltpu.VMEM)
    return pl.pallas_call(
        functools.partial(send_kernel, PAGES_DEV, capacity, query_rows, block_at),
        out_shape=jax.ShapeDtypeStruct((owners, block_at + 16, width), jnp.bfloat16),
        in_specs=[vmem] * 5,
        out_specs=vmem,
        cost_estimate=pl.CostEstimate(
            flops=2 * rows * width * (features + owners * capacity),
            bytes_accessed=2 * (rows * features + features * width + owners * (block_at + 16) * width),
            transcendentals=rows,
        ),
    )(meta, patch_rows, proj_weight, proj_bias.reshape(1, width), own_half)


def score_kernel(page_total, token_slots, query_rows, token_block, table_ref, received_ref, tokens_ref, counts_ref,
                 out_ref, ordered_ref, sims_ref):
    owners = received_ref.shape[0]
    ordered_rows, width = ordered_ref.shape
    capacity = (ordered_rows - 16 * page_total - 16) // owners
    total_queries = out_ref.shape[1]
    totals = [sum(table_ref[chunk * page_total + page] for chunk in range(owners)) for page in range(page_total)]
    firsts = []
    at = 0
    for page in range(page_total):
        firsts.append(at)
        at = at + (totals[page] + 15) // 16 * 16
    target = lax.broadcasted_iota(jnp.int32, (ordered_rows, capacity), 0)
    slot = lax.broadcasted_iota(jnp.int32, (1, capacity), 1)
    ordered = jnp.zeros((ordered_rows, width), jnp.float32)
    before = [0] * page_total
    for chunk in range(owners):
        position = jnp.full((1, capacity), -1, jnp.int32)
        low = 0
        for page in range(page_total):
            high = low + table_ref[chunk * page_total + page]
            inside = (slot >= low) & (slot < high)
            position = jnp.where(inside, slot + (firsts[page] + before[page] - low), position)
            before[page] = before[page] + (high - low)
            low = high
        place = (position == target).astype(jnp.bfloat16)
        rows = received_ref[chunk, query_rows : query_rows + capacity, :]
        ordered = ordered + jnp.dot(place, rows, preferred_element_type=jnp.float32)
    ordered_ref[...] = ordered.astype(jnp.bfloat16)
    sources = token_block // tokens_ref.shape[1]
    sub = lax.broadcasted_iota(jnp.int32, (8, token_block), 0)
    token_id = lax.broadcasted_iota(jnp.int32, (token_block, total_queries), 0)
    query_id = lax.broadcasted_iota(jnp.int32, (token_block, total_queries), 1)

    def block_scores(block, total):
        tokens = tokens_ref[pl.ds(block * sources, sources)].reshape(token_block, width)
        sims_ref[...] = lax.dot_general(
            ordered_ref[...], tokens, (((1,), (1,)), ((), ())), preferred_element_type=jnp.float32
        )
        best_rows = []
        for page in range(page_total):
            first = firsts[page]
            whole = totals[page] // 16
            rest = totals[page] % 16

            def step(i, carry):
                start = pl.multiple_of(first + i * 16, 16)
                return (
                    jnp.maximum(carry[0], sims_ref[pl.ds(start, 8), :]),
                    jnp.maximum(carry[1], sims_ref[pl.ds(start + 8, 8), :]),
                )

            floor = jnp.full((8, token_block), -2.0, jnp.float32)
            low, high = lax.fori_loop(0, whole, step, (floor, floor))
            start = pl.multiple_of(first + whole * 16, 16)
            low = jnp.maximum(low, jnp.where(sub < rest, sims_ref[pl.ds(start, 8), :], jnp.float32(-2.0)))
            high = jnp.maximum(high, jnp.where(sub + 8 < rest, sims_ref[pl.ds(start + 8, 8), :], jnp.float32(-2.0)))
            best_rows.append(jnp.max(jnp.maximum(low, high), axis=0, keepdims=True))
        best = jnp.concatenate(best_rows, axis=0)
        token = token_id + block * token_block
        live = ((token // token_slots) == query_id) & ((token % token_slots) < counts_ref[...])
        return total + jnp.dot(
            best, live.astype(jnp.float32), precision=lax.Precision.HIGHEST, preferred_element_type=jnp.float32
        )

    blocks = tokens_ref.shape[0] * tokens_ref.shape[1] // token_block
    out_ref[...] = lax.fori_loop(
        0, blocks, block_scores, jnp.zeros((page_total, total_queries), jnp.float32)
    )


def page_scores(received, tokens, table, counts, page_total, token_slots, query_rows, capacity):
    owners = received.shape[0]
    width = received.shape[2]
    ordered_rows = owners * capacity + 16 * page_total + 16
    token_total = tokens.shape[0] * tokens.shape[1]
    total_queries = counts.shape[1]
    token_block = min(token_total, 1024)
    vmem = pl.BlockSpec(memory_space=pltpu.VMEM)
    return pl.pallas_call(
        functools.partial(score_kernel, page_total, token_slots, query_rows, token_block),
        out_shape=jax.ShapeDtypeStruct((page_total, total_queries), jnp.float32),
        in_specs=[pl.BlockSpec(memory_space=pltpu.SMEM), vmem, vmem, vmem],
        out_specs=vmem,
        scratch_shapes=[
            pltpu.VMEM((ordered_rows, width), jnp.bfloat16),
            pltpu.VMEM((ordered_rows, token_block), jnp.float32),
        ],
        cost_estimate=pl.CostEstimate(
            flops=2 * ordered_rows * width * (owners * capacity + token_total),
            bytes_accessed=2 * received.size + 2 * tokens.size + 4 * page_total * total_queries,
            transcendentals=0,
        ),
    )(table, received, tokens, counts)


def shards(patch_rows, owner_ids, page_ids, proj_weight, proj_bias, query_tokens, query_counts):
    owners = lax.axis_size("blk")
    halves = lax.axis_size("inner")
    rows = patch_rows.shape[0]
    capacity = 2 * rows // owners
    per_block = query_tokens.shape[0]
    token_slots = query_tokens.shape[1]
    width = query_tokens.shape[2]
    total_queries = per_block * owners
    half_queries = per_block // halves
    query_rows = half_queries * token_slots
    own_half = lax.dynamic_slice_in_dim(query_tokens, lax.axis_index("inner") * half_queries, half_queries, axis=0)
    message = send_message(
        patch_rows, owner_ids, page_ids, proj_weight, proj_bias, own_half.reshape(query_rows, width), query_counts,
        owners, capacity,
    )
    received = lax.all_to_all(message, "blk", split_axis=0, concat_axis=0, tiled=True)
    halves_in = lax.all_gather(received[:, :query_rows], "inner", axis=1, tiled=True)
    block_at = -(-(query_rows + capacity) // 16) * 16
    combos = -(-owners * PAGES_DEV // 128) * 128
    count_rows = combos // 128
    page_counts = received[:, block_at : block_at + count_rows].reshape(owners, combos)
    page_counts = lax.dynamic_slice_in_dim(page_counts, lax.axis_index("blk") * PAGES_DEV, PAGES_DEV, axis=1)
    table = page_counts.astype(jnp.int32).reshape(owners * PAGES_DEV)
    counts = received[:, block_at + count_rows, :per_block].astype(jnp.int32).reshape(1, total_queries)
    return page_scores(received, halves_in, table, counts, PAGES_DEV, token_slots, query_rows, capacity)


def solution(mesh):
    in_specs = (
        P(("groups", "blk", "inner"), None),
        P(("groups", "blk", "inner"), None),
        P(("groups", "blk", "inner")),
        P(),
        P(),
        P(("groups", "blk"), None, None),
        P(("groups", "blk")),
    )
    out_specs = P(("groups", "blk", "inner"), None)
    return jax.shard_map(shards, mesh=mesh, in_specs=in_specs, out_specs=out_specs, check_vma=False)
```

```python
import functools
import math

import jax
import jax.numpy as jnp
from jax import lax
from jax.experimental import pallas as pl
from jax.experimental.pallas import tpu as pltpu
from jax.sharding import PartitionSpec as P

PAGES_DEV = 8


def send_kernel(page_total, capacity, query_rows, block_at, scalars_ref, owner_ref, page_ref, rows_ref, weight_ref,
                bias_ref, queries_ref, message_ref):
    owners = message_ref.shape[0]
    rows = rows_ref.shape[0]
    proj = jnp.dot(rows_ref[...], weight_ref[...], preferred_element_type=jnp.float32) + bias_ref[...]
    scale = lax.rsqrt(jnp.sum(proj * proj, axis=1, keepdims=True) + 1e-06)
    local = (proj * scale).astype(jnp.bfloat16)
    diagonal = lax.broadcasted_iota(jnp.int32, (rows, rows), 0) == lax.broadcasted_iota(jnp.int32, (rows, rows), 1)
    spread = jnp.where(diagonal, owner_ref[...].astype(jnp.float32), 0.0).astype(jnp.bfloat16)
    owner = lax.dot_general(
        jnp.ones((1, rows), jnp.bfloat16), spread, (((1,), (1,)), ((), ())), preferred_element_type=jnp.float32
    ).astype(jnp.int32)
    combo = owner * page_total + page_ref[...]
    combos = -(-owners * page_total // 128) * 128
    combo_id = lax.broadcasted_iota(jnp.int32, (combos, rows), 0)
    onehot = (combo == combo_id).astype(jnp.bfloat16)
    earlier = (
        lax.broadcasted_iota(jnp.int32, (rows, rows), 0) < lax.broadcasted_iota(jnp.int32, (rows, rows), 1)
    ).astype(jnp.bfloat16)
    seen = jnp.dot(onehot, earlier, preferred_element_type=jnp.float32)
    count = jnp.sum(onehot.astype(jnp.float32), axis=1, keepdims=True)
    row_id = lax.broadcasted_iota(jnp.int32, (combos, combos), 0)
    col_id = lax.broadcasted_iota(jnp.int32, (combos, combos), 1)
    same_owner_lower = (row_id // page_total == col_id // page_total) & (col_id % page_total < row_id % page_total)
    offset = jnp.dot(same_owner_lower.astype(jnp.bfloat16), count.astype(jnp.bfloat16),
                     preferred_element_type=jnp.float32)
    base = (lax.broadcasted_iota(jnp.int32, (combos, 1), 0) // page_total * capacity).astype(jnp.float32) + offset
    slot = jnp.sum(onehot.astype(jnp.float32) * (base + seen), axis=0, keepdims=True).astype(jnp.int32)
    count_rows = [
        lax.dot_general(
            jnp.ones((1, rows), jnp.bfloat16), onehot[group * 128 : (group + 1) * 128],
            (((1,), (1,)), ((), ())), preferred_element_type=jnp.float32,
        )
        for group in range(combos // 128)
    ]
    lane = lax.broadcasted_iota(jnp.int32, (1, 128), 1)
    query_count_row = jnp.zeros((1, 128), jnp.float32)
    for query in range(scalars_ref.shape[0] - 1):
        query_count_row = jnp.where(lane == query, scalars_ref[query + 1].astype(jnp.float32), query_count_row)
    block_rows = message_ref.shape[1] - block_at
    block = jnp.concatenate(
        count_rows
        + [query_count_row, jnp.zeros((block_rows - len(count_rows) - 1, 128), jnp.float32)],
        axis=0,
    ).astype(jnp.bfloat16)
    own_half = queries_ref[pl.ds(pl.multiple_of(scalars_ref[0] * query_rows, query_rows), query_rows), :]
    slot_id = lax.broadcasted_iota(jnp.int32, (capacity, rows), 0)
    for owner in range(owners):
        placed = (slot == slot_id + owner * capacity).astype(jnp.bfloat16)
        message_ref[owner, 0:query_rows, :] = own_half
        message_ref[owner, query_rows : query_rows + capacity, :] = jnp.dot(
            placed, local, preferred_element_type=jnp.float32
        ).astype(jnp.bfloat16)
        message_ref[owner, block_at:, :] = block


def send_message(patch_rows, owner_ids, page_ids, proj_weight, proj_bias, query_tokens, query_counts, owners, capacity,
                 halves):
    rows, features = patch_rows.shape
    per_block, token_slots, width = query_tokens.shape
    query_rows = per_block // halves * token_slots
    block_at = -(-(query_rows + capacity) // 16) * 16
    scalars = jnp.concatenate([lax.axis_index("inner").astype(jnp.int32).reshape(1), query_counts])
    vmem = pl.BlockSpec(memory_space=pltpu.VMEM)
    return pl.pallas_call(
        functools.partial(send_kernel, PAGES_DEV, capacity, query_rows, block_at),
        out_shape=jax.ShapeDtypeStruct((owners, block_at + 16, width), jnp.bfloat16),
        in_specs=[pl.BlockSpec(memory_space=pltpu.SMEM)] + [vmem] * 6,
        out_specs=vmem,
        cost_estimate=pl.CostEstimate(
            flops=2 * rows * width * (features + owners * capacity),
            bytes_accessed=2 * (rows * features + features * width + owners * (block_at + 16) * width),
            transcendentals=rows,
        ),
    )(
        scalars, owner_ids, page_ids.reshape(1, rows), patch_rows, proj_weight, proj_bias.reshape(1, width),
        query_tokens.reshape(per_block * token_slots, width),
    )


def score_kernel(page_total, token_slots, query_rows, token_block, table_ref, received_ref, tokens_ref, out_ref,
                 ordered_ref, sims_ref):
    owners = received_ref.shape[0]
    ordered_rows, width = ordered_ref.shape
    capacity = (ordered_rows - 16 * page_total - 16) // owners
    total_queries = out_ref.shape[1]
    totals = [sum(table_ref[chunk * page_total + page] for chunk in range(owners)) for page in range(page_total)]
    firsts = []
    at = 0
    for page in range(page_total):
        firsts.append(at)
        at = at + (totals[page] + 15) // 16 * 16
    target = lax.broadcasted_iota(jnp.int32, (ordered_rows, capacity), 0)
    slot = lax.broadcasted_iota(jnp.int32, (1, capacity), 1)
    ordered = jnp.zeros((ordered_rows, width), jnp.float32)
    before = [0] * page_total
    for chunk in range(owners):
        position = jnp.full((1, capacity), -1, jnp.int32)
        low = 0
        for page in range(page_total):
            high = low + table_ref[chunk * page_total + page]
            inside = (slot >= low) & (slot < high)
            position = jnp.where(inside, slot + (firsts[page] + before[page] - low), position)
            before[page] = before[page] + (high - low)
            low = high
        place = (position == target).astype(jnp.bfloat16)
        rows = received_ref[chunk, query_rows : query_rows + capacity, :]
        ordered = ordered + jnp.dot(place, rows, preferred_element_type=jnp.float32)
    ordered_ref[...] = ordered.astype(jnp.bfloat16)
    sources = token_block // tokens_ref.shape[1]
    sub = lax.broadcasted_iota(jnp.int32, (8, token_block), 0)
    query_lane = lax.broadcasted_iota(jnp.int32, (1, total_queries), 1)
    live_count = jnp.zeros((1, total_queries), jnp.int32)
    for query in range(total_queries):
        live_count = jnp.where(query_lane == query, table_ref[owners * page_total + query], live_count)
    token_id = lax.broadcasted_iota(jnp.int32, (token_block, total_queries), 0)
    query_id = lax.broadcasted_iota(jnp.int32, (token_block, total_queries), 1)

    def block_scores(block, total):
        tokens = tokens_ref[pl.ds(block * sources, sources)].reshape(token_block, width)
        sims_ref[...] = lax.dot_general(
            ordered_ref[...], tokens, (((1,), (1,)), ((), ())), preferred_element_type=jnp.float32
        )
        best_rows = []
        for page in range(page_total):
            first = firsts[page]
            whole = totals[page] // 16
            rest = totals[page] % 16

            def step(i, carry):
                start = pl.multiple_of(first + i * 16, 16)
                return (
                    jnp.maximum(carry[0], sims_ref[pl.ds(start, 8), :]),
                    jnp.maximum(carry[1], sims_ref[pl.ds(start + 8, 8), :]),
                )

            floor = jnp.full((8, token_block), -2.0, jnp.float32)
            low, high = lax.fori_loop(0, whole, step, (floor, floor))
            start = pl.multiple_of(first + whole * 16, 16)
            low = jnp.maximum(low, jnp.where(sub < rest, sims_ref[pl.ds(start, 8), :], jnp.float32(-2.0)))
            high = jnp.maximum(high, jnp.where(sub + 8 < rest, sims_ref[pl.ds(start + 8, 8), :], jnp.float32(-2.0)))
            best_rows.append(jnp.max(jnp.maximum(low, high), axis=0, keepdims=True))
        best = jnp.concatenate(best_rows, axis=0)
        token = token_id + block * token_block
        live = ((token // token_slots) == query_id) & ((token % token_slots) < live_count)
        return total + jnp.dot(
            best, live.astype(jnp.float32), precision=lax.Precision.HIGHEST, preferred_element_type=jnp.float32
        )

    blocks = tokens_ref.shape[0] * tokens_ref.shape[1] // token_block
    out_ref[...] = lax.fori_loop(
        0, blocks, block_scores, jnp.zeros((page_total, total_queries), jnp.float32)
    )


def page_scores(received, tokens, table, total_queries, page_total, token_slots, query_rows, capacity):
    owners = received.shape[0]
    width = received.shape[2]
    ordered_rows = owners * capacity + 16 * page_total + 16
    token_total = tokens.shape[0] * tokens.shape[1]
    token_block = min(token_total, 1024)
    vmem = pl.BlockSpec(memory_space=pltpu.VMEM)
    return pl.pallas_call(
        functools.partial(score_kernel, page_total, token_slots, query_rows, token_block),
        out_shape=jax.ShapeDtypeStruct((page_total, total_queries), jnp.float32),
        in_specs=[pl.BlockSpec(memory_space=pltpu.SMEM), vmem, vmem],
        out_specs=vmem,
        scratch_shapes=[
            pltpu.VMEM((ordered_rows, width), jnp.bfloat16),
            pltpu.VMEM((ordered_rows, token_block), jnp.float32),
        ],
        cost_estimate=pl.CostEstimate(
            flops=2 * ordered_rows * width * (owners * capacity + token_total),
            bytes_accessed=2 * received.size + 2 * tokens.size + 4 * page_total * total_queries,
            transcendentals=0,
        ),
    )(table, received, tokens)


def shards(patch_rows, owner_ids, page_ids, proj_weight, proj_bias, query_tokens, query_counts):
    owners = lax.axis_size("blk")
    halves = lax.axis_size("inner")
    rows = patch_rows.shape[0]
    capacity = 2 * rows // owners
    per_block = query_tokens.shape[0]
    token_slots = query_tokens.shape[1]
    width = query_tokens.shape[2]
    total_queries = per_block * owners
    half_queries = per_block // halves
    query_rows = half_queries * token_slots
    message = send_message(
        patch_rows, owner_ids, page_ids, proj_weight, proj_bias, query_tokens, query_counts, owners, capacity, halves
    )
    received = lax.all_to_all(message, "blk", split_axis=0, concat_axis=0, tiled=True)
    halves_in = lax.all_gather(received[:, :query_rows], "inner", axis=1, tiled=True)
    block_at = -(-(query_rows + capacity) // 16) * 16
    combos = -(-owners * PAGES_DEV // 128) * 128
    count_rows = combos // 128
    page_counts = received[:, block_at : block_at + count_rows].reshape(owners, combos)
    page_counts = lax.dynamic_slice_in_dim(page_counts, lax.axis_index("blk") * PAGES_DEV, PAGES_DEV, axis=1)
    counts = received[:, block_at + count_rows, :per_block]
    table = jnp.concatenate([page_counts.reshape(owners * PAGES_DEV), counts.reshape(total_queries)]).astype(jnp.int32)
    return page_scores(received, halves_in, table, total_queries, PAGES_DEV, token_slots, query_rows, capacity)


def solution(mesh):
    in_specs = (
        P(("groups", "blk", "inner"), None),
        P(("groups", "blk", "inner"), None),
        P(("groups", "blk", "inner")),
        P(),
        P(),
        P(("groups", "blk"), None, None),
        P(("groups", "blk")),
    )
    out_specs = P(("groups", "blk", "inner"), None)
    return jax.shard_map(shards, mesh=mesh, in_specs=in_specs, out_specs=out_specs, check_vma=False)
```

```python
import functools
import math

import jax
import jax.numpy as jnp
from jax import lax
from jax.experimental import pallas as pl
from jax.experimental.pallas import tpu as pltpu
from jax.sharding import PartitionSpec as P

PAGES_DEV = 8


def send_kernel(page_total, capacity, query_rows, block_at, query_counts_ref, owner_ref, page_ref, rows_ref, weight_ref,
                bias_ref, queries_ref, message_ref):
    owners = message_ref.shape[0]
    rows = rows_ref.shape[0]
    proj = jnp.dot(rows_ref[...], weight_ref[...], preferred_element_type=jnp.float32) + bias_ref[...]
    scale = lax.rsqrt(jnp.sum(proj * proj, axis=1, keepdims=True) + 1e-06)
    local = (proj * scale).astype(jnp.bfloat16)
    combo = owner_ref[...].reshape(1, rows) * page_total + page_ref[...].reshape(1, rows)
    combos = -(-owners * page_total // 128) * 128
    combo_id = lax.broadcasted_iota(jnp.int32, (combos, rows), 0)
    onehot = (combo == combo_id).astype(jnp.bfloat16)
    earlier = (
        lax.broadcasted_iota(jnp.int32, (rows, rows), 0) < lax.broadcasted_iota(jnp.int32, (rows, rows), 1)
    ).astype(jnp.bfloat16)
    seen = jnp.dot(onehot, earlier, preferred_element_type=jnp.float32)
    count = jnp.sum(onehot.astype(jnp.float32), axis=1, keepdims=True)
    row_id = lax.broadcasted_iota(jnp.int32, (combos, combos), 0)
    col_id = lax.broadcasted_iota(jnp.int32, (combos, combos), 1)
    same_owner_lower = (row_id // page_total == col_id // page_total) & (col_id % page_total < row_id % page_total)
    offset = jnp.dot(same_owner_lower.astype(jnp.bfloat16), count.astype(jnp.bfloat16),
                     preferred_element_type=jnp.float32)
    base = (lax.broadcasted_iota(jnp.int32, (combos, 1), 0) // page_total * capacity).astype(jnp.float32) + offset
    slot = jnp.sum(onehot.astype(jnp.float32) * (base + seen), axis=0, keepdims=True).astype(jnp.int32)
    count_rows = [
        lax.dot_general(
            jnp.ones((1, rows), jnp.bfloat16), onehot[group * 128 : (group + 1) * 128],
            (((1,), (1,)), ((), ())), preferred_element_type=jnp.float32,
        )
        for group in range(combos // 128)
    ]
    lane = lax.broadcasted_iota(jnp.int32, (1, 128), 1)
    query_count_row = jnp.zeros((1, 128), jnp.float32)
    for query in range(query_counts_ref.shape[0]):
        query_count_row = jnp.where(lane == query, query_counts_ref[query].astype(jnp.float32), query_count_row)
    block_rows = message_ref.shape[1] - block_at
    block = jnp.concatenate(
        count_rows
        + [query_count_row, jnp.zeros((block_rows - len(count_rows) - 1, 128), jnp.float32)],
        axis=0,
    ).astype(jnp.bfloat16)
    own_half = queries_ref[pl.ds(pl.multiple_of(lax.axis_index("inner") * query_rows, query_rows), query_rows), :]
    slot_id = lax.broadcasted_iota(jnp.int32, (capacity, rows), 0)
    for owner in range(owners):
        placed = (slot == slot_id + owner * capacity).astype(jnp.bfloat16)
        message_ref[owner, 0:query_rows, :] = own_half
        message_ref[owner, query_rows : query_rows + capacity, :] = jnp.dot(
            placed, local, preferred_element_type=jnp.float32
        ).astype(jnp.bfloat16)
        message_ref[owner, block_at:, :] = block


def send_message(patch_rows, owner_ids, page_ids, proj_weight, proj_bias, query_tokens, query_counts, owners, capacity,
                 halves):
    rows, features = patch_rows.shape
    per_block, token_slots, width = query_tokens.shape
    query_rows = per_block // halves * token_slots
    block_at = -(-(query_rows + capacity) // 16) * 16
    vmem = pl.BlockSpec(memory_space=pltpu.VMEM)
    return pl.pallas_call(
        functools.partial(send_kernel, PAGES_DEV, capacity, query_rows, block_at),
        out_shape=jax.ShapeDtypeStruct((owners, block_at + 16, width), jnp.bfloat16),
        in_specs=[pl.BlockSpec(memory_space=pltpu.SMEM)] + [vmem] * 6,
        out_specs=vmem,
        cost_estimate=pl.CostEstimate(
            flops=2 * rows * width * (features + owners * capacity),
            bytes_accessed=2 * (rows * features + features * width + owners * (block_at + 16) * width),
            transcendentals=rows,
        ),
    )(
        query_counts, owner_ids.reshape(rows), page_ids, patch_rows, proj_weight, proj_bias.reshape(1, width),
        query_tokens.reshape(per_block * token_slots, width),
    )


def score_kernel(page_total, token_slots, query_rows, token_block, table_ref, received_ref, tokens_ref, out_ref,
                 ordered_ref, sims_ref):
    owners = received_ref.shape[0]
    ordered_rows, width = ordered_ref.shape
    capacity = (ordered_rows - 16 * page_total - 16) // owners
    total_queries = out_ref.shape[1]
    totals = [sum(table_ref[chunk * page_total + page] for chunk in range(owners)) for page in range(page_total)]
    firsts = []
    at = 0
    for page in range(page_total):
        firsts.append(at)
        at = at + (totals[page] + 15) // 16 * 16
    target = lax.broadcasted_iota(jnp.int32, (ordered_rows, capacity), 0)
    slot = lax.broadcasted_iota(jnp.int32, (1, capacity), 1)
    ordered = jnp.zeros((ordered_rows, width), jnp.float32)
    before = [0] * page_total
    for chunk in range(owners):
        position = jnp.full((1, capacity), -1, jnp.int32)
        low = 0
        for page in range(page_total):
            high = low + table_ref[chunk * page_total + page]
            inside = (slot >= low) & (slot < high)
            position = jnp.where(inside, slot + (firsts[page] + before[page] - low), position)
            before[page] = before[page] + (high - low)
            low = high
        place = (position == target).astype(jnp.bfloat16)
        rows = received_ref[chunk, query_rows : query_rows + capacity, :]
        ordered = ordered + jnp.dot(place, rows, preferred_element_type=jnp.float32)
    ordered_ref[...] = ordered.astype(jnp.bfloat16)
    sources = token_block // tokens_ref.shape[1]
    sub = lax.broadcasted_iota(jnp.int32, (8, token_block), 0)
    query_lane = lax.broadcasted_iota(jnp.int32, (1, total_queries), 1)
    live_count = jnp.zeros((1, total_queries), jnp.int32)
    for query in range(total_queries):
        live_count = jnp.where(query_lane == query, table_ref[owners * page_total + query], live_count)
    token_id = lax.broadcasted_iota(jnp.int32, (token_block, total_queries), 0)
    query_id = lax.broadcasted_iota(jnp.int32, (token_block, total_queries), 1)

    def block_scores(block, total):
        tokens = tokens_ref[pl.ds(block * sources, sources)].reshape(token_block, width)
        sims_ref[...] = lax.dot_general(
            ordered_ref[...], tokens, (((1,), (1,)), ((), ())), preferred_element_type=jnp.float32
        )
        best_rows = []
        for page in range(page_total):
            first = firsts[page]
            whole = totals[page] // 16
            rest = totals[page] % 16

            def step(i, carry):
                start = pl.multiple_of(first + i * 16, 16)
                return (
                    jnp.maximum(carry[0], sims_ref[pl.ds(start, 8), :]),
                    jnp.maximum(carry[1], sims_ref[pl.ds(start + 8, 8), :]),
                )

            floor = jnp.full((8, token_block), -2.0, jnp.float32)
            low, high = lax.fori_loop(0, whole, step, (floor, floor))
            start = pl.multiple_of(first + whole * 16, 16)
            low = jnp.maximum(low, jnp.where(sub < rest, sims_ref[pl.ds(start, 8), :], jnp.float32(-2.0)))
            high = jnp.maximum(high, jnp.where(sub + 8 < rest, sims_ref[pl.ds(start + 8, 8), :], jnp.float32(-2.0)))
            best_rows.append(jnp.max(jnp.maximum(low, high), axis=0, keepdims=True))
        best = jnp.concatenate(best_rows, axis=0)
        token = token_id + block * token_block
        live = ((token // token_slots) == query_id) & ((token % token_slots) < live_count)
        return total + jnp.dot(
            best, live.astype(jnp.float32), precision=lax.Precision.HIGHEST, preferred_element_type=jnp.float32
        )

    blocks = tokens_ref.shape[0] * tokens_ref.shape[1] // token_block
    out_ref[...] = lax.fori_loop(
        0, blocks, block_scores, jnp.zeros((page_total, total_queries), jnp.float32)
    )


def page_scores(received, tokens, table, total_queries, page_total, token_slots, query_rows, capacity):
    owners = received.shape[0]
    width = received.shape[2]
    ordered_rows = owners * capacity + 16 * page_total + 16
    token_total = tokens.shape[0] * tokens.shape[1]
    token_block = min(token_total, 1024)
    vmem = pl.BlockSpec(memory_space=pltpu.VMEM)
    return pl.pallas_call(
        functools.partial(score_kernel, page_total, token_slots, query_rows, token_block),
        out_shape=jax.ShapeDtypeStruct((page_total, total_queries), jnp.float32),
        in_specs=[pl.BlockSpec(memory_space=pltpu.SMEM), vmem, vmem],
        out_specs=vmem,
        scratch_shapes=[
            pltpu.VMEM((ordered_rows, width), jnp.bfloat16),
            pltpu.VMEM((ordered_rows, token_block), jnp.float32),
        ],
        cost_estimate=pl.CostEstimate(
            flops=2 * ordered_rows * width * (owners * capacity + token_total),
            bytes_accessed=2 * received.size + 2 * tokens.size + 4 * page_total * total_queries,
            transcendentals=0,
        ),
    )(table, received, tokens)


def shards(patch_rows, owner_ids, page_ids, proj_weight, proj_bias, query_tokens, query_counts):
    owners = lax.axis_size("blk")
    halves = lax.axis_size("inner")
    rows = patch_rows.shape[0]
    capacity = 2 * rows // owners
    per_block = query_tokens.shape[0]
    token_slots = query_tokens.shape[1]
    width = query_tokens.shape[2]
    total_queries = per_block * owners
    half_queries = per_block // halves
    query_rows = half_queries * token_slots
    message = send_message(
        patch_rows, owner_ids, page_ids, proj_weight, proj_bias, query_tokens, query_counts, owners, capacity, halves
    )
    received = lax.all_to_all(message, "blk", split_axis=0, concat_axis=0, tiled=True)
    halves_in = lax.all_gather(received[:, :query_rows], "inner", axis=1, tiled=True)
    block_at = -(-(query_rows + capacity) // 16) * 16
    combos = -(-owners * PAGES_DEV // 128) * 128
    count_rows = combos // 128
    page_counts = received[:, block_at : block_at + count_rows].reshape(owners, combos)
    page_counts = lax.dynamic_slice_in_dim(page_counts, lax.axis_index("blk") * PAGES_DEV, PAGES_DEV, axis=1)
    counts = received[:, block_at + count_rows, :per_block]
    table = jnp.concatenate([page_counts.reshape(owners * PAGES_DEV), counts.reshape(total_queries)]).astype(jnp.int32)
    return page_scores(received, halves_in, table, total_queries, PAGES_DEV, token_slots, query_rows, capacity)


def solution(mesh):
    in_specs = (
        P(("groups", "blk", "inner"), None),
        P(("groups", "blk", "inner"), None),
        P(("groups", "blk", "inner")),
        P(),
        P(),
        P(("groups", "blk"), None, None),
        P(("groups", "blk")),
    )
    out_specs = P(("groups", "blk", "inner"), None)
    return jax.shard_map(shards, mesh=mesh, in_specs=in_specs, out_specs=out_specs, check_vma=False)
```

```python
import functools
import math

import jax
import jax.numpy as jnp
from jax import lax
from jax.experimental import pallas as pl
from jax.experimental.pallas import tpu as pltpu
from jax.sharding import PartitionSpec as P

PAGES_DEV = 8


def send_kernel(page_total, capacity, query_rows, block_at, query_counts_ref, owner_ref, page_ref, rows_ref, weight_ref,
                bias_ref, queries_ref, message_ref):
    owners = message_ref.shape[0]
    rows = rows_ref.shape[0]
    proj = jnp.dot(rows_ref[...], weight_ref[...], preferred_element_type=jnp.float32) + bias_ref[...]
    scale = lax.rsqrt(jnp.sum(proj * proj, axis=1, keepdims=True) + 1e-06)
    local = (proj * scale).astype(jnp.bfloat16)
    combo = owner_ref[...].reshape(1, rows) * page_total + page_ref[...].reshape(1, rows)
    combos = -(-owners * page_total // 128) * 128
    combo_id = lax.broadcasted_iota(jnp.int32, (combos, rows), 0)
    onehot = (combo == combo_id).astype(jnp.bfloat16)
    earlier = (
        lax.broadcasted_iota(jnp.int32, (rows, rows), 0) < lax.broadcasted_iota(jnp.int32, (rows, rows), 1)
    ).astype(jnp.bfloat16)
    seen = jnp.dot(onehot, earlier, preferred_element_type=jnp.float32)
    count = jnp.sum(onehot.astype(jnp.float32), axis=1, keepdims=True)
    row_id = lax.broadcasted_iota(jnp.int32, (combos, combos), 0)
    col_id = lax.broadcasted_iota(jnp.int32, (combos, combos), 1)
    same_owner_lower = (row_id // page_total == col_id // page_total) & (col_id % page_total < row_id % page_total)
    offset = jnp.dot(same_owner_lower.astype(jnp.bfloat16), count.astype(jnp.bfloat16),
                     preferred_element_type=jnp.float32)
    base = (lax.broadcasted_iota(jnp.int32, (combos, 1), 0) // page_total * capacity).astype(jnp.float32) + offset
    slot = jnp.sum(onehot.astype(jnp.float32) * (base + seen), axis=0, keepdims=True).astype(jnp.int32)
    count_rows = [
        lax.dot_general(
            jnp.ones((1, rows), jnp.bfloat16), onehot[group * 128 : (group + 1) * 128],
            (((1,), (1,)), ((), ())), preferred_element_type=jnp.float32,
        )
        for group in range(combos // 128)
    ]
    lane = lax.broadcasted_iota(jnp.int32, (1, 128), 1)
    query_count_row = jnp.zeros((1, 128), jnp.float32)
    for query in range(query_counts_ref.shape[0]):
        query_count_row = jnp.where(lane == query, query_counts_ref[query].astype(jnp.float32), query_count_row)
    block_rows = message_ref.shape[1] - block_at
    block = jnp.concatenate(
        count_rows
        + [query_count_row, jnp.zeros((block_rows - len(count_rows) - 1, 128), jnp.float32)],
        axis=0,
    ).astype(jnp.bfloat16)
    own_half = queries_ref[pl.ds(pl.multiple_of(lax.axis_index("inner") * query_rows, query_rows), query_rows), :]
    slot_id = lax.broadcasted_iota(jnp.int32, (capacity, rows), 0)
    for owner in range(owners):
        placed = (slot == slot_id + owner * capacity).astype(jnp.bfloat16)
        message_ref[owner, 0:query_rows, :] = own_half
        message_ref[owner, query_rows : query_rows + capacity, :] = jnp.dot(
            placed, local, preferred_element_type=jnp.float32
        ).astype(jnp.bfloat16)
        message_ref[owner, block_at:, :] = block


def send_message(patch_rows, owner_ids, page_ids, proj_weight, proj_bias, query_tokens, query_counts, owners, capacity,
                 halves):
    rows, features = patch_rows.shape
    per_block, token_slots, width = query_tokens.shape
    query_rows = per_block // halves * token_slots
    block_at = -(-(query_rows + capacity) // 16) * 16
    vmem = pl.BlockSpec(memory_space=pltpu.VMEM)
    return pl.pallas_call(
        functools.partial(send_kernel, PAGES_DEV, capacity, query_rows, block_at),
        out_shape=jax.ShapeDtypeStruct((owners, block_at + 16, width), jnp.bfloat16),
        in_specs=[pl.BlockSpec(memory_space=pltpu.SMEM)] + [vmem] * 6,
        out_specs=vmem,
        cost_estimate=pl.CostEstimate(
            flops=2 * rows * width * (features + owners * capacity),
            bytes_accessed=2 * (rows * features + features * width + owners * (block_at + 16) * width),
            transcendentals=rows,
        ),
    )(
        query_counts, owner_ids.reshape(rows), page_ids, patch_rows, proj_weight, proj_bias.reshape(1, width),
        query_tokens.reshape(per_block * token_slots, width),
    )


def page_runs(table_ref, owners, page_total):
    totals = [sum(table_ref[chunk * page_total + page] for chunk in range(owners)) for page in range(page_total)]
    firsts = []
    at = 0
    for page in range(page_total):
        firsts.append(at)
        at = at + (totals[page] + 15) // 16 * 16
    return totals, firsts


def half_scores(table_ref, ordered_ref, sims_ref, tokens_ref, half, owners, page_total, token_slots, per_block,
                total_queries):
    ordered_rows, width = ordered_ref.shape
    token_block = sims_ref.shape[1]
    half_rows = tokens_ref.shape[1]
    half_queries = half_rows // token_slots
    totals, firsts = page_runs(table_ref, owners, page_total)
    query_lane = lax.broadcasted_iota(jnp.int32, (1, total_queries), 1)
    live_count = jnp.zeros((1, total_queries), jnp.int32)
    for query in range(total_queries):
        live_count = jnp.where(query_lane == query, table_ref[owners * page_total + query], live_count)
    sub = lax.broadcasted_iota(jnp.int32, (8, token_block), 0)
    token_id = lax.broadcasted_iota(jnp.int32, (token_block, total_queries), 0)
    query_id = lax.broadcasted_iota(jnp.int32, (token_block, total_queries), 1)
    sources = token_block // half_rows

    def block_scores(block, total):
        tokens = tokens_ref[pl.ds(block * sources, sources)].reshape(token_block, width)
        sims_ref[...] = lax.dot_general(
            ordered_ref[...], tokens, (((1,), (1,)), ((), ())), preferred_element_type=jnp.float32
        )
        best_rows = []
        for page in range(page_total):
            first = firsts[page]
            whole = totals[page] // 16
            rest = totals[page] % 16

            def step(i, carry):
                start = pl.multiple_of(first + i * 16, 16)
                return (
                    jnp.maximum(carry[0], sims_ref[pl.ds(start, 8), :]),
                    jnp.maximum(carry[1], sims_ref[pl.ds(start + 8, 8), :]),
                )

            floor = jnp.full((8, token_block), -2.0, jnp.float32)
            low, high = lax.fori_loop(0, whole, step, (floor, floor))
            start = pl.multiple_of(first + whole * 16, 16)
            low = jnp.maximum(low, jnp.where(sub < rest, sims_ref[pl.ds(start, 8), :], jnp.float32(-2.0)))
            high = jnp.maximum(high, jnp.where(sub + 8 < rest, sims_ref[pl.ds(start + 8, 8), :], jnp.float32(-2.0)))
            best_rows.append(jnp.max(jnp.maximum(low, high), axis=0, keepdims=True))
        best = jnp.concatenate(best_rows, axis=0)
        token = token_id + block * token_block
        query = token // half_rows * per_block + half * half_queries + token % half_rows // token_slots
        live = (query == query_id) & ((token % token_slots) < live_count)
        return total + jnp.dot(
            best, live.astype(jnp.float32), precision=lax.Precision.HIGHEST, preferred_element_type=jnp.float32
        )

    blocks = tokens_ref.shape[0] * half_rows // token_block
    return lax.fori_loop(0, blocks, block_scores, jnp.zeros((page_total, total_queries), jnp.float32))


def first_kernel(page_total, token_slots, per_block, query_rows, table_ref, received_ref, out_ref, ordered_ref,
                 sims_ref):
    owners = received_ref.shape[0]
    ordered_rows, width = ordered_ref.shape
    capacity = (ordered_rows - 16 * page_total - 16) // owners
    totals, firsts = page_runs(table_ref, owners, page_total)
    target = lax.broadcasted_iota(jnp.int32, (ordered_rows, capacity), 0)
    slot = lax.broadcasted_iota(jnp.int32, (1, capacity), 1)
    ordered = jnp.zeros((ordered_rows, width), jnp.float32)
    before = [0] * page_total
    for chunk in range(owners):
        position = jnp.full((1, capacity), -1, jnp.int32)
        low = 0
        for page in range(page_total):
            high = low + table_ref[chunk * page_total + page]
            inside = (slot >= low) & (slot < high)
            position = jnp.where(inside, slot + (firsts[page] + before[page] - low), position)
            before[page] = before[page] + (high - low)
            low = high
        place = (position == target).astype(jnp.bfloat16)
        rows = received_ref[chunk, query_rows : query_rows + capacity, :]
        ordered = ordered + jnp.dot(place, rows, preferred_element_type=jnp.float32)
    ordered_ref[...] = ordered.astype(jnp.bfloat16)
    out_ref[...] = half_scores(
        table_ref, ordered_ref, sims_ref, received_ref.at[:, 0:query_rows, :], lax.axis_index("inner"), owners,
        page_total, token_slots, per_block, out_ref.shape[1],
    )


def second_kernel(page_total, token_slots, per_block, table_ref, ordered_ref, partner_ref, partial_ref, out_ref,
                  sims_ref):
    owners = partner_ref.shape[0]
    out_ref[...] = partial_ref[...] + half_scores(
        table_ref, ordered_ref, sims_ref, partner_ref, 1 - lax.axis_index("inner"), owners, page_total, token_slots,
        per_block, out_ref.shape[1],
    )


def page_scores(received, table, total_queries, page_total, token_slots, per_block, query_rows, capacity):
    owners = received.shape[0]
    width = received.shape[2]
    ordered_rows = owners * capacity + 16 * page_total + 16
    token_block = min(owners * query_rows, 1024)
    vmem = pl.BlockSpec(memory_space=pltpu.VMEM)
    smem = pl.BlockSpec(memory_space=pltpu.SMEM)
    partner = lax.ppermute(received[:, :query_rows], "inner", [(0, 1), (1, 0)])
    half_flops = 2 * ordered_rows * width * owners * query_rows
    partial, ordered = pl.pallas_call(
        functools.partial(first_kernel, page_total, token_slots, per_block, query_rows),
        out_shape=(
            jax.ShapeDtypeStruct((page_total, total_queries), jnp.float32),
            jax.ShapeDtypeStruct((ordered_rows, width), jnp.bfloat16),
        ),
        in_specs=[smem, vmem],
        out_specs=(vmem, vmem),
        scratch_shapes=[pltpu.VMEM((ordered_rows, token_block), jnp.float32)],
        cost_estimate=pl.CostEstimate(
            flops=2 * ordered_rows * width * owners * capacity + half_flops,
            bytes_accessed=2 * received.size + 2 * ordered_rows * width + 4 * page_total * total_queries,
            transcendentals=0,
        ),
    )(table, received)
    return pl.pallas_call(
        functools.partial(second_kernel, page_total, token_slots, per_block),
        out_shape=jax.ShapeDtypeStruct((page_total, total_queries), jnp.float32),
        in_specs=[smem, vmem, vmem, vmem],
        out_specs=vmem,
        scratch_shapes=[pltpu.VMEM((ordered_rows, token_block), jnp.float32)],
        cost_estimate=pl.CostEstimate(
            flops=half_flops,
            bytes_accessed=2 * ordered_rows * width + 2 * partner.size + 8 * page_total * total_queries,
            transcendentals=0,
        ),
    )(table, ordered, partner, partial)


def shards(patch_rows, owner_ids, page_ids, proj_weight, proj_bias, query_tokens, query_counts):
    owners = lax.axis_size("blk")
    halves = lax.axis_size("inner")
    rows = patch_rows.shape[0]
    capacity = 2 * rows // owners
    per_block = query_tokens.shape[0]
    token_slots = query_tokens.shape[1]
    width = query_tokens.shape[2]
    total_queries = per_block * owners
    half_queries = per_block // halves
    query_rows = half_queries * token_slots
    message = send_message(
        patch_rows, owner_ids, page_ids, proj_weight, proj_bias, query_tokens, query_counts, owners, capacity, halves
    )
    received = lax.all_to_all(message, "blk", split_axis=0, concat_axis=0, tiled=True)
    block_at = -(-(query_rows + capacity) // 16) * 16
    combos = -(-owners * PAGES_DEV // 128) * 128
    count_rows = combos // 128
    page_counts = received[:, block_at : block_at + count_rows].reshape(owners, combos)
    page_counts = lax.dynamic_slice_in_dim(page_counts, lax.axis_index("blk") * PAGES_DEV, PAGES_DEV, axis=1)
    counts = received[:, block_at + count_rows, :per_block]
    table = jnp.concatenate([page_counts.reshape(owners * PAGES_DEV), counts.reshape(total_queries)]).astype(jnp.int32)
    return page_scores(received, table, total_queries, PAGES_DEV, token_slots, per_block, query_rows, capacity)


def solution(mesh):
    in_specs = (
        P(("groups", "blk", "inner"), None),
        P(("groups", "blk", "inner"), None),
        P(("groups", "blk", "inner")),
        P(),
        P(),
        P(("groups", "blk"), None, None),
        P(("groups", "blk")),
    )
    out_specs = P(("groups", "blk", "inner"), None)
    return jax.shard_map(shards, mesh=mesh, in_specs=in_specs, out_specs=out_specs, check_vma=False)
```

```python
import functools
import math

import jax
import jax.numpy as jnp
from jax import lax
from jax.experimental import pallas as pl
from jax.experimental.pallas import tpu as pltpu
from jax.sharding import PartitionSpec as P

PAGES_DEV = 8


def send_kernel(page_total, capacity, query_rows, block_at, query_counts_ref, owner_ref, page_ref, rows_ref, weight_ref,
                bias_ref, queries_ref, message_ref):
    owners = message_ref.shape[0]
    rows = rows_ref.shape[0]
    proj = jnp.dot(rows_ref[...], weight_ref[...], preferred_element_type=jnp.float32) + bias_ref[...]
    scale = lax.rsqrt(jnp.sum(proj * proj, axis=1, keepdims=True) + 1e-06)
    local = (proj * scale).astype(jnp.bfloat16)
    combo = owner_ref[...].reshape(1, rows) * page_total + page_ref[...].reshape(1, rows)
    combos = -(-owners * page_total // 128) * 128
    combo_id = lax.broadcasted_iota(jnp.int32, (combos, rows), 0)
    onehot = (combo == combo_id).astype(jnp.bfloat16)
    earlier = (
        lax.broadcasted_iota(jnp.int32, (rows, rows), 0) < lax.broadcasted_iota(jnp.int32, (rows, rows), 1)
    ).astype(jnp.bfloat16)
    seen = jnp.dot(onehot, earlier, preferred_element_type=jnp.float32)
    count = jnp.sum(onehot.astype(jnp.float32), axis=1, keepdims=True)
    row_id = lax.broadcasted_iota(jnp.int32, (combos, combos), 0)
    col_id = lax.broadcasted_iota(jnp.int32, (combos, combos), 1)
    same_owner_lower = (row_id // page_total == col_id // page_total) & (col_id % page_total < row_id % page_total)
    offset = jnp.dot(same_owner_lower.astype(jnp.bfloat16), count.astype(jnp.bfloat16),
                     preferred_element_type=jnp.float32)
    base = (lax.broadcasted_iota(jnp.int32, (combos, 1), 0) // page_total * capacity).astype(jnp.float32) + offset
    slot = jnp.sum(onehot.astype(jnp.float32) * (base + seen), axis=0, keepdims=True).astype(jnp.int32)
    count_rows = [
        lax.dot_general(
            jnp.ones((1, rows), jnp.bfloat16), onehot[group * 128 : (group + 1) * 128],
            (((1,), (1,)), ((), ())), preferred_element_type=jnp.float32,
        )
        for group in range(combos // 128)
    ]
    lane = lax.broadcasted_iota(jnp.int32, (1, 128), 1)
    query_count_row = jnp.zeros((1, 128), jnp.float32)
    for query in range(query_counts_ref.shape[0]):
        query_count_row = jnp.where(lane == query, query_counts_ref[query].astype(jnp.float32), query_count_row)
    block_rows = message_ref.shape[1] - block_at
    block = jnp.concatenate(
        count_rows
        + [query_count_row, jnp.zeros((block_rows - len(count_rows) - 1, 128), jnp.float32)],
        axis=0,
    ).astype(jnp.bfloat16)
    own_half = queries_ref[pl.ds(pl.multiple_of(lax.axis_index("inner") * query_rows, query_rows), query_rows), :]
    slot_id = lax.broadcasted_iota(jnp.int32, (capacity, rows), 0)
    for owner in range(owners):
        placed = (slot == slot_id + owner * capacity).astype(jnp.bfloat16)
        message_ref[owner, 0:query_rows, :] = own_half
        message_ref[owner, query_rows : query_rows + capacity, :] = jnp.dot(
            placed, local, preferred_element_type=jnp.float32
        ).astype(jnp.bfloat16)
        message_ref[owner, block_at:, :] = block


def send_message(patch_rows, owner_ids, page_ids, proj_weight, proj_bias, query_tokens, query_counts, owners, capacity,
                 halves):
    rows, features = patch_rows.shape
    per_block, token_slots, width = query_tokens.shape
    query_rows = per_block // halves * token_slots
    block_at = -(-(query_rows + capacity) // 16) * 16
    vmem = pl.BlockSpec(memory_space=pltpu.VMEM)
    return pl.pallas_call(
        functools.partial(send_kernel, PAGES_DEV, capacity, query_rows, block_at),
        out_shape=jax.ShapeDtypeStruct((owners, block_at + 16, width), jnp.bfloat16),
        in_specs=[pl.BlockSpec(memory_space=pltpu.SMEM)] + [vmem] * 6,
        out_specs=vmem,
        cost_estimate=pl.CostEstimate(
            flops=2 * rows * width * (features + owners * capacity),
            bytes_accessed=2 * (rows * features + features * width + owners * (block_at + 16) * width),
            transcendentals=rows,
        ),
    )(
        query_counts, owner_ids.reshape(rows), page_ids, patch_rows, proj_weight, proj_bias.reshape(1, width),
        query_tokens.reshape(per_block * token_slots, width),
    )


def score_kernel(page_total, token_slots, query_rows, token_block, table_ref, received_ref, tokens_ref, out_ref,
                 ordered_ref, sims_ref):
    owners = received_ref.shape[0]
    ordered_rows, width = ordered_ref.shape
    capacity = (ordered_rows - 16 * page_total - 16) // owners
    total_queries = out_ref.shape[1]
    totals = [sum(table_ref[chunk * page_total + page] for chunk in range(owners)) for page in range(page_total)]
    firsts = []
    at = 0
    for page in range(page_total):
        firsts.append(at)
        at = at + (totals[page] + 15) // 16 * 16
    target = lax.broadcasted_iota(jnp.int32, (ordered_rows, capacity), 0)
    slot = lax.broadcasted_iota(jnp.int32, (1, capacity), 1)
    ordered = jnp.zeros((ordered_rows, width), jnp.float32)
    before = [0] * page_total
    for chunk in range(owners):
        position = jnp.full((1, capacity), -1, jnp.int32)
        low = 0
        for page in range(page_total):
            high = low + table_ref[chunk * page_total + page]
            inside = (slot >= low) & (slot < high)
            position = jnp.where(inside, slot + (firsts[page] + before[page] - low), position)
            before[page] = before[page] + (high - low)
            low = high
        place = (position == target).astype(jnp.bfloat16)
        rows = received_ref[chunk, query_rows : query_rows + capacity, :]
        ordered = ordered + jnp.dot(place, rows, preferred_element_type=jnp.float32)
    ordered_ref[...] = ordered.astype(jnp.bfloat16)
    sources = token_block // tokens_ref.shape[1]
    sub = lax.broadcasted_iota(jnp.int32, (8, token_block), 0)
    query_lane = lax.broadcasted_iota(jnp.int32, (1, total_queries), 1)
    live_count = jnp.zeros((1, total_queries), jnp.int32)
    for query in range(total_queries):
        live_count = jnp.where(query_lane == query, table_ref[owners * page_total + query], live_count)
    token_id = lax.broadcasted_iota(jnp.int32, (token_block, total_queries), 0)
    query_id = lax.broadcasted_iota(jnp.int32, (token_block, total_queries), 1)

    def block_scores(block, total):
        tokens = tokens_ref[pl.ds(block * sources, sources)].reshape(token_block, width)
        sims_ref[...] = lax.dot_general(
            ordered_ref[...], tokens, (((1,), (1,)), ((), ())), preferred_element_type=jnp.float32
        )
        best_rows = []
        for page in range(page_total):
            first = firsts[page]
            whole = totals[page] // 16
            rest = totals[page] % 16

            def step(i, carry):
                start = pl.multiple_of(first + i * 16, 16)
                return (
                    jnp.maximum(carry[0], sims_ref[pl.ds(start, 8), :]),
                    jnp.maximum(carry[1], sims_ref[pl.ds(start + 8, 8), :]),
                )

            floor = jnp.full((8, token_block), -2.0, jnp.float32)
            low, high = lax.fori_loop(0, whole, step, (floor, floor))
            start = pl.multiple_of(first + whole * 16, 16)
            low = jnp.maximum(low, jnp.where(sub < rest, sims_ref[pl.ds(start, 8), :], jnp.float32(-2.0)))
            high = jnp.maximum(high, jnp.where(sub + 8 < rest, sims_ref[pl.ds(start + 8, 8), :], jnp.float32(-2.0)))
            best_rows.append(jnp.max(jnp.maximum(low, high), axis=0, keepdims=True))
        best = jnp.concatenate(best_rows, axis=0)
        token = token_id + block * token_block
        live = ((token // token_slots) == query_id) & ((token % token_slots) < live_count)
        return total + jnp.dot(
            best, live.astype(jnp.float32), precision=lax.Precision.HIGHEST, preferred_element_type=jnp.float32
        )

    blocks = tokens_ref.shape[0] * tokens_ref.shape[1] // token_block
    out_ref[...] = lax.fori_loop(
        0, blocks, block_scores, jnp.zeros((page_total, total_queries), jnp.float32)
    )


def page_scores(received, tokens, table, total_queries, page_total, token_slots, query_rows, capacity):
    owners = received.shape[0]
    width = received.shape[2]
    ordered_rows = owners * capacity + 16 * page_total + 16
    token_total = tokens.shape[0] * tokens.shape[1]
    token_block = min(token_total, 2048)
    vmem = pl.BlockSpec(memory_space=pltpu.VMEM)
    return pl.pallas_call(
        functools.partial(score_kernel, page_total, token_slots, query_rows, token_block),
        out_shape=jax.ShapeDtypeStruct((page_total, total_queries), jnp.float32),
        in_specs=[pl.BlockSpec(memory_space=pltpu.SMEM), vmem, vmem],
        out_specs=vmem,
        scratch_shapes=[
            pltpu.VMEM((ordered_rows, width), jnp.bfloat16),
            pltpu.VMEM((ordered_rows, token_block), jnp.float32),
        ],
        cost_estimate=pl.CostEstimate(
            flops=2 * ordered_rows * width * (owners * capacity + token_total),
            bytes_accessed=2 * received.size + 2 * tokens.size + 4 * page_total * total_queries,
            transcendentals=0,
        ),
    )(table, received, tokens)


def shards(patch_rows, owner_ids, page_ids, proj_weight, proj_bias, query_tokens, query_counts):
    owners = lax.axis_size("blk")
    halves = lax.axis_size("inner")
    rows = patch_rows.shape[0]
    capacity = 2 * rows // owners
    per_block = query_tokens.shape[0]
    token_slots = query_tokens.shape[1]
    width = query_tokens.shape[2]
    total_queries = per_block * owners
    half_queries = per_block // halves
    query_rows = half_queries * token_slots
    message = send_message(
        patch_rows, owner_ids, page_ids, proj_weight, proj_bias, query_tokens, query_counts, owners, capacity, halves
    )
    received = lax.all_to_all(message, "blk", split_axis=0, concat_axis=0, tiled=True)
    halves_in = lax.all_gather(received[:, :query_rows], "inner", axis=1, tiled=True)
    block_at = -(-(query_rows + capacity) // 16) * 16
    combos = -(-owners * PAGES_DEV // 128) * 128
    count_rows = combos // 128
    page_counts = received[:, block_at : block_at + count_rows].reshape(owners, combos)
    page_counts = lax.dynamic_slice_in_dim(page_counts, lax.axis_index("blk") * PAGES_DEV, PAGES_DEV, axis=1)
    counts = received[:, block_at + count_rows, :per_block]
    table = jnp.concatenate([page_counts.reshape(owners * PAGES_DEV), counts.reshape(total_queries)]).astype(jnp.int32)
    return page_scores(received, halves_in, table, total_queries, PAGES_DEV, token_slots, query_rows, capacity)


def solution(mesh):
    in_specs = (
        P(("groups", "blk", "inner"), None),
        P(("groups", "blk", "inner"), None),
        P(("groups", "blk", "inner")),
        P(),
        P(),
        P(("groups", "blk"), None, None),
        P(("groups", "blk")),
    )
    out_specs = P(("groups", "blk", "inner"), None)
    return jax.shard_map(shards, mesh=mesh, in_specs=in_specs, out_specs=out_specs, check_vma=False)
```

```python
import functools
import math

import jax
import jax.numpy as jnp
from jax import lax
from jax.experimental import pallas as pl
from jax.experimental.pallas import tpu as pltpu
from jax.sharding import PartitionSpec as P

PAGES_DEV = 8


def send_kernel(page_total, capacity, query_rows, block_at, query_counts_ref, owner_ref, page_ref, rows_ref, weight_ref,
                bias_ref, queries_ref, message_ref):
    owners = message_ref.shape[0]
    rows = rows_ref.shape[0]
    proj = jnp.dot(rows_ref[...], weight_ref[...], preferred_element_type=jnp.float32) + bias_ref[...]
    scale = lax.rsqrt(jnp.sum(proj * proj, axis=1, keepdims=True) + 1e-06)
    local = (proj * scale).astype(jnp.bfloat16)
    combo = owner_ref[...].reshape(1, rows) * page_total + page_ref[...].reshape(1, rows)
    combos = -(-owners * page_total // 128) * 128
    combo_id = lax.broadcasted_iota(jnp.int32, (combos, rows), 0)
    onehot = (combo == combo_id).astype(jnp.bfloat16)
    earlier = (
        lax.broadcasted_iota(jnp.int32, (rows, rows), 0) < lax.broadcasted_iota(jnp.int32, (rows, rows), 1)
    ).astype(jnp.bfloat16)
    seen = jnp.dot(onehot, earlier, preferred_element_type=jnp.float32)
    count = jnp.sum(onehot.astype(jnp.float32), axis=1, keepdims=True)
    row_id = lax.broadcasted_iota(jnp.int32, (combos, combos), 0)
    col_id = lax.broadcasted_iota(jnp.int32, (combos, combos), 1)
    same_owner_lower = (row_id // page_total == col_id // page_total) & (col_id % page_total < row_id % page_total)
    offset = jnp.dot(same_owner_lower.astype(jnp.bfloat16), count.astype(jnp.bfloat16),
                     preferred_element_type=jnp.float32)
    base = (lax.broadcasted_iota(jnp.int32, (combos, 1), 0) // page_total * capacity).astype(jnp.float32) + offset
    slot = jnp.sum(onehot.astype(jnp.float32) * (base + seen), axis=0, keepdims=True).astype(jnp.int32)
    count_rows = [
        lax.dot_general(
            jnp.ones((1, rows), jnp.bfloat16), onehot[group * 128 : (group + 1) * 128],
            (((1,), (1,)), ((), ())), preferred_element_type=jnp.float32,
        )
        for group in range(combos // 128)
    ]
    lane = lax.broadcasted_iota(jnp.int32, (1, 128), 1)
    query_count_row = jnp.zeros((1, 128), jnp.float32)
    for query in range(query_counts_ref.shape[0]):
        query_count_row = jnp.where(lane == query, query_counts_ref[query].astype(jnp.float32), query_count_row)
    block_rows = message_ref.shape[1] - block_at
    block = jnp.concatenate(
        count_rows
        + [query_count_row, jnp.zeros((block_rows - len(count_rows) - 1, 128), jnp.float32)],
        axis=0,
    ).astype(jnp.bfloat16)
    own_half = queries_ref[pl.ds(pl.multiple_of(lax.axis_index("inner") * query_rows, query_rows), query_rows), :]
    slot_id = lax.broadcasted_iota(jnp.int32, (capacity, rows), 0)
    for owner in range(owners):
        placed = (slot == slot_id + owner * capacity).astype(jnp.bfloat16)
        message_ref[owner, 0:query_rows, :] = own_half
        message_ref[owner, query_rows : query_rows + capacity, :] = jnp.dot(
            placed, local, preferred_element_type=jnp.float32
        ).astype(jnp.bfloat16)
        message_ref[owner, block_at:, :] = block


def send_message(patch_rows, owner_ids, page_ids, proj_weight, proj_bias, query_tokens, query_counts, owners, capacity,
                 halves):
    rows, features = patch_rows.shape
    per_block, token_slots, width = query_tokens.shape
    query_rows = per_block // halves * token_slots
    block_at = -(-(query_rows + capacity) // 16) * 16
    vmem = pl.BlockSpec(memory_space=pltpu.VMEM)
    return pl.pallas_call(
        functools.partial(send_kernel, PAGES_DEV, capacity, query_rows, block_at),
        out_shape=jax.ShapeDtypeStruct((owners, block_at + 16, width), jnp.bfloat16),
        in_specs=[pl.BlockSpec(memory_space=pltpu.SMEM)] + [vmem] * 6,
        out_specs=vmem,
        cost_estimate=pl.CostEstimate(
            flops=2 * rows * width * (features + owners * capacity),
            bytes_accessed=2 * (rows * features + features * width + owners * (block_at + 16) * width),
            transcendentals=rows,
        ),
    )(
        query_counts, owner_ids.reshape(rows), page_ids, patch_rows, proj_weight, proj_bias.reshape(1, width),
        query_tokens.reshape(per_block * token_slots, width),
    )


def score_kernel(page_total, token_slots, query_rows, token_block, table_ref, received_ref, tokens_ref, out_ref,
                 ordered_ref, sims_ref):
    owners = received_ref.shape[0]
    ordered_rows, width = ordered_ref.shape
    capacity = (ordered_rows - 16 * page_total - 16) // owners
    total_queries = out_ref.shape[1]
    totals = [sum(table_ref[chunk * page_total + page] for chunk in range(owners)) for page in range(page_total)]
    firsts = []
    at = 0
    for page in range(page_total):
        firsts.append(at)
        at = at + (totals[page] + 15) // 16 * 16
    target = lax.broadcasted_iota(jnp.int32, (ordered_rows, capacity), 0)
    slot = lax.broadcasted_iota(jnp.int32, (1, capacity), 1)
    ordered = jnp.zeros((ordered_rows, width), jnp.float32)
    before = [0] * page_total
    for chunk in range(owners):
        position = jnp.full((1, capacity), -1, jnp.int32)
        low = 0
        for page in range(page_total):
            high = low + table_ref[chunk * page_total + page]
            inside = (slot >= low) & (slot < high)
            position = jnp.where(inside, slot + (firsts[page] + before[page] - low), position)
            before[page] = before[page] + (high - low)
            low = high
        place = (position == target).astype(jnp.bfloat16)
        rows = received_ref[chunk, query_rows : query_rows + capacity, :]
        ordered = ordered + jnp.dot(place, rows, preferred_element_type=jnp.float32)
    ordered_ref[...] = ordered.astype(jnp.bfloat16)
    sources = token_block // tokens_ref.shape[1]
    sub = lax.broadcasted_iota(jnp.int32, (8, token_block), 0)
    query_lane = lax.broadcasted_iota(jnp.int32, (1, total_queries), 1)
    live_count = jnp.zeros((1, total_queries), jnp.int32)
    for query in range(total_queries):
        live_count = jnp.where(query_lane == query, table_ref[owners * page_total + query], live_count)
    token_id = lax.broadcasted_iota(jnp.int32, (token_block, total_queries), 0)
    query_id = lax.broadcasted_iota(jnp.int32, (token_block, total_queries), 1)

    def block_scores(block, total):
        tokens = tokens_ref[pl.ds(block * sources, sources)].reshape(token_block, width)
        sims_ref[...] = lax.dot_general(
            ordered_ref[...], tokens, (((1,), (1,)), ((), ())), preferred_element_type=jnp.float32
        )
        best_rows = []
        for page in range(page_total):
            first = firsts[page]
            whole = totals[page] // 16
            rest = totals[page] % 16

            def step(i, carry):
                start = pl.multiple_of(first + i * 16, 16)
                return (
                    jnp.maximum(carry[0], sims_ref[pl.ds(start, 8), :]),
                    jnp.maximum(carry[1], sims_ref[pl.ds(start + 8, 8), :]),
                )

            floor = jnp.full((8, token_block), -2.0, jnp.float32)
            low, high = lax.fori_loop(0, whole, step, (floor, floor))
            start = pl.multiple_of(first + whole * 16, 16)
            low = jnp.maximum(low, jnp.where(sub < rest, sims_ref[pl.ds(start, 8), :], jnp.float32(-2.0)))
            high = jnp.maximum(high, jnp.where(sub + 8 < rest, sims_ref[pl.ds(start + 8, 8), :], jnp.float32(-2.0)))
            best_rows.append(jnp.max(jnp.maximum(low, high), axis=0, keepdims=True))
        best = jnp.concatenate(best_rows, axis=0)
        token = token_id + block * token_block
        live = ((token // token_slots) == query_id) & ((token % token_slots) < live_count)
        return total + jnp.dot(
            best, live.astype(jnp.float32), precision=lax.Precision.HIGHEST, preferred_element_type=jnp.float32
        )

    blocks = tokens_ref.shape[0] * tokens_ref.shape[1] // token_block
    out_ref[...] = lax.fori_loop(
        0, blocks, block_scores, jnp.zeros((page_total, total_queries), jnp.float32)
    )


def page_scores(received, tokens, table, total_queries, page_total, token_slots, query_rows, capacity):
    owners = received.shape[0]
    width = received.shape[2]
    ordered_rows = owners * capacity + 16 * page_total + 16
    token_total = tokens.shape[0] * tokens.shape[1]
    token_block = min(token_total, 512)
    vmem = pl.BlockSpec(memory_space=pltpu.VMEM)
    return pl.pallas_call(
        functools.partial(score_kernel, page_total, token_slots, query_rows, token_block),
        out_shape=jax.ShapeDtypeStruct((page_total, total_queries), jnp.float32),
        in_specs=[pl.BlockSpec(memory_space=pltpu.SMEM), vmem, vmem],
        out_specs=vmem,
        scratch_shapes=[
            pltpu.VMEM((ordered_rows, width), jnp.bfloat16),
            pltpu.VMEM((ordered_rows, token_block), jnp.float32),
        ],
        cost_estimate=pl.CostEstimate(
            flops=2 * ordered_rows * width * (owners * capacity + token_total),
            bytes_accessed=2 * received.size + 2 * tokens.size + 4 * page_total * total_queries,
            transcendentals=0,
        ),
    )(table, received, tokens)


def shards(patch_rows, owner_ids, page_ids, proj_weight, proj_bias, query_tokens, query_counts):
    owners = lax.axis_size("blk")
    halves = lax.axis_size("inner")
    rows = patch_rows.shape[0]
    capacity = 2 * rows // owners
    per_block = query_tokens.shape[0]
    token_slots = query_tokens.shape[1]
    width = query_tokens.shape[2]
    total_queries = per_block * owners
    half_queries = per_block // halves
    query_rows = half_queries * token_slots
    message = send_message(
        patch_rows, owner_ids, page_ids, proj_weight, proj_bias, query_tokens, query_counts, owners, capacity, halves
    )
    received = lax.all_to_all(message, "blk", split_axis=0, concat_axis=0, tiled=True)
    halves_in = lax.all_gather(received[:, :query_rows], "inner", axis=1, tiled=True)
    block_at = -(-(query_rows + capacity) // 16) * 16
    combos = -(-owners * PAGES_DEV // 128) * 128
    count_rows = combos // 128
    page_counts = received[:, block_at : block_at + count_rows].reshape(owners, combos)
    page_counts = lax.dynamic_slice_in_dim(page_counts, lax.axis_index("blk") * PAGES_DEV, PAGES_DEV, axis=1)
    counts = received[:, block_at + count_rows, :per_block]
    table = jnp.concatenate([page_counts.reshape(owners * PAGES_DEV), counts.reshape(total_queries)]).astype(jnp.int32)
    return page_scores(received, halves_in, table, total_queries, PAGES_DEV, token_slots, query_rows, capacity)


def solution(mesh):
    in_specs = (
        P(("groups", "blk", "inner"), None),
        P(("groups", "blk", "inner"), None),
        P(("groups", "blk", "inner")),
        P(),
        P(),
        P(("groups", "blk"), None, None),
        P(("groups", "blk")),
    )
    out_specs = P(("groups", "blk", "inner"), None)
    return jax.shard_map(shards, mesh=mesh, in_specs=in_specs, out_specs=out_specs, check_vma=False)
```

```python
import functools
import math

import jax
import jax.numpy as jnp
from jax import lax
from jax.experimental import pallas as pl
from jax.experimental.pallas import tpu as pltpu
from jax.sharding import PartitionSpec as P

PAGES_DEV = 8


def send_kernel(page_total, capacity, query_rows, block_at, query_counts_ref, owner_ref, page_ref, rows_ref, weight_ref,
                bias_ref, queries_ref, message_ref, local_ref):
    step = pl.program_id(0)
    row_block = rows_ref.shape[0]
    proj = jnp.dot(rows_ref[...], weight_ref[...], preferred_element_type=jnp.float32) + bias_ref[...]
    scale = lax.rsqrt(jnp.sum(proj * proj, axis=1, keepdims=True) + 1e-06)
    local_ref[pl.ds(pl.multiple_of(step * row_block, row_block), row_block), :] = (proj * scale).astype(jnp.bfloat16)

    @pl.when(step == pl.num_programs(0) - 1)
    def _():
        send_layout(page_total, capacity, query_rows, block_at, query_counts_ref, owner_ref, page_ref, queries_ref,
                    message_ref, local_ref[...])


def send_layout(page_total, capacity, query_rows, block_at, query_counts_ref, owner_ref, page_ref, queries_ref,
                message_ref, local):
    owners = message_ref.shape[0]
    rows = local.shape[0]
    combo = owner_ref[...].reshape(1, rows) * page_total + page_ref[...].reshape(1, rows)
    combos = -(-owners * page_total // 128) * 128
    combo_id = lax.broadcasted_iota(jnp.int32, (combos, rows), 0)
    onehot = (combo == combo_id).astype(jnp.bfloat16)
    earlier = (
        lax.broadcasted_iota(jnp.int32, (rows, rows), 0) < lax.broadcasted_iota(jnp.int32, (rows, rows), 1)
    ).astype(jnp.bfloat16)
    seen = jnp.dot(onehot, earlier, preferred_element_type=jnp.float32)
    count = jnp.sum(onehot.astype(jnp.float32), axis=1, keepdims=True)
    row_id = lax.broadcasted_iota(jnp.int32, (combos, combos), 0)
    col_id = lax.broadcasted_iota(jnp.int32, (combos, combos), 1)
    same_owner_lower = (row_id // page_total == col_id // page_total) & (col_id % page_total < row_id % page_total)
    offset = jnp.dot(same_owner_lower.astype(jnp.bfloat16), count.astype(jnp.bfloat16),
                     preferred_element_type=jnp.float32)
    base = (lax.broadcasted_iota(jnp.int32, (combos, 1), 0) // page_total * capacity).astype(jnp.float32) + offset
    slot = jnp.sum(onehot.astype(jnp.float32) * (base + seen), axis=0, keepdims=True).astype(jnp.int32)
    count_rows = [
        lax.dot_general(
            jnp.ones((1, rows), jnp.bfloat16), onehot[group * 128 : (group + 1) * 128],
            (((1,), (1,)), ((), ())), preferred_element_type=jnp.float32,
        )
        for group in range(combos // 128)
    ]
    lane = lax.broadcasted_iota(jnp.int32, (1, 128), 1)
    query_count_row = jnp.zeros((1, 128), jnp.float32)
    for query in range(query_counts_ref.shape[0]):
        query_count_row = jnp.where(lane == query, query_counts_ref[query].astype(jnp.float32), query_count_row)
    block_rows = message_ref.shape[1] - block_at
    block = jnp.concatenate(
        count_rows
        + [query_count_row, jnp.zeros((block_rows - len(count_rows) - 1, 128), jnp.float32)],
        axis=0,
    ).astype(jnp.bfloat16)
    own_half = queries_ref[pl.ds(pl.multiple_of(lax.axis_index("inner") * query_rows, query_rows), query_rows), :]
    slot_id = lax.broadcasted_iota(jnp.int32, (capacity, rows), 0)
    for owner in range(owners):
        placed = (slot == slot_id + owner * capacity).astype(jnp.bfloat16)
        message_ref[owner, 0:query_rows, :] = own_half
        message_ref[owner, query_rows : query_rows + capacity, :] = jnp.dot(
            placed, local, preferred_element_type=jnp.float32
        ).astype(jnp.bfloat16)
        message_ref[owner, block_at:, :] = block


def send_message(patch_rows, owner_ids, page_ids, proj_weight, proj_bias, query_tokens, query_counts, owners, capacity,
                 halves):
    rows, features = patch_rows.shape
    per_block, token_slots, width = query_tokens.shape
    query_rows = per_block // halves * token_slots
    block_at = -(-(query_rows + capacity) // 16) * 16
    row_block = 128 if rows % 128 == 0 else rows
    message_rows = block_at + 16
    whole = lambda *shape: pl.BlockSpec(shape, lambda i: (0,) * len(shape))
    return pl.pallas_call(
        functools.partial(send_kernel, PAGES_DEV, capacity, query_rows, block_at),
        out_shape=jax.ShapeDtypeStruct((owners, message_rows, width), jnp.bfloat16),
        grid=(rows // row_block,),
        in_specs=[
            pl.BlockSpec(memory_space=pltpu.SMEM),
            whole(rows),
            whole(rows),
            pl.BlockSpec((row_block, features), lambda i: (i, 0)),
            whole(features, width),
            whole(1, width),
            whole(per_block * token_slots, width),
        ],
        out_specs=whole(owners, message_rows, width),
        scratch_shapes=[pltpu.VMEM((rows, width), jnp.bfloat16)],
        cost_estimate=pl.CostEstimate(
            flops=2 * rows * width * (features + owners * capacity),
            bytes_accessed=2 * (rows * features + features * width + owners * (block_at + 16) * width),
            transcendentals=rows,
        ),
    )(
        query_counts, owner_ids.reshape(rows), page_ids, patch_rows, proj_weight, proj_bias.reshape(1, width),
        query_tokens.reshape(per_block * token_slots, width),
    )


def score_kernel(page_total, token_slots, query_rows, token_block, table_ref, received_ref, tokens_ref, out_ref,
                 ordered_ref, sims_ref):
    owners = received_ref.shape[0]
    ordered_rows, width = ordered_ref.shape
    capacity = (ordered_rows - 16 * page_total - 16) // owners
    total_queries = out_ref.shape[1]
    totals = [sum(table_ref[chunk * page_total + page] for chunk in range(owners)) for page in range(page_total)]
    firsts = []
    at = 0
    for page in range(page_total):
        firsts.append(at)
        at = at + (totals[page] + 15) // 16 * 16
    target = lax.broadcasted_iota(jnp.int32, (ordered_rows, capacity), 0)
    slot = lax.broadcasted_iota(jnp.int32, (1, capacity), 1)
    ordered = jnp.zeros((ordered_rows, width), jnp.float32)
    before = [0] * page_total
    for chunk in range(owners):
        position = jnp.full((1, capacity), -1, jnp.int32)
        low = 0
        for page in range(page_total):
            high = low + table_ref[chunk * page_total + page]
            inside = (slot >= low) & (slot < high)
            position = jnp.where(inside, slot + (firsts[page] + before[page] - low), position)
            before[page] = before[page] + (high - low)
            low = high
        place = (position == target).astype(jnp.bfloat16)
        rows = received_ref[chunk, query_rows : query_rows + capacity, :]
        ordered = ordered + jnp.dot(place, rows, preferred_element_type=jnp.float32)
    ordered_ref[...] = ordered.astype(jnp.bfloat16)
    sources = token_block // tokens_ref.shape[1]
    sub = lax.broadcasted_iota(jnp.int32, (8, token_block), 0)
    query_lane = lax.broadcasted_iota(jnp.int32, (1, total_queries), 1)
    live_count = jnp.zeros((1, total_queries), jnp.int32)
    for query in range(total_queries):
        live_count = jnp.where(query_lane == query, table_ref[owners * page_total + query], live_count)
    token_id = lax.broadcasted_iota(jnp.int32, (token_block, total_queries), 0)
    query_id = lax.broadcasted_iota(jnp.int32, (token_block, total_queries), 1)

    def block_scores(block, total):
        tokens = tokens_ref[pl.ds(block * sources, sources)].reshape(token_block, width)
        sims_ref[...] = lax.dot_general(
            ordered_ref[...], tokens, (((1,), (1,)), ((), ())), preferred_element_type=jnp.float32
        )
        best_rows = []
        for page in range(page_total):
            first = firsts[page]
            whole = totals[page] // 16
            rest = totals[page] % 16

            def step(i, carry):
                start = pl.multiple_of(first + i * 16, 16)
                return (
                    jnp.maximum(carry[0], sims_ref[pl.ds(start, 8), :]),
                    jnp.maximum(carry[1], sims_ref[pl.ds(start + 8, 8), :]),
                )

            floor = jnp.full((8, token_block), -2.0, jnp.float32)
            low, high = lax.fori_loop(0, whole, step, (floor, floor))
            start = pl.multiple_of(first + whole * 16, 16)
            low = jnp.maximum(low, jnp.where(sub < rest, sims_ref[pl.ds(start, 8), :], jnp.float32(-2.0)))
            high = jnp.maximum(high, jnp.where(sub + 8 < rest, sims_ref[pl.ds(start + 8, 8), :], jnp.float32(-2.0)))
            best_rows.append(jnp.max(jnp.maximum(low, high), axis=0, keepdims=True))
        best = jnp.concatenate(best_rows, axis=0)
        token = token_id + block * token_block
        live = ((token // token_slots) == query_id) & ((token % token_slots) < live_count)
        return total + jnp.dot(
            best, live.astype(jnp.float32), precision=lax.Precision.HIGHEST, preferred_element_type=jnp.float32
        )

    blocks = tokens_ref.shape[0] * tokens_ref.shape[1] // token_block
    out_ref[...] = lax.fori_loop(
        0, blocks, block_scores, jnp.zeros((page_total, total_queries), jnp.float32)
    )


def page_scores(received, tokens, table, total_queries, page_total, token_slots, query_rows, capacity):
    owners = received.shape[0]
    width = received.shape[2]
    ordered_rows = owners * capacity + 16 * page_total + 16
    token_total = tokens.shape[0] * tokens.shape[1]
    token_block = min(token_total, 1024)
    vmem = pl.BlockSpec(memory_space=pltpu.VMEM)
    return pl.pallas_call(
        functools.partial(score_kernel, page_total, token_slots, query_rows, token_block),
        out_shape=jax.ShapeDtypeStruct((page_total, total_queries), jnp.float32),
        in_specs=[pl.BlockSpec(memory_space=pltpu.SMEM), vmem, vmem],
        out_specs=vmem,
        scratch_shapes=[
            pltpu.VMEM((ordered_rows, width), jnp.bfloat16),
            pltpu.VMEM((ordered_rows, token_block), jnp.float32),
        ],
        cost_estimate=pl.CostEstimate(
            flops=2 * ordered_rows * width * (owners * capacity + token_total),
            bytes_accessed=2 * received.size + 2 * tokens.size + 4 * page_total * total_queries,
            transcendentals=0,
        ),
    )(table, received, tokens)


def shards(patch_rows, owner_ids, page_ids, proj_weight, proj_bias, query_tokens, query_counts):
    owners = lax.axis_size("blk")
    halves = lax.axis_size("inner")
    rows = patch_rows.shape[0]
    capacity = 2 * rows // owners
    per_block = query_tokens.shape[0]
    token_slots = query_tokens.shape[1]
    width = query_tokens.shape[2]
    total_queries = per_block * owners
    half_queries = per_block // halves
    query_rows = half_queries * token_slots
    message = send_message(
        patch_rows, owner_ids, page_ids, proj_weight, proj_bias, query_tokens, query_counts, owners, capacity, halves
    )
    received = lax.all_to_all(message, "blk", split_axis=0, concat_axis=0, tiled=True)
    halves_in = lax.all_gather(received[:, :query_rows], "inner", axis=1, tiled=True)
    block_at = -(-(query_rows + capacity) // 16) * 16
    combos = -(-owners * PAGES_DEV // 128) * 128
    count_rows = combos // 128
    page_counts = received[:, block_at : block_at + count_rows].reshape(owners, combos)
    page_counts = lax.dynamic_slice_in_dim(page_counts, lax.axis_index("blk") * PAGES_DEV, PAGES_DEV, axis=1)
    counts = received[:, block_at + count_rows, :per_block]
    table = jnp.concatenate([page_counts.reshape(owners * PAGES_DEV), counts.reshape(total_queries)]).astype(jnp.int32)
    return page_scores(received, halves_in, table, total_queries, PAGES_DEV, token_slots, query_rows, capacity)


def solution(mesh):
    in_specs = (
        P(("groups", "blk", "inner"), None),
        P(("groups", "blk", "inner"), None),
        P(("groups", "blk", "inner")),
        P(),
        P(),
        P(("groups", "blk"), None, None),
        P(("groups", "blk")),
    )
    out_specs = P(("groups", "blk", "inner"), None)
    return jax.shard_map(shards, mesh=mesh, in_specs=in_specs, out_specs=out_specs, check_vma=False)
```

```python
import functools
import math

import jax
import jax.numpy as jnp
from jax import lax
from jax.experimental import pallas as pl
from jax.experimental.pallas import tpu as pltpu
from jax.sharding import PartitionSpec as P

PAGES_DEV = 8


def send_kernel(page_total, capacity, query_rows, block_at, query_counts_ref, owner_ref, page_ref, rows_ref, weight_ref,
                bias_ref, queries_ref, message_ref):
    owners = message_ref.shape[0]
    rows = rows_ref.shape[0]
    proj = jnp.dot(rows_ref[...], weight_ref[...], preferred_element_type=jnp.float32) + bias_ref[...]
    scale = lax.rsqrt(jnp.sum(proj * proj, axis=1, keepdims=True) + 1e-06)
    local = (proj * scale).astype(jnp.bfloat16)
    combo = owner_ref[...].reshape(1, rows) * page_total + page_ref[...].reshape(1, rows)
    combos = -(-owners * page_total // 128) * 128
    combo_id = lax.broadcasted_iota(jnp.int32, (combos, rows), 0)
    onehot = (combo == combo_id).astype(jnp.bfloat16)
    earlier = (
        lax.broadcasted_iota(jnp.int32, (rows, rows), 0) < lax.broadcasted_iota(jnp.int32, (rows, rows), 1)
    ).astype(jnp.bfloat16)
    seen = jnp.dot(onehot, earlier, preferred_element_type=jnp.float32)
    count = jnp.sum(onehot.astype(jnp.float32), axis=1, keepdims=True)
    row_id = lax.broadcasted_iota(jnp.int32, (combos, combos), 0)
    col_id = lax.broadcasted_iota(jnp.int32, (combos, combos), 1)
    same_owner_lower = (row_id // page_total == col_id // page_total) & (col_id % page_total < row_id % page_total)
    offset = jnp.dot(same_owner_lower.astype(jnp.bfloat16), count.astype(jnp.bfloat16),
                     preferred_element_type=jnp.float32)
    base = (lax.broadcasted_iota(jnp.int32, (combos, 1), 0) // page_total * capacity).astype(jnp.float32) + offset
    slot = jnp.sum(onehot.astype(jnp.float32) * (base + seen), axis=0, keepdims=True).astype(jnp.int32)
    count_rows = [
        lax.dot_general(
            jnp.ones((1, rows), jnp.bfloat16), onehot[group * 128 : (group + 1) * 128],
            (((1,), (1,)), ((), ())), preferred_element_type=jnp.float32,
        )
        for group in range(combos // 128)
    ]
    lane = lax.broadcasted_iota(jnp.int32, (1, 128), 1)
    query_count_row = jnp.zeros((1, 128), jnp.float32)
    for query in range(query_counts_ref.shape[0]):
        query_count_row = jnp.where(lane == query, query_counts_ref[query].astype(jnp.float32), query_count_row)
    block_rows = message_ref.shape[1] - block_at
    block = jnp.concatenate(
        count_rows
        + [query_count_row, jnp.zeros((block_rows - len(count_rows) - 1, 128), jnp.float32)],
        axis=0,
    ).astype(jnp.bfloat16)
    own_half = queries_ref[pl.ds(pl.multiple_of(lax.axis_index("inner") * query_rows, query_rows), query_rows), :]
    slot_id = lax.broadcasted_iota(jnp.int32, (capacity, rows), 0)
    for owner in range(owners):
        placed = (slot == slot_id + owner * capacity).astype(jnp.bfloat16)
        message_ref[owner, 0:query_rows, :] = own_half
        message_ref[owner, query_rows : query_rows + capacity, :] = jnp.dot(
            placed, local, preferred_element_type=jnp.float32
        ).astype(jnp.bfloat16)
        message_ref[owner, block_at:, :] = block


def send_message(patch_rows, owner_ids, page_ids, proj_weight, proj_bias, query_tokens, query_counts, owners, capacity,
                 halves):
    rows, features = patch_rows.shape
    per_block, token_slots, width = query_tokens.shape
    query_rows = per_block // halves * token_slots
    block_at = -(-(query_rows + capacity) // 16) * 16
    vmem = pl.BlockSpec(memory_space=pltpu.VMEM)
    return pl.pallas_call(
        functools.partial(send_kernel, PAGES_DEV, capacity, query_rows, block_at),
        out_shape=jax.ShapeDtypeStruct((owners, block_at + 16, width), jnp.bfloat16),
        in_specs=[pl.BlockSpec(memory_space=pltpu.SMEM)] + [vmem] * 6,
        out_specs=vmem,
        cost_estimate=pl.CostEstimate(
            flops=2 * rows * width * (features + owners * capacity),
            bytes_accessed=2 * (rows * features + features * width + owners * (block_at + 16) * width),
            transcendentals=rows,
        ),
    )(
        query_counts, owner_ids.reshape(rows), page_ids, patch_rows, proj_weight, proj_bias.reshape(1, width),
        query_tokens.reshape(per_block * token_slots, width),
    )


def score_kernel(page_total, token_slots, query_rows, token_block, table_ref, received_ref, tokens_ref, out_ref,
                 ordered_ref, sims_ref, rows_ref):
    owners = received_ref.shape[0]
    ordered_rows, width = ordered_ref.shape
    capacity = (ordered_rows - 16 * page_total - 16) // owners
    total_queries = out_ref.shape[1]
    totals = [sum(table_ref[chunk * page_total + page] for chunk in range(owners)) for page in range(page_total)]
    firsts = []
    at = 0
    for page in range(page_total):
        firsts.append(at)
        at = at + (totals[page] + 15) // 16 * 16
    slot = lax.broadcasted_iota(jnp.int32, (1, capacity), 1)
    before = [0] * page_total
    positions = []
    for chunk in range(owners):
        position = jnp.full((1, capacity), -1, jnp.int32)
        low = 0
        for page in range(page_total):
            high = low + table_ref[chunk * page_total + page]
            inside = (slot >= low) & (slot < high)
            position = jnp.where(inside, slot + (firsts[page] + before[page] - low), position)
            before[page] = before[page] + (high - low)
            low = high
        positions.append(position)
        rows_ref[chunk * capacity : (chunk + 1) * capacity, :] = received_ref[chunk, query_rows : query_rows + capacity, :]
    position = jnp.concatenate(positions, axis=1)
    place = (position == lax.broadcasted_iota(jnp.int32, (ordered_rows, owners * capacity), 0)).astype(jnp.bfloat16)
    ordered_ref[...] = jnp.dot(place, rows_ref[...], preferred_element_type=jnp.float32).astype(jnp.bfloat16)
    sources = token_block // tokens_ref.shape[1]
    sub = lax.broadcasted_iota(jnp.int32, (8, token_block), 0)
    query_lane = lax.broadcasted_iota(jnp.int32, (1, total_queries), 1)
    live_count = jnp.zeros((1, total_queries), jnp.int32)
    for query in range(total_queries):
        live_count = jnp.where(query_lane == query, table_ref[owners * page_total + query], live_count)
    token_id = lax.broadcasted_iota(jnp.int32, (token_block, total_queries), 0)
    query_id = lax.broadcasted_iota(jnp.int32, (token_block, total_queries), 1)

    def block_scores(block, total):
        tokens = tokens_ref[pl.ds(block * sources, sources)].reshape(token_block, width)
        sims_ref[...] = lax.dot_general(
            ordered_ref[...], tokens, (((1,), (1,)), ((), ())), preferred_element_type=jnp.float32
        )
        best_rows = []
        for page in range(page_total):
            first = firsts[page]
            whole = totals[page] // 16
            rest = totals[page] % 16

            def step(i, carry):
                start = pl.multiple_of(first + i * 16, 16)
                return (
                    jnp.maximum(carry[0], sims_ref[pl.ds(start, 8), :]),
                    jnp.maximum(carry[1], sims_ref[pl.ds(start + 8, 8), :]),
                )

            floor = jnp.full((8, token_block), -2.0, jnp.float32)
            low, high = lax.fori_loop(0, whole, step, (floor, floor))
            start = pl.multiple_of(first + whole * 16, 16)
            low = jnp.maximum(low, jnp.where(sub < rest, sims_ref[pl.ds(start, 8), :], jnp.float32(-2.0)))
            high = jnp.maximum(high, jnp.where(sub + 8 < rest, sims_ref[pl.ds(start + 8, 8), :], jnp.float32(-2.0)))
            best_rows.append(jnp.max(jnp.maximum(low, high), axis=0, keepdims=True))
        best = jnp.concatenate(best_rows, axis=0)
        token = token_id + block * token_block
        live = ((token // token_slots) == query_id) & ((token % token_slots) < live_count)
        return total + jnp.dot(
            best, live.astype(jnp.float32), precision=lax.Precision.HIGHEST, preferred_element_type=jnp.float32
        )

    blocks = tokens_ref.shape[0] * tokens_ref.shape[1] // token_block
    out_ref[...] = lax.fori_loop(
        0, blocks, block_scores, jnp.zeros((page_total, total_queries), jnp.float32)
    )


def page_scores(received, tokens, table, total_queries, page_total, token_slots, query_rows, capacity):
    owners = received.shape[0]
    width = received.shape[2]
    ordered_rows = owners * capacity + 16 * page_total + 16
    token_total = tokens.shape[0] * tokens.shape[1]
    token_block = min(token_total, 1024)
    vmem = pl.BlockSpec(memory_space=pltpu.VMEM)
    return pl.pallas_call(
        functools.partial(score_kernel, page_total, token_slots, query_rows, token_block),
        out_shape=jax.ShapeDtypeStruct((page_total, total_queries), jnp.float32),
        in_specs=[pl.BlockSpec(memory_space=pltpu.SMEM), vmem, vmem],
        out_specs=vmem,
        scratch_shapes=[
            pltpu.VMEM((ordered_rows, width), jnp.bfloat16),
            pltpu.VMEM((ordered_rows, token_block), jnp.float32),
            pltpu.VMEM((owners * capacity, width), jnp.bfloat16),
        ],
        cost_estimate=pl.CostEstimate(
            flops=2 * ordered_rows * width * (owners * capacity + token_total),
            bytes_accessed=2 * received.size + 2 * tokens.size + 4 * page_total * total_queries,
            transcendentals=0,
        ),
    )(table, received, tokens)


def shards(patch_rows, owner_ids, page_ids, proj_weight, proj_bias, query_tokens, query_counts):
    owners = lax.axis_size("blk")
    halves = lax.axis_size("inner")
    rows = patch_rows.shape[0]
    capacity = 2 * rows // owners
    per_block = query_tokens.shape[0]
    token_slots = query_tokens.shape[1]
    width = query_tokens.shape[2]
    total_queries = per_block * owners
    half_queries = per_block // halves
    query_rows = half_queries * token_slots
    message = send_message(
        patch_rows, owner_ids, page_ids, proj_weight, proj_bias, query_tokens, query_counts, owners, capacity, halves
    )
    received = lax.all_to_all(message, "blk", split_axis=0, concat_axis=0, tiled=True)
    halves_in = lax.all_gather(received[:, :query_rows], "inner", axis=1, tiled=True)
    block_at = -(-(query_rows + capacity) // 16) * 16
    combos = -(-owners * PAGES_DEV // 128) * 128
    count_rows = combos // 128
    page_counts = received[:, block_at : block_at + count_rows].reshape(owners, combos)
    page_counts = lax.dynamic_slice_in_dim(page_counts, lax.axis_index("blk") * PAGES_DEV, PAGES_DEV, axis=1)
    counts = received[:, block_at + count_rows, :per_block]
    table = jnp.concatenate([page_counts.reshape(owners * PAGES_DEV), counts.reshape(total_queries)]).astype(jnp.int32)
    return page_scores(received, halves_in, table, total_queries, PAGES_DEV, token_slots, query_rows, capacity)


def solution(mesh):
    in_specs = (
        P(("groups", "blk", "inner"), None),
        P(("groups", "blk", "inner"), None),
        P(("groups", "blk", "inner")),
        P(),
        P(),
        P(("groups", "blk"), None, None),
        P(("groups", "blk")),
    )
    out_specs = P(("groups", "blk", "inner"), None)
    return jax.shard_map(shards, mesh=mesh, in_specs=in_specs, out_specs=out_specs, check_vma=False)
```

```python
import functools
import math

import jax
import jax.numpy as jnp
from jax import lax
from jax.experimental import pallas as pl
from jax.experimental.pallas import tpu as pltpu
from jax.sharding import PartitionSpec as P

PAGES_DEV = 8


def send_kernel(page_total, capacity, query_rows, block_at, query_counts_ref, owner_ref, page_ref, rows_ref, weight_ref,
                bias_ref, queries_ref, message_ref):
    owners = message_ref.shape[0]
    rows = rows_ref.shape[0]
    proj = jnp.dot(rows_ref[...], weight_ref[...], preferred_element_type=jnp.float32) + bias_ref[...]
    scale = lax.rsqrt(jnp.sum(proj * proj, axis=1, keepdims=True) + 1e-06)
    local = (proj * scale).astype(jnp.bfloat16)
    combo = owner_ref[...].reshape(1, rows) * page_total + page_ref[...].reshape(1, rows)
    combos = -(-owners * page_total // 128) * 128
    combo_id = lax.broadcasted_iota(jnp.int32, (combos, rows), 0)
    onehot = (combo == combo_id).astype(jnp.bfloat16)
    earlier = (
        lax.broadcasted_iota(jnp.int32, (rows, rows), 0) < lax.broadcasted_iota(jnp.int32, (rows, rows), 1)
    ).astype(jnp.bfloat16)
    seen = jnp.dot(onehot, earlier, preferred_element_type=jnp.float32)
    count = jnp.sum(onehot.astype(jnp.float32), axis=1, keepdims=True)
    row_id = lax.broadcasted_iota(jnp.int32, (combos, combos), 0)
    col_id = lax.broadcasted_iota(jnp.int32, (combos, combos), 1)
    same_owner_lower = (row_id // page_total == col_id // page_total) & (col_id % page_total < row_id % page_total)
    offset = jnp.dot(same_owner_lower.astype(jnp.bfloat16), count.astype(jnp.bfloat16),
                     preferred_element_type=jnp.float32)
    base = (lax.broadcasted_iota(jnp.int32, (combos, 1), 0) // page_total * capacity).astype(jnp.float32) + offset
    slot = jnp.sum(onehot.astype(jnp.float32) * (base + seen), axis=0, keepdims=True).astype(jnp.int32)
    count_rows = [
        lax.dot_general(
            jnp.ones((1, rows), jnp.bfloat16), onehot[group * 128 : (group + 1) * 128],
            (((1,), (1,)), ((), ())), preferred_element_type=jnp.float32,
        )
        for group in range(combos // 128)
    ]
    lane = lax.broadcasted_iota(jnp.int32, (1, 128), 1)
    query_count_row = jnp.zeros((1, 128), jnp.float32)
    for query in range(query_counts_ref.shape[0]):
        query_count_row = jnp.where(lane == query, query_counts_ref[query].astype(jnp.float32), query_count_row)
    block_rows = message_ref.shape[1] - block_at
    block = jnp.concatenate(
        count_rows
        + [query_count_row, jnp.zeros((block_rows - len(count_rows) - 1, 128), jnp.float32)],
        axis=0,
    ).astype(jnp.bfloat16)
    own_half = queries_ref[pl.ds(pl.multiple_of(lax.axis_index("inner") * query_rows, query_rows), query_rows), :]
    slot_id = lax.broadcasted_iota(jnp.int32, (capacity, rows), 0)
    for owner in range(owners):
        placed = (slot == slot_id + owner * capacity).astype(jnp.bfloat16)
        message_ref[owner, 0:query_rows, :] = own_half
        message_ref[owner, query_rows : query_rows + capacity, :] = jnp.dot(
            placed, local, preferred_element_type=jnp.float32
        ).astype(jnp.bfloat16)
        message_ref[owner, block_at:, :] = block


def send_message(patch_rows, owner_ids, page_ids, proj_weight, proj_bias, query_tokens, query_counts, owners, capacity,
                 halves):
    rows, features = patch_rows.shape
    per_block, token_slots, width = query_tokens.shape
    query_rows = per_block // halves * token_slots
    block_at = -(-(query_rows + capacity) // 16) * 16
    vmem = pl.BlockSpec(memory_space=pltpu.VMEM)
    return pl.pallas_call(
        functools.partial(send_kernel, PAGES_DEV, capacity, query_rows, block_at),
        out_shape=jax.ShapeDtypeStruct((owners, block_at + 16, width), jnp.bfloat16),
        in_specs=[pl.BlockSpec(memory_space=pltpu.SMEM)] + [vmem] * 6,
        out_specs=vmem,
        cost_estimate=pl.CostEstimate(
            flops=2 * rows * width * (features + owners * capacity),
            bytes_accessed=2 * (rows * features + features * width + owners * (block_at + 16) * width),
            transcendentals=rows,
        ),
    )(
        query_counts, owner_ids.reshape(1, rows), page_ids, patch_rows, proj_weight, proj_bias.reshape(1, width),
        query_tokens.reshape(per_block * token_slots, width),
    )


def score_kernel(page_total, token_slots, query_rows, token_block, table_ref, received_ref, tokens_ref, out_ref,
                 ordered_ref, sims_ref, rows_ref):
    owners = received_ref.shape[0]
    ordered_rows, width = ordered_ref.shape
    capacity = (ordered_rows - 16 * page_total - 16) // owners
    total_queries = out_ref.shape[1]
    totals = [sum(table_ref[chunk * page_total + page] for chunk in range(owners)) for page in range(page_total)]
    firsts = []
    at = 0
    for page in range(page_total):
        firsts.append(at)
        at = at + (totals[page] + 15) // 16 * 16
    slot = lax.broadcasted_iota(jnp.int32, (1, capacity), 1)
    before = [0] * page_total
    positions = []
    for chunk in range(owners):
        position = jnp.full((1, capacity), -1, jnp.int32)
        low = 0
        for page in range(page_total):
            high = low + table_ref[chunk * page_total + page]
            inside = (slot >= low) & (slot < high)
            position = jnp.where(inside, slot + (firsts[page] + before[page] - low), position)
            before[page] = before[page] + (high - low)
            low = high
        positions.append(position)
        rows_ref[chunk * capacity : (chunk + 1) * capacity, :] = received_ref[chunk, query_rows : query_rows + capacity, :]
    position = jnp.concatenate(positions, axis=1)
    place = (position == lax.broadcasted_iota(jnp.int32, (ordered_rows, owners * capacity), 0)).astype(jnp.bfloat16)
    ordered_ref[...] = jnp.dot(place, rows_ref[...], preferred_element_type=jnp.float32).astype(jnp.bfloat16)
    sources = token_block // tokens_ref.shape[1]
    sub = lax.broadcasted_iota(jnp.int32, (8, token_block), 0)
    query_lane = lax.broadcasted_iota(jnp.int32, (1, total_queries), 1)
    live_count = jnp.zeros((1, total_queries), jnp.int32)
    for query in range(total_queries):
        live_count = jnp.where(query_lane == query, table_ref[owners * page_total + query], live_count)
    token_id = lax.broadcasted_iota(jnp.int32, (token_block, total_queries), 0)
    query_id = lax.broadcasted_iota(jnp.int32, (token_block, total_queries), 1)

    def block_scores(block, total):
        tokens = tokens_ref[pl.ds(block * sources, sources)].reshape(token_block, width)
        sims_ref[...] = lax.dot_general(
            ordered_ref[...], tokens, (((1,), (1,)), ((), ())), preferred_element_type=jnp.float32
        )
        best_rows = []
        for page in range(page_total):
            first = firsts[page]
            whole = totals[page] // 16
            rest = totals[page] % 16

            def step(i, carry):
                start = pl.multiple_of(first + i * 16, 16)
                return (
                    jnp.maximum(carry[0], sims_ref[pl.ds(start, 8), :]),
                    jnp.maximum(carry[1], sims_ref[pl.ds(start + 8, 8), :]),
                )

            floor = jnp.full((8, token_block), -2.0, jnp.float32)
            low, high = lax.fori_loop(0, whole, step, (floor, floor))
            start = pl.multiple_of(first + whole * 16, 16)
            low = jnp.maximum(low, jnp.where(sub < rest, sims_ref[pl.ds(start, 8), :], jnp.float32(-2.0)))
            high = jnp.maximum(high, jnp.where(sub + 8 < rest, sims_ref[pl.ds(start + 8, 8), :], jnp.float32(-2.0)))
            best_rows.append(jnp.max(jnp.maximum(low, high), axis=0, keepdims=True))
        best = jnp.concatenate(best_rows, axis=0)
        token = token_id + block * token_block
        live = ((token // token_slots) == query_id) & ((token % token_slots) < live_count)
        return total + jnp.dot(
            best, live.astype(jnp.float32), precision=lax.Precision.HIGHEST, preferred_element_type=jnp.float32
        )

    blocks = tokens_ref.shape[0] * tokens_ref.shape[1] // token_block
    out_ref[...] = lax.fori_loop(
        0, blocks, block_scores, jnp.zeros((page_total, total_queries), jnp.float32)
    )


def page_scores(received, tokens, table, total_queries, page_total, token_slots, query_rows, capacity):
    owners = received.shape[0]
    width = received.shape[2]
    ordered_rows = owners * capacity + 16 * page_total + 16
    token_total = tokens.shape[0] * tokens.shape[1]
    token_block = min(token_total, 1024)
    vmem = pl.BlockSpec(memory_space=pltpu.VMEM)
    return pl.pallas_call(
        functools.partial(score_kernel, page_total, token_slots, query_rows, token_block),
        out_shape=jax.ShapeDtypeStruct((page_total, total_queries), jnp.float32),
        in_specs=[pl.BlockSpec(memory_space=pltpu.SMEM), vmem, vmem],
        out_specs=vmem,
        scratch_shapes=[
            pltpu.VMEM((ordered_rows, width), jnp.bfloat16),
            pltpu.VMEM((ordered_rows, token_block), jnp.float32),
            pltpu.VMEM((owners * capacity, width), jnp.bfloat16),
        ],
        cost_estimate=pl.CostEstimate(
            flops=2 * ordered_rows * width * (owners * capacity + token_total),
            bytes_accessed=2 * received.size + 2 * tokens.size + 4 * page_total * total_queries,
            transcendentals=0,
        ),
    )(table, received, tokens)


def shards(patch_rows, owner_ids, page_ids, proj_weight, proj_bias, query_tokens, query_counts):
    owners = lax.axis_size("blk")
    halves = lax.axis_size("inner")
    rows = patch_rows.shape[0]
    capacity = 2 * rows // owners
    per_block = query_tokens.shape[0]
    token_slots = query_tokens.shape[1]
    width = query_tokens.shape[2]
    total_queries = per_block * owners
    half_queries = per_block // halves
    query_rows = half_queries * token_slots
    message = send_message(
        patch_rows, owner_ids, page_ids, proj_weight, proj_bias, query_tokens, query_counts, owners, capacity, halves
    )
    received = lax.all_to_all(message, "blk", split_axis=0, concat_axis=0, tiled=True)
    halves_in = lax.all_gather(received[:, :query_rows], "inner", axis=1, tiled=True)
    block_at = -(-(query_rows + capacity) // 16) * 16
    combos = -(-owners * PAGES_DEV // 128) * 128
    count_rows = combos // 128
    page_counts = received[:, block_at : block_at + count_rows].reshape(owners, combos)
    page_counts = lax.dynamic_slice_in_dim(page_counts, lax.axis_index("blk") * PAGES_DEV, PAGES_DEV, axis=1)
    counts = received[:, block_at + count_rows, :per_block]
    table = jnp.concatenate([page_counts.reshape(owners * PAGES_DEV), counts.reshape(total_queries)]).astype(jnp.int32)
    return page_scores(received, halves_in, table, total_queries, PAGES_DEV, token_slots, query_rows, capacity)


def solution(mesh):
    in_specs = (
        P(("groups", "blk", "inner"), None),
        P(("groups", "blk", "inner"), None),
        P(("groups", "blk", "inner")),
        P(),
        P(),
        P(("groups", "blk"), None, None),
        P(("groups", "blk")),
    )
    out_specs = P(("groups", "blk", "inner"), None)
    return jax.shard_map(shards, mesh=mesh, in_specs=in_specs, out_specs=out_specs, check_vma=False)
```

```python
import functools
import math

import jax
import jax.numpy as jnp
from jax import lax
from jax.experimental import pallas as pl
from jax.experimental.pallas import tpu as pltpu
from jax.sharding import PartitionSpec as P

PAGES_DEV = 8


def send_kernel(page_total, capacity, query_rows, block_at, query_counts_ref, owner_ref, page_ref, rows_ref, weight_ref,
                bias_ref, queries_ref, message_ref):
    owners = message_ref.shape[0]
    rows = rows_ref.shape[0]
    proj = jnp.dot(rows_ref[...], weight_ref[...], preferred_element_type=jnp.float32) + bias_ref[...]
    scale = lax.rsqrt(jnp.sum(proj * proj, axis=1, keepdims=True) + 1e-06)
    local = (proj * scale).astype(jnp.bfloat16)
    combo = owner_ref[...].reshape(1, rows) * page_total + page_ref[...].reshape(1, rows)
    combos = -(-owners * page_total // 128) * 128
    combo_id = lax.broadcasted_iota(jnp.int32, (combos, rows), 0)
    onehot = (combo == combo_id).astype(jnp.bfloat16)
    earlier = (
        lax.broadcasted_iota(jnp.int32, (rows, rows), 0) < lax.broadcasted_iota(jnp.int32, (rows, rows), 1)
    ).astype(jnp.bfloat16)
    seen = jnp.dot(onehot, earlier, preferred_element_type=jnp.float32)
    count = jnp.sum(onehot.astype(jnp.float32), axis=1, keepdims=True)
    row_id = lax.broadcasted_iota(jnp.int32, (combos, combos), 0)
    col_id = lax.broadcasted_iota(jnp.int32, (combos, combos), 1)
    same_owner_lower = (row_id // page_total == col_id // page_total) & (col_id % page_total < row_id % page_total)
    offset = jnp.dot(same_owner_lower.astype(jnp.bfloat16), count.astype(jnp.bfloat16),
                     preferred_element_type=jnp.float32)
    base = (lax.broadcasted_iota(jnp.int32, (combos, 1), 0) // page_total * capacity).astype(jnp.float32) + offset
    slot = jnp.sum(onehot.astype(jnp.float32) * (base + seen), axis=0, keepdims=True).astype(jnp.int32)
    count_rows = [
        lax.dot_general(
            jnp.ones((1, rows), jnp.bfloat16), onehot[group * 128 : (group + 1) * 128],
            (((1,), (1,)), ((), ())), preferred_element_type=jnp.float32,
        )
        for group in range(combos // 128)
    ]
    lane = lax.broadcasted_iota(jnp.int32, (1, 128), 1)
    query_count_row = jnp.zeros((1, 128), jnp.float32)
    for query in range(query_counts_ref.shape[0]):
        query_count_row = jnp.where(lane == query, query_counts_ref[query].astype(jnp.float32), query_count_row)
    block_rows = message_ref.shape[1] - block_at
    block = jnp.concatenate(
        count_rows
        + [query_count_row, jnp.zeros((block_rows - len(count_rows) - 1, 128), jnp.float32)],
        axis=0,
    ).astype(jnp.bfloat16)
    own_half = queries_ref[pl.ds(pl.multiple_of(lax.axis_index("inner") * query_rows, query_rows), query_rows), :]
    slot_id = lax.broadcasted_iota(jnp.int32, (capacity, rows), 0)
    for owner in range(owners):
        placed = (slot == slot_id + owner * capacity).astype(jnp.bfloat16)
        message_ref[owner, 0:query_rows, :] = own_half
        message_ref[owner, query_rows : query_rows + capacity, :] = jnp.dot(
            placed, local, preferred_element_type=jnp.float32
        ).astype(jnp.bfloat16)
        message_ref[owner, block_at:, :] = block


def send_message(patch_rows, owner_ids, page_ids, proj_weight, proj_bias, query_tokens, query_counts, owners, capacity,
                 halves):
    rows, features = patch_rows.shape
    per_block, token_slots, width = query_tokens.shape
    query_rows = per_block // halves * token_slots
    block_at = -(-(query_rows + capacity) // 16) * 16
    vmem = pl.BlockSpec(memory_space=pltpu.VMEM)
    return pl.pallas_call(
        functools.partial(send_kernel, PAGES_DEV, capacity, query_rows, block_at),
        out_shape=jax.ShapeDtypeStruct((owners, block_at + 16, width), jnp.bfloat16),
        in_specs=[pl.BlockSpec(memory_space=pltpu.SMEM)] + [vmem] * 6,
        out_specs=vmem,
        cost_estimate=pl.CostEstimate(
            flops=2 * rows * width * (features + owners * capacity),
            bytes_accessed=2 * (rows * features + features * width + owners * (block_at + 16) * width),
            transcendentals=rows,
        ),
    )(
        query_counts, owner_ids.reshape(1, rows), page_ids, patch_rows, proj_weight, proj_bias.reshape(1, width),
        query_tokens.reshape(per_block * token_slots, width),
    )


def score_kernel(page_total, token_slots, query_rows, token_block, block_at, received_ref, tokens_ref, out_ref,
                 ordered_ref, sims_ref, rows_ref, counts_vmem, counts_smem, copy_sem):
    owners = received_ref.shape[0]
    ordered_rows, width = ordered_ref.shape
    capacity = (ordered_rows - 16 * page_total - 16) // owners
    total_queries = out_ref.shape[1]
    per_block = total_queries // owners
    count_rows = counts_vmem.shape[1] - 1
    counts_vmem[...] = received_ref[:, block_at : block_at + count_rows + 1, :].astype(jnp.float32).astype(jnp.int32)
    copy = pltpu.make_async_copy(counts_vmem, counts_smem, copy_sem)
    copy.start()
    copy.wait()
    mine = lax.axis_index("blk") * page_total

    class Table:
        def __getitem__(self, index):
            chunk, rest = divmod(index, page_total)
            if chunk < owners:
                lane = mine + rest
                return counts_smem[chunk, lane // 128, lane % 128]
            query = index - owners * page_total
            return counts_smem[query // per_block, count_rows, query % per_block]

    table_ref = Table()
    totals = [sum(table_ref[chunk * page_total + page] for chunk in range(owners)) for page in range(page_total)]
    firsts = []
    at = 0
    for page in range(page_total):
        firsts.append(at)
        at = at + (totals[page] + 15) // 16 * 16
    slot = lax.broadcasted_iota(jnp.int32, (1, capacity), 1)
    before = [0] * page_total
    positions = []
    for chunk in range(owners):
        position = jnp.full((1, capacity), -1, jnp.int32)
        low = 0
        for page in range(page_total):
            high = low + table_ref[chunk * page_total + page]
            inside = (slot >= low) & (slot < high)
            position = jnp.where(inside, slot + (firsts[page] + before[page] - low), position)
            before[page] = before[page] + (high - low)
            low = high
        positions.append(position)
        rows_ref[chunk * capacity : (chunk + 1) * capacity, :] = received_ref[chunk, query_rows : query_rows + capacity, :]
    position = jnp.concatenate(positions, axis=1)
    place = (position == lax.broadcasted_iota(jnp.int32, (ordered_rows, owners * capacity), 0)).astype(jnp.bfloat16)
    ordered_ref[...] = jnp.dot(place, rows_ref[...], preferred_element_type=jnp.float32).astype(jnp.bfloat16)
    sources = token_block // tokens_ref.shape[1]
    sub = lax.broadcasted_iota(jnp.int32, (8, token_block), 0)
    query_lane = lax.broadcasted_iota(jnp.int32, (1, total_queries), 1)
    live_count = jnp.zeros((1, total_queries), jnp.int32)
    for query in range(total_queries):
        live_count = jnp.where(query_lane == query, table_ref[owners * page_total + query], live_count)
    token_id = lax.broadcasted_iota(jnp.int32, (token_block, total_queries), 0)
    query_id = lax.broadcasted_iota(jnp.int32, (token_block, total_queries), 1)

    def block_scores(block, total):
        tokens = tokens_ref[pl.ds(block * sources, sources)].reshape(token_block, width)
        sims_ref[...] = lax.dot_general(
            ordered_ref[...], tokens, (((1,), (1,)), ((), ())), preferred_element_type=jnp.float32
        )
        best_rows = []
        for page in range(page_total):
            first = firsts[page]
            whole = totals[page] // 16
            rest = totals[page] % 16

            def step(i, carry):
                start = pl.multiple_of(first + i * 16, 16)
                return (
                    jnp.maximum(carry[0], sims_ref[pl.ds(start, 8), :]),
                    jnp.maximum(carry[1], sims_ref[pl.ds(start + 8, 8), :]),
                )

            floor = jnp.full((8, token_block), -2.0, jnp.float32)
            low, high = lax.fori_loop(0, whole, step, (floor, floor))
            start = pl.multiple_of(first + whole * 16, 16)
            low = jnp.maximum(low, jnp.where(sub < rest, sims_ref[pl.ds(start, 8), :], jnp.float32(-2.0)))
            high = jnp.maximum(high, jnp.where(sub + 8 < rest, sims_ref[pl.ds(start + 8, 8), :], jnp.float32(-2.0)))
            best_rows.append(jnp.max(jnp.maximum(low, high), axis=0, keepdims=True))
        best = jnp.concatenate(best_rows, axis=0)
        token = token_id + block * token_block
        live = ((token // token_slots) == query_id) & ((token % token_slots) < live_count)
        return total + jnp.dot(
            best, live.astype(jnp.float32), precision=lax.Precision.HIGHEST, preferred_element_type=jnp.float32
        )

    blocks = tokens_ref.shape[0] * tokens_ref.shape[1] // token_block
    out_ref[...] = lax.fori_loop(
        0, blocks, block_scores, jnp.zeros((page_total, total_queries), jnp.float32)
    )


def page_scores(received, tokens, total_queries, page_total, token_slots, query_rows, capacity, block_at, count_rows):
    owners = received.shape[0]
    width = received.shape[2]
    ordered_rows = owners * capacity + 16 * page_total + 16
    token_total = tokens.shape[0] * tokens.shape[1]
    token_block = min(token_total, 1024)
    vmem = pl.BlockSpec(memory_space=pltpu.VMEM)
    return pl.pallas_call(
        functools.partial(score_kernel, page_total, token_slots, query_rows, token_block, block_at),
        out_shape=jax.ShapeDtypeStruct((page_total, total_queries), jnp.float32),
        in_specs=[vmem, vmem],
        out_specs=vmem,
        scratch_shapes=[
            pltpu.VMEM((ordered_rows, width), jnp.bfloat16),
            pltpu.VMEM((ordered_rows, token_block), jnp.float32),
            pltpu.VMEM((owners * capacity, width), jnp.bfloat16),
            pltpu.VMEM((owners, count_rows + 1, width), jnp.int32),
            pltpu.SMEM((owners, count_rows + 1, width), jnp.int32),
            pltpu.SemaphoreType.DMA,
        ],
        cost_estimate=pl.CostEstimate(
            flops=2 * ordered_rows * width * (owners * capacity + token_total),
            bytes_accessed=2 * received.size + 2 * tokens.size + 4 * page_total * total_queries,
            transcendentals=0,
        ),
    )(received, tokens)


def shards(patch_rows, owner_ids, page_ids, proj_weight, proj_bias, query_tokens, query_counts):
    owners = lax.axis_size("blk")
    halves = lax.axis_size("inner")
    rows = patch_rows.shape[0]
    capacity = 2 * rows // owners
    per_block = query_tokens.shape[0]
    token_slots = query_tokens.shape[1]
    width = query_tokens.shape[2]
    total_queries = per_block * owners
    half_queries = per_block // halves
    query_rows = half_queries * token_slots
    message = send_message(
        patch_rows, owner_ids, page_ids, proj_weight, proj_bias, query_tokens, query_counts, owners, capacity, halves
    )
    received = lax.all_to_all(message, "blk", split_axis=0, concat_axis=0, tiled=True)
    halves_in = lax.all_gather(received[:, :query_rows], "inner", axis=1, tiled=True)
    block_at = -(-(query_rows + capacity) // 16) * 16
    combos = -(-owners * PAGES_DEV // 128) * 128
    count_rows = combos // 128
    return page_scores(
        received, halves_in, total_queries, PAGES_DEV, token_slots, query_rows, capacity, block_at, count_rows
    )


def solution(mesh):
    in_specs = (
        P(("groups", "blk", "inner"), None),
        P(("groups", "blk", "inner"), None),
        P(("groups", "blk", "inner")),
        P(),
        P(),
        P(("groups", "blk"), None, None),
        P(("groups", "blk")),
    )
    out_specs = P(("groups", "blk", "inner"), None)
    return jax.shard_map(shards, mesh=mesh, in_specs=in_specs, out_specs=out_specs, check_vma=False)
```

```python
import functools
import math

import jax
import jax.numpy as jnp
from jax import lax
from jax.experimental import pallas as pl
from jax.experimental.pallas import tpu as pltpu
from jax.sharding import PartitionSpec as P

PAGES_DEV = 8


def send_kernel(page_total, capacity, query_rows, block_at, query_counts_ref, owner_ref, page_ref, rows_ref, weight_ref,
                bias_ref, queries_ref, message_ref):
    owners = message_ref.shape[0]
    rows = rows_ref.shape[0]
    proj = jnp.dot(rows_ref[...], weight_ref[...], preferred_element_type=jnp.float32) + bias_ref[...]
    scale = lax.rsqrt(jnp.sum(proj * proj, axis=1, keepdims=True) + 1e-06)
    local = (proj * scale).astype(jnp.bfloat16)
    combo = owner_ref[...].reshape(1, rows) * page_total + page_ref[...].reshape(1, rows)
    combos = -(-owners * page_total // 128) * 128
    combo_id = lax.broadcasted_iota(jnp.int32, (combos, rows), 0)
    onehot = (combo == combo_id).astype(jnp.bfloat16)
    earlier = (
        lax.broadcasted_iota(jnp.int32, (rows, rows), 0) < lax.broadcasted_iota(jnp.int32, (rows, rows), 1)
    ).astype(jnp.bfloat16)
    seen = jnp.dot(onehot, earlier, preferred_element_type=jnp.float32)
    count = jnp.sum(onehot.astype(jnp.float32), axis=1, keepdims=True)
    row_id = lax.broadcasted_iota(jnp.int32, (combos, combos), 0)
    col_id = lax.broadcasted_iota(jnp.int32, (combos, combos), 1)
    same_owner_lower = (row_id // page_total == col_id // page_total) & (col_id % page_total < row_id % page_total)
    offset = jnp.dot(same_owner_lower.astype(jnp.bfloat16), count.astype(jnp.bfloat16),
                     preferred_element_type=jnp.float32)
    base = (lax.broadcasted_iota(jnp.int32, (combos, 1), 0) // page_total * capacity).astype(jnp.float32) + offset
    slot = jnp.sum(onehot.astype(jnp.float32) * (base + seen), axis=0, keepdims=True).astype(jnp.int32)
    count_rows = [
        lax.dot_general(
            jnp.ones((1, rows), jnp.bfloat16), onehot[group * 128 : (group + 1) * 128],
            (((1,), (1,)), ((), ())), preferred_element_type=jnp.float32,
        )
        for group in range(combos // 128)
    ]
    lane = lax.broadcasted_iota(jnp.int32, (1, 128), 1)
    query_count_row = jnp.zeros((1, 128), jnp.float32)
    for query in range(query_counts_ref.shape[0]):
        query_count_row = jnp.where(lane == query, query_counts_ref[query].astype(jnp.float32), query_count_row)
    block_rows = message_ref.shape[1] - block_at
    block = jnp.concatenate(
        count_rows
        + [query_count_row, jnp.zeros((block_rows - len(count_rows) - 1, 128), jnp.float32)],
        axis=0,
    ).astype(jnp.bfloat16)
    own_half = queries_ref[pl.ds(pl.multiple_of(lax.axis_index("inner") * query_rows, query_rows), query_rows), :]
    slot_id = lax.broadcasted_iota(jnp.int32, (capacity, rows), 0)
    for owner in range(owners):
        placed = (slot == slot_id + owner * capacity).astype(jnp.bfloat16)
        message_ref[owner, 0:query_rows, :] = own_half
        message_ref[owner, query_rows : query_rows + capacity, :] = jnp.dot(
            placed, local, preferred_element_type=jnp.float32
        ).astype(jnp.bfloat16)
        message_ref[owner, block_at:, :] = block


def send_message(patch_rows, owner_ids, page_ids, proj_weight, proj_bias, query_tokens, query_counts, owners, capacity,
                 halves):
    rows, features = patch_rows.shape
    per_block, token_slots, width = query_tokens.shape
    query_rows = per_block // halves * token_slots
    block_at = -(-(query_rows + capacity) // 16) * 16
    vmem = pl.BlockSpec(memory_space=pltpu.VMEM)
    return pl.pallas_call(
        functools.partial(send_kernel, PAGES_DEV, capacity, query_rows, block_at),
        out_shape=jax.ShapeDtypeStruct((owners, block_at + 16, width), jnp.bfloat16),
        in_specs=[pl.BlockSpec(memory_space=pltpu.SMEM)] + [vmem] * 6,
        out_specs=vmem,
        cost_estimate=pl.CostEstimate(
            flops=2 * rows * width * (features + owners * capacity),
            bytes_accessed=2 * (rows * features + features * width + owners * (block_at + 16) * width),
            transcendentals=rows,
        ),
    )(
        query_counts, owner_ids.reshape(1, rows), page_ids, patch_rows, proj_weight, proj_bias.reshape(1, width),
        query_tokens.reshape(per_block * token_slots, width),
    )


def page_runs(table_ref, owners, page_total):
    totals = [sum(table_ref[chunk * page_total + page] for chunk in range(owners)) for page in range(page_total)]
    firsts = []
    at = 0
    for page in range(page_total):
        firsts.append(at)
        at = at + (totals[page] + 15) // 16 * 16
    return totals, firsts


def half_scores(table_ref, ordered_ref, sims_ref, tokens_ref, half, owners, page_total, token_slots, per_block,
                total_queries):
    ordered_rows, width = ordered_ref.shape
    token_block = sims_ref.shape[1]
    half_rows = tokens_ref.shape[1]
    half_queries = half_rows // token_slots
    totals, firsts = page_runs(table_ref, owners, page_total)
    query_lane = lax.broadcasted_iota(jnp.int32, (1, total_queries), 1)
    live_count = jnp.zeros((1, total_queries), jnp.int32)
    for query in range(total_queries):
        live_count = jnp.where(query_lane == query, table_ref[owners * page_total + query], live_count)
    sub = lax.broadcasted_iota(jnp.int32, (8, token_block), 0)
    token_id = lax.broadcasted_iota(jnp.int32, (token_block, total_queries), 0)
    query_id = lax.broadcasted_iota(jnp.int32, (token_block, total_queries), 1)
    sources = token_block // half_rows

    def block_scores(block, total):
        tokens = tokens_ref[pl.ds(block * sources, sources)].reshape(token_block, width)
        sims_ref[...] = lax.dot_general(
            ordered_ref[...], tokens, (((1,), (1,)), ((), ())), preferred_element_type=jnp.float32
        )
        best_rows = []
        for page in range(page_total):
            first = firsts[page]
            whole = totals[page] // 16
            rest = totals[page] % 16

            def step(i, carry):
                start = pl.multiple_of(first + i * 16, 16)
                return (
                    jnp.maximum(carry[0], sims_ref[pl.ds(start, 8), :]),
                    jnp.maximum(carry[1], sims_ref[pl.ds(start + 8, 8), :]),
                )

            floor = jnp.full((8, token_block), -2.0, jnp.float32)
            low, high = lax.fori_loop(0, whole, step, (floor, floor))
            start = pl.multiple_of(first + whole * 16, 16)
            low = jnp.maximum(low, jnp.where(sub < rest, sims_ref[pl.ds(start, 8), :], jnp.float32(-2.0)))
            high = jnp.maximum(high, jnp.where(sub + 8 < rest, sims_ref[pl.ds(start + 8, 8), :], jnp.float32(-2.0)))
            best_rows.append(jnp.max(jnp.maximum(low, high), axis=0, keepdims=True))
        best = jnp.concatenate(best_rows, axis=0)
        token = token_id + block * token_block
        query = token // half_rows * per_block + half * half_queries + token % half_rows // token_slots
        live = (query == query_id) & ((token % token_slots) < live_count)
        return total + jnp.dot(
            best, live.astype(jnp.float32), precision=lax.Precision.HIGHEST, preferred_element_type=jnp.float32
        )

    blocks = tokens_ref.shape[0] * half_rows // token_block
    return lax.fori_loop(0, blocks, block_scores, jnp.zeros((page_total, total_queries), jnp.float32))


def score_kernel(page_total, token_slots, query_rows, table_ref, received_ref, partner_ref, out_ref, ordered_ref,
                 sims_ref, rows_ref):
    owners = received_ref.shape[0]
    ordered_rows, width = ordered_ref.shape
    capacity = (ordered_rows - 16 * page_total - 16) // owners
    total_queries = out_ref.shape[1]
    totals = [sum(table_ref[chunk * page_total + page] for chunk in range(owners)) for page in range(page_total)]
    firsts = []
    at = 0
    for page in range(page_total):
        firsts.append(at)
        at = at + (totals[page] + 15) // 16 * 16
    slot = lax.broadcasted_iota(jnp.int32, (1, capacity), 1)
    before = [0] * page_total
    positions = []
    for chunk in range(owners):
        position = jnp.full((1, capacity), -1, jnp.int32)
        low = 0
        for page in range(page_total):
            high = low + table_ref[chunk * page_total + page]
            inside = (slot >= low) & (slot < high)
            position = jnp.where(inside, slot + (firsts[page] + before[page] - low), position)
            before[page] = before[page] + (high - low)
            low = high
        positions.append(position)
        rows_ref[chunk * capacity : (chunk + 1) * capacity, :] = received_ref[chunk, query_rows : query_rows + capacity, :]
    position = jnp.concatenate(positions, axis=1)
    place = (position == lax.broadcasted_iota(jnp.int32, (ordered_rows, owners * capacity), 0)).astype(jnp.bfloat16)
    ordered_ref[...] = jnp.dot(place, rows_ref[...], preferred_element_type=jnp.float32).astype(jnp.bfloat16)
    inner = lax.axis_index("inner")
    out_ref[...] = half_scores(
        table_ref, ordered_ref, sims_ref, received_ref.at[:, 0:query_rows, :], inner, owners, page_total, token_slots,
        total_queries // owners, total_queries,
    ) + half_scores(
        table_ref, ordered_ref, sims_ref, partner_ref, 1 - inner, owners, page_total, token_slots,
        total_queries // owners, total_queries,
    )


def page_scores(received, tokens, table, total_queries, page_total, token_slots, query_rows, capacity):
    owners = received.shape[0]
    width = received.shape[2]
    ordered_rows = owners * capacity + 16 * page_total + 16
    token_block = min(owners * query_rows, 1024)
    vmem = pl.BlockSpec(memory_space=pltpu.VMEM)
    return pl.pallas_call(
        functools.partial(score_kernel, page_total, token_slots, query_rows),
        out_shape=jax.ShapeDtypeStruct((page_total, total_queries), jnp.float32),
        in_specs=[pl.BlockSpec(memory_space=pltpu.SMEM), vmem, vmem],
        out_specs=vmem,
        scratch_shapes=[
            pltpu.VMEM((ordered_rows, width), jnp.bfloat16),
            pltpu.VMEM((ordered_rows, token_block), jnp.float32),
            pltpu.VMEM((owners * capacity, width), jnp.bfloat16),
        ],
        cost_estimate=pl.CostEstimate(
            flops=2 * ordered_rows * width * owners * (capacity + 2 * query_rows),
            bytes_accessed=2 * received.size + 2 * tokens.size + 4 * page_total * total_queries,
            transcendentals=0,
        ),
    )(table, received, tokens)


def shards(patch_rows, owner_ids, page_ids, proj_weight, proj_bias, query_tokens, query_counts):
    owners = lax.axis_size("blk")
    halves = lax.axis_size("inner")
    rows = patch_rows.shape[0]
    capacity = 2 * rows // owners
    per_block = query_tokens.shape[0]
    token_slots = query_tokens.shape[1]
    width = query_tokens.shape[2]
    total_queries = per_block * owners
    half_queries = per_block // halves
    query_rows = half_queries * token_slots
    message = send_message(
        patch_rows, owner_ids, page_ids, proj_weight, proj_bias, query_tokens, query_counts, owners, capacity, halves
    )
    received = lax.all_to_all(message, "blk", split_axis=0, concat_axis=0, tiled=True)
    partner = lax.ppermute(received[:, :query_rows], "inner", [(0, 1), (1, 0)])
    block_at = -(-(query_rows + capacity) // 16) * 16
    combos = -(-owners * PAGES_DEV // 128) * 128
    count_rows = combos // 128
    page_counts = received[:, block_at : block_at + count_rows].reshape(owners, combos)
    page_counts = lax.dynamic_slice_in_dim(page_counts, lax.axis_index("blk") * PAGES_DEV, PAGES_DEV, axis=1)
    counts = received[:, block_at + count_rows, :per_block]
    table = jnp.concatenate([page_counts.reshape(owners * PAGES_DEV), counts.reshape(total_queries)]).astype(jnp.int32)
    return page_scores(received, partner, table, total_queries, PAGES_DEV, token_slots, query_rows, capacity)


def solution(mesh):
    in_specs = (
        P(("groups", "blk", "inner"), None),
        P(("groups", "blk", "inner"), None),
        P(("groups", "blk", "inner")),
        P(),
        P(),
        P(("groups", "blk"), None, None),
        P(("groups", "blk")),
    )
    out_specs = P(("groups", "blk", "inner"), None)
    return jax.shard_map(shards, mesh=mesh, in_specs=in_specs, out_specs=out_specs, check_vma=False)
```

```python
import functools
import math

import jax
import jax.numpy as jnp
from jax import lax
from jax.experimental import pallas as pl
from jax.experimental.pallas import tpu as pltpu
from jax.sharding import PartitionSpec as P

PAGES_DEV = 8


def send_kernel(page_total, capacity, query_rows, block_at, query_counts_ref, owner_ref, page_ref, rows_ref, weight_ref,
                bias_ref, queries_ref, message_ref):
    owners = message_ref.shape[0]
    rows = rows_ref.shape[0]
    proj = jnp.dot(rows_ref[...], weight_ref[...], preferred_element_type=jnp.float32) + bias_ref[...]
    scale = lax.rsqrt(jnp.sum(proj * proj, axis=1, keepdims=True) + 1e-06)
    local = (proj * scale).astype(jnp.bfloat16)
    combo = owner_ref[...].reshape(1, rows) * page_total + page_ref[...].reshape(1, rows)
    combos = -(-owners * page_total // 128) * 128
    combo_id = lax.broadcasted_iota(jnp.int32, (combos, rows), 0)
    onehot = (combo == combo_id).astype(jnp.bfloat16)
    earlier = (
        lax.broadcasted_iota(jnp.int32, (rows, rows), 0) < lax.broadcasted_iota(jnp.int32, (rows, rows), 1)
    ).astype(jnp.bfloat16)
    seen = jnp.dot(onehot, earlier, preferred_element_type=jnp.float32)
    count = jnp.sum(onehot.astype(jnp.float32), axis=1, keepdims=True)
    row_id = lax.broadcasted_iota(jnp.int32, (combos, combos), 0)
    col_id = lax.broadcasted_iota(jnp.int32, (combos, combos), 1)
    same_owner_lower = (row_id // page_total == col_id // page_total) & (col_id % page_total < row_id % page_total)
    offset = jnp.dot(same_owner_lower.astype(jnp.bfloat16), count.astype(jnp.bfloat16),
                     preferred_element_type=jnp.float32)
    base = (lax.broadcasted_iota(jnp.int32, (combos, 1), 0) // page_total * capacity).astype(jnp.float32) + offset
    slot = jnp.sum(onehot.astype(jnp.float32) * (base + seen), axis=0, keepdims=True).astype(jnp.int32)
    count_rows = [
        lax.dot_general(
            jnp.ones((1, rows), jnp.bfloat16), onehot[group * 128 : (group + 1) * 128],
            (((1,), (1,)), ((), ())), preferred_element_type=jnp.float32,
        )
        for group in range(combos // 128)
    ]
    lane = lax.broadcasted_iota(jnp.int32, (1, 128), 1)
    query_count_row = jnp.zeros((1, 128), jnp.float32)
    for query in range(query_counts_ref.shape[0]):
        query_count_row = jnp.where(lane == query, query_counts_ref[query].astype(jnp.float32), query_count_row)
    block_rows = message_ref.shape[1] - block_at
    block = jnp.concatenate(
        count_rows
        + [query_count_row, jnp.zeros((block_rows - len(count_rows) - 1, 128), jnp.float32)],
        axis=0,
    ).astype(jnp.bfloat16)
    own_half = queries_ref[pl.ds(pl.multiple_of(lax.axis_index("inner") * query_rows, query_rows), query_rows), :]
    slot_id = lax.broadcasted_iota(jnp.int32, (capacity, rows), 0)
    for owner in range(owners):
        placed = (slot == slot_id + owner * capacity).astype(jnp.bfloat16)
        message_ref[owner, 0:query_rows, :] = own_half
        message_ref[owner, query_rows : query_rows + capacity, :] = jnp.dot(
            placed, local, preferred_element_type=jnp.float32
        ).astype(jnp.bfloat16)
        message_ref[owner, block_at:, :] = block


def send_message(patch_rows, owner_ids, page_ids, proj_weight, proj_bias, query_tokens, query_counts, owners, capacity,
                 halves):
    rows, features = patch_rows.shape
    per_block, token_slots, width = query_tokens.shape
    query_rows = per_block // halves * token_slots
    block_at = -(-(query_rows + capacity) // 16) * 16
    vmem = pl.BlockSpec(memory_space=pltpu.VMEM)
    return pl.pallas_call(
        functools.partial(send_kernel, PAGES_DEV, capacity, query_rows, block_at),
        out_shape=jax.ShapeDtypeStruct((owners, block_at + 16, width), jnp.bfloat16),
        in_specs=[pl.BlockSpec(memory_space=pltpu.SMEM)] + [vmem] * 6,
        out_specs=vmem,
        cost_estimate=pl.CostEstimate(
            flops=2 * rows * width * (features + owners * capacity),
            bytes_accessed=2 * (rows * features + features * width + owners * (block_at + 16) * width),
            transcendentals=rows,
        ),
    )(
        query_counts, owner_ids.reshape(1, rows), page_ids, patch_rows, proj_weight, proj_bias.reshape(1, width),
        query_tokens.reshape(per_block * token_slots, width),
    )


def score_kernel(page_total, token_slots, query_rows, token_block, table_ref, received_ref, partner_ref, out_ref,
                 ordered_ref, sims_ref, rows_ref, tokens_ref):
    owners = received_ref.shape[0]
    ordered_rows, width = ordered_ref.shape
    capacity = (ordered_rows - 16 * page_total - 16) // owners
    total_queries = out_ref.shape[1]
    totals = [sum(table_ref[chunk * page_total + page] for chunk in range(owners)) for page in range(page_total)]
    firsts = []
    at = 0
    for page in range(page_total):
        firsts.append(at)
        at = at + (totals[page] + 15) // 16 * 16
    slot = lax.broadcasted_iota(jnp.int32, (1, capacity), 1)
    before = [0] * page_total
    positions = []
    for chunk in range(owners):
        position = jnp.full((1, capacity), -1, jnp.int32)
        low = 0
        for page in range(page_total):
            high = low + table_ref[chunk * page_total + page]
            inside = (slot >= low) & (slot < high)
            position = jnp.where(inside, slot + (firsts[page] + before[page] - low), position)
            before[page] = before[page] + (high - low)
            low = high
        positions.append(position)
        rows_ref[chunk * capacity : (chunk + 1) * capacity, :] = received_ref[chunk, query_rows : query_rows + capacity, :]
    position = jnp.concatenate(positions, axis=1)
    place = (position == lax.broadcasted_iota(jnp.int32, (ordered_rows, owners * capacity), 0)).astype(jnp.bfloat16)
    ordered_ref[...] = jnp.dot(place, rows_ref[...], preferred_element_type=jnp.float32).astype(jnp.bfloat16)
    inner = lax.axis_index("inner")
    tokens_ref[:, pl.ds(pl.multiple_of(inner * query_rows, query_rows), query_rows), :] = (
        received_ref[:, 0:query_rows, :]
    )
    tokens_ref[:, pl.ds(pl.multiple_of((1 - inner) * query_rows, query_rows), query_rows), :] = partner_ref[...]
    sources = token_block // tokens_ref.shape[1]
    sub = lax.broadcasted_iota(jnp.int32, (8, token_block), 0)
    query_lane = lax.broadcasted_iota(jnp.int32, (1, total_queries), 1)
    live_count = jnp.zeros((1, total_queries), jnp.int32)
    for query in range(total_queries):
        live_count = jnp.where(query_lane == query, table_ref[owners * page_total + query], live_count)
    token_id = lax.broadcasted_iota(jnp.int32, (token_block, total_queries), 0)
    query_id = lax.broadcasted_iota(jnp.int32, (token_block, total_queries), 1)

    def block_scores(block, total):
        tokens = tokens_ref[pl.ds(block * sources, sources)].reshape(token_block, width)
        sims_ref[...] = lax.dot_general(
            ordered_ref[...], tokens, (((1,), (1,)), ((), ())), preferred_element_type=jnp.float32
        )
        best_rows = []
        for page in range(page_total):
            first = firsts[page]
            whole = totals[page] // 16
            rest = totals[page] % 16

            def step(i, carry):
                start = pl.multiple_of(first + i * 16, 16)
                return (
                    jnp.maximum(carry[0], sims_ref[pl.ds(start, 8), :]),
                    jnp.maximum(carry[1], sims_ref[pl.ds(start + 8, 8), :]),
                )

            floor = jnp.full((8, token_block), -2.0, jnp.float32)
            low, high = lax.fori_loop(0, whole, step, (floor, floor))
            start = pl.multiple_of(first + whole * 16, 16)
            low = jnp.maximum(low, jnp.where(sub < rest, sims_ref[pl.ds(start, 8), :], jnp.float32(-2.0)))
            high = jnp.maximum(high, jnp.where(sub + 8 < rest, sims_ref[pl.ds(start + 8, 8), :], jnp.float32(-2.0)))
            best_rows.append(jnp.max(jnp.maximum(low, high), axis=0, keepdims=True))
        best = jnp.concatenate(best_rows, axis=0)
        token = token_id + block * token_block
        live = ((token // token_slots) == query_id) & ((token % token_slots) < live_count)
        return total + jnp.dot(
            best, live.astype(jnp.float32), precision=lax.Precision.HIGHEST, preferred_element_type=jnp.float32
        )

    blocks = tokens_ref.shape[0] * tokens_ref.shape[1] // token_block
    out_ref[...] = lax.fori_loop(
        0, blocks, block_scores, jnp.zeros((page_total, total_queries), jnp.float32)
    )


def page_scores(received, tokens, table, total_queries, page_total, token_slots, query_rows, capacity):
    owners = received.shape[0]
    width = received.shape[2]
    ordered_rows = owners * capacity + 16 * page_total + 16
    token_total = 2 * tokens.shape[0] * tokens.shape[1]
    token_block = min(token_total, 1024)
    vmem = pl.BlockSpec(memory_space=pltpu.VMEM)
    return pl.pallas_call(
        functools.partial(score_kernel, page_total, token_slots, query_rows, token_block),
        out_shape=jax.ShapeDtypeStruct((page_total, total_queries), jnp.float32),
        in_specs=[pl.BlockSpec(memory_space=pltpu.SMEM), vmem, vmem],
        out_specs=vmem,
        scratch_shapes=[
            pltpu.VMEM((ordered_rows, width), jnp.bfloat16),
            pltpu.VMEM((ordered_rows, token_block), jnp.float32),
            pltpu.VMEM((owners * capacity, width), jnp.bfloat16),
            pltpu.VMEM((owners, 2 * query_rows, width), jnp.bfloat16),
        ],
        cost_estimate=pl.CostEstimate(
            flops=2 * ordered_rows * width * (owners * capacity + token_total),
            bytes_accessed=2 * received.size + 2 * tokens.size + 4 * page_total * total_queries,
            transcendentals=0,
        ),
    )(table, received, tokens)


def shards(patch_rows, owner_ids, page_ids, proj_weight, proj_bias, query_tokens, query_counts):
    owners = lax.axis_size("blk")
    halves = lax.axis_size("inner")
    rows = patch_rows.shape[0]
    capacity = 2 * rows // owners
    per_block = query_tokens.shape[0]
    token_slots = query_tokens.shape[1]
    width = query_tokens.shape[2]
    total_queries = per_block * owners
    half_queries = per_block // halves
    query_rows = half_queries * token_slots
    message = send_message(
        patch_rows, owner_ids, page_ids, proj_weight, proj_bias, query_tokens, query_counts, owners, capacity, halves
    )
    received = lax.all_to_all(message, "blk", split_axis=0, concat_axis=0, tiled=True)
    partner = lax.ppermute(received[:, :query_rows], "inner", [(0, 1), (1, 0)])
    block_at = -(-(query_rows + capacity) // 16) * 16
    combos = -(-owners * PAGES_DEV // 128) * 128
    count_rows = combos // 128
    page_counts = received[:, block_at : block_at + count_rows].reshape(owners, combos)
    page_counts = lax.dynamic_slice_in_dim(page_counts, lax.axis_index("blk") * PAGES_DEV, PAGES_DEV, axis=1)
    counts = received[:, block_at + count_rows, :per_block]
    table = jnp.concatenate([page_counts.reshape(owners * PAGES_DEV), counts.reshape(total_queries)]).astype(jnp.int32)
    return page_scores(received, partner, table, total_queries, PAGES_DEV, token_slots, query_rows, capacity)


def solution(mesh):
    in_specs = (
        P(("groups", "blk", "inner"), None),
        P(("groups", "blk", "inner"), None),
        P(("groups", "blk", "inner")),
        P(),
        P(),
        P(("groups", "blk"), None, None),
        P(("groups", "blk")),
    )
    out_specs = P(("groups", "blk", "inner"), None)
    return jax.shard_map(shards, mesh=mesh, in_specs=in_specs, out_specs=out_specs, check_vma=False)
```

```python
import functools
import math

import jax
import jax.numpy as jnp
from jax import lax
from jax.experimental import pallas as pl
from jax.experimental.pallas import tpu as pltpu
from jax.sharding import PartitionSpec as P

PAGES_DEV = 8


def send_kernel(page_total, capacity, query_rows, block_at, query_counts_ref, owner_ref, page_ref, rows_ref, weight_ref,
                bias_ref, queries_ref, message_ref):
    owners = message_ref.shape[0]
    rows = rows_ref.shape[0]
    proj = jnp.dot(rows_ref[...], weight_ref[...], preferred_element_type=jnp.float32) + bias_ref[...]
    scale = lax.rsqrt(jnp.sum(proj * proj, axis=1, keepdims=True) + 1e-06)
    local = (proj * scale).astype(jnp.bfloat16)
    combo = owner_ref[...].reshape(1, rows) * page_total + page_ref[...].reshape(1, rows)
    combos = -(-owners * page_total // 128) * 128
    combo_id = lax.broadcasted_iota(jnp.int32, (combos, rows), 0)
    onehot = (combo == combo_id).astype(jnp.bfloat16)
    lane = 128 if rows % 128 == 0 else rows
    earlier = (
        lax.broadcasted_iota(jnp.int32, (lane, lane), 0) < lax.broadcasted_iota(jnp.int32, (lane, lane), 1)
    ).astype(jnp.bfloat16)
    parts = []
    count = jnp.zeros((combos, 1), jnp.float32)
    for start in range(0, rows, lane):
        part = onehot[:, start : start + lane]
        parts.append(jnp.dot(part, earlier, preferred_element_type=jnp.float32) + count)
        count = count + jnp.sum(part.astype(jnp.float32), axis=1, keepdims=True)
    seen = jnp.concatenate(parts, axis=1)
    row_id = lax.broadcasted_iota(jnp.int32, (combos, combos), 0)
    col_id = lax.broadcasted_iota(jnp.int32, (combos, combos), 1)
    same_owner_lower = (row_id // page_total == col_id // page_total) & (col_id % page_total < row_id % page_total)
    offset = jnp.dot(same_owner_lower.astype(jnp.bfloat16), count.astype(jnp.bfloat16),
                     preferred_element_type=jnp.float32)
    base = (lax.broadcasted_iota(jnp.int32, (combos, 1), 0) // page_total * capacity).astype(jnp.float32) + offset
    slot = jnp.sum(onehot.astype(jnp.float32) * (base + seen), axis=0, keepdims=True).astype(jnp.int32)
    count_rows = [
        lax.dot_general(
            jnp.ones((1, rows), jnp.bfloat16), onehot[group * 128 : (group + 1) * 128],
            (((1,), (1,)), ((), ())), preferred_element_type=jnp.float32,
        )
        for group in range(combos // 128)
    ]
    lane = lax.broadcasted_iota(jnp.int32, (1, 128), 1)
    query_count_row = jnp.zeros((1, 128), jnp.float32)
    for query in range(query_counts_ref.shape[0]):
        query_count_row = jnp.where(lane == query, query_counts_ref[query].astype(jnp.float32), query_count_row)
    block_rows = message_ref.shape[1] - block_at
    block = jnp.concatenate(
        count_rows
        + [query_count_row, jnp.zeros((block_rows - len(count_rows) - 1, 128), jnp.float32)],
        axis=0,
    ).astype(jnp.bfloat16)
    own_half = queries_ref[pl.ds(pl.multiple_of(lax.axis_index("inner") * query_rows, query_rows), query_rows), :]
    slot_id = lax.broadcasted_iota(jnp.int32, (capacity, rows), 0)
    for owner in range(owners):
        placed = (slot == slot_id + owner * capacity).astype(jnp.bfloat16)
        message_ref[owner, 0:query_rows, :] = own_half
        message_ref[owner, query_rows : query_rows + capacity, :] = jnp.dot(
            placed, local, preferred_element_type=jnp.float32
        ).astype(jnp.bfloat16)
        message_ref[owner, block_at:, :] = block


def send_message(patch_rows, owner_ids, page_ids, proj_weight, proj_bias, query_tokens, query_counts, owners, capacity,
                 halves):
    rows, features = patch_rows.shape
    per_block, token_slots, width = query_tokens.shape
    query_rows = per_block // halves * token_slots
    block_at = -(-(query_rows + capacity) // 16) * 16
    vmem = pl.BlockSpec(memory_space=pltpu.VMEM)
    return pl.pallas_call(
        functools.partial(send_kernel, PAGES_DEV, capacity, query_rows, block_at),
        out_shape=jax.ShapeDtypeStruct((owners, block_at + 16, width), jnp.bfloat16),
        in_specs=[pl.BlockSpec(memory_space=pltpu.SMEM)] + [vmem] * 6,
        out_specs=vmem,
        cost_estimate=pl.CostEstimate(
            flops=2 * rows * width * (features + owners * capacity),
            bytes_accessed=2 * (rows * features + features * width + owners * (block_at + 16) * width),
            transcendentals=rows,
        ),
    )(
        query_counts, owner_ids.reshape(1, rows), page_ids, patch_rows, proj_weight, proj_bias.reshape(1, width),
        query_tokens.reshape(per_block * token_slots, width),
    )


def score_kernel(page_total, token_slots, query_rows, token_block, table_ref, received_ref, partner_ref, out_ref,
                 ordered_ref, sims_ref, rows_ref, tokens_ref):
    owners = received_ref.shape[0]
    ordered_rows, width = ordered_ref.shape
    capacity = (ordered_rows - 16 * page_total - 16) // owners
    total_queries = out_ref.shape[1]
    totals = [sum(table_ref[chunk * page_total + page] for chunk in range(owners)) for page in range(page_total)]
    firsts = []
    at = 0
    for page in range(page_total):
        firsts.append(at)
        at = at + (totals[page] + 15) // 16 * 16
    slot = lax.broadcasted_iota(jnp.int32, (1, capacity), 1)
    before = [0] * page_total
    positions = []
    for chunk in range(owners):
        position = jnp.full((1, capacity), -1, jnp.int32)
        low = 0
        for page in range(page_total):
            high = low + table_ref[chunk * page_total + page]
            inside = (slot >= low) & (slot < high)
            position = jnp.where(inside, slot + (firsts[page] + before[page] - low), position)
            before[page] = before[page] + (high - low)
            low = high
        positions.append(position)
        rows_ref[chunk * capacity : (chunk + 1) * capacity, :] = received_ref[chunk, query_rows : query_rows + capacity, :]
    position = jnp.concatenate(positions, axis=1)
    place = (position == lax.broadcasted_iota(jnp.int32, (ordered_rows, owners * capacity), 0)).astype(jnp.bfloat16)
    ordered_ref[...] = jnp.dot(place, rows_ref[...], preferred_element_type=jnp.float32).astype(jnp.bfloat16)
    inner = lax.axis_index("inner")
    tokens_ref[:, pl.ds(pl.multiple_of(inner * query_rows, query_rows), query_rows), :] = (
        received_ref[:, 0:query_rows, :]
    )
    tokens_ref[:, pl.ds(pl.multiple_of((1 - inner) * query_rows, query_rows), query_rows), :] = partner_ref[...]
    sources = token_block // tokens_ref.shape[1]
    sub = lax.broadcasted_iota(jnp.int32, (8, token_block), 0)
    query_lane = lax.broadcasted_iota(jnp.int32, (1, total_queries), 1)
    live_count = jnp.zeros((1, total_queries), jnp.int32)
    for query in range(total_queries):
        live_count = jnp.where(query_lane == query, table_ref[owners * page_total + query], live_count)
    token_id = lax.broadcasted_iota(jnp.int32, (token_block, total_queries), 0)
    query_id = lax.broadcasted_iota(jnp.int32, (token_block, total_queries), 1)

    def block_scores(block, total):
        tokens = tokens_ref[pl.ds(block * sources, sources)].reshape(token_block, width)
        sims_ref[...] = lax.dot_general(
            ordered_ref[...], tokens, (((1,), (1,)), ((), ())), preferred_element_type=jnp.float32
        )
        best_rows = []
        for page in range(page_total):
            first = firsts[page]
            whole = totals[page] // 16
            rest = totals[page] % 16

            def step(i, carry):
                start = pl.multiple_of(first + i * 16, 16)
                return (
                    jnp.maximum(carry[0], sims_ref[pl.ds(start, 8), :]),
                    jnp.maximum(carry[1], sims_ref[pl.ds(start + 8, 8), :]),
                )

            floor = jnp.full((8, token_block), -2.0, jnp.float32)
            low, high = lax.fori_loop(0, whole, step, (floor, floor))
            start = pl.multiple_of(first + whole * 16, 16)
            low = jnp.maximum(low, jnp.where(sub < rest, sims_ref[pl.ds(start, 8), :], jnp.float32(-2.0)))
            high = jnp.maximum(high, jnp.where(sub + 8 < rest, sims_ref[pl.ds(start + 8, 8), :], jnp.float32(-2.0)))
            best_rows.append(jnp.max(jnp.maximum(low, high), axis=0, keepdims=True))
        best = jnp.concatenate(best_rows, axis=0)
        token = token_id + block * token_block
        live = ((token // token_slots) == query_id) & ((token % token_slots) < live_count)
        return total + jnp.dot(
            best, live.astype(jnp.float32), precision=lax.Precision.HIGHEST, preferred_element_type=jnp.float32
        )

    blocks = tokens_ref.shape[0] * tokens_ref.shape[1] // token_block
    out_ref[...] = lax.fori_loop(
        0, blocks, block_scores, jnp.zeros((page_total, total_queries), jnp.float32)
    )


def page_scores(received, tokens, table, total_queries, page_total, token_slots, query_rows, capacity):
    owners = received.shape[0]
    width = received.shape[2]
    ordered_rows = owners * capacity + 16 * page_total + 16
    token_total = 2 * tokens.shape[0] * tokens.shape[1]
    token_block = min(token_total, 1024)
    vmem = pl.BlockSpec(memory_space=pltpu.VMEM)
    return pl.pallas_call(
        functools.partial(score_kernel, page_total, token_slots, query_rows, token_block),
        out_shape=jax.ShapeDtypeStruct((page_total, total_queries), jnp.float32),
        in_specs=[pl.BlockSpec(memory_space=pltpu.SMEM), vmem, vmem],
        out_specs=vmem,
        scratch_shapes=[
            pltpu.VMEM((ordered_rows, width), jnp.bfloat16),
            pltpu.VMEM((ordered_rows, token_block), jnp.float32),
            pltpu.VMEM((owners * capacity, width), jnp.bfloat16),
            pltpu.VMEM((owners, 2 * query_rows, width), jnp.bfloat16),
        ],
        cost_estimate=pl.CostEstimate(
            flops=2 * ordered_rows * width * (owners * capacity + token_total),
            bytes_accessed=2 * received.size + 2 * tokens.size + 4 * page_total * total_queries,
            transcendentals=0,
        ),
    )(table, received, tokens)


def shards(patch_rows, owner_ids, page_ids, proj_weight, proj_bias, query_tokens, query_counts):
    owners = lax.axis_size("blk")
    halves = lax.axis_size("inner")
    rows = patch_rows.shape[0]
    capacity = 2 * rows // owners
    per_block = query_tokens.shape[0]
    token_slots = query_tokens.shape[1]
    width = query_tokens.shape[2]
    total_queries = per_block * owners
    half_queries = per_block // halves
    query_rows = half_queries * token_slots
    message = send_message(
        patch_rows, owner_ids, page_ids, proj_weight, proj_bias, query_tokens, query_counts, owners, capacity, halves
    )
    received = lax.all_to_all(message, "blk", split_axis=0, concat_axis=0, tiled=True)
    partner = lax.ppermute(received[:, :query_rows], "inner", [(0, 1), (1, 0)])
    block_at = -(-(query_rows + capacity) // 16) * 16
    combos = -(-owners * PAGES_DEV // 128) * 128
    count_rows = combos // 128
    page_counts = received[:, block_at : block_at + count_rows].reshape(owners, combos)
    page_counts = lax.dynamic_slice_in_dim(page_counts, lax.axis_index("blk") * PAGES_DEV, PAGES_DEV, axis=1)
    counts = received[:, block_at + count_rows, :per_block]
    table = jnp.concatenate([page_counts.reshape(owners * PAGES_DEV), counts.reshape(total_queries)]).astype(jnp.int32)
    return page_scores(received, partner, table, total_queries, PAGES_DEV, token_slots, query_rows, capacity)


def solution(mesh):
    in_specs = (
        P(("groups", "blk", "inner"), None),
        P(("groups", "blk", "inner"), None),
        P(("groups", "blk", "inner")),
        P(),
        P(),
        P(("groups", "blk"), None, None),
        P(("groups", "blk")),
    )
    out_specs = P(("groups", "blk", "inner"), None)
    return jax.shard_map(shards, mesh=mesh, in_specs=in_specs, out_specs=out_specs, check_vma=False)
```

```python
import functools
import math

import jax
import jax.numpy as jnp
from jax import lax
from jax.experimental import pallas as pl
from jax.experimental.pallas import tpu as pltpu
from jax.sharding import PartitionSpec as P

PAGES_DEV = 8


def send_kernel(page_total, capacity, query_rows, block_at, query_counts_ref, owner_ref, page_ref, rows_hbm, weight_ref,
                bias_ref, queries_ref, message_ref, rows_ref, copy_sem):
    owners = message_ref.shape[0]
    rows = rows_ref.shape[0]
    copy = pltpu.make_async_copy(rows_hbm, rows_ref, copy_sem)
    copy.start()
    combo = owner_ref[...].reshape(1, rows) * page_total + page_ref[...].reshape(1, rows)
    combos = -(-owners * page_total // 128) * 128
    combo_id = lax.broadcasted_iota(jnp.int32, (combos, rows), 0)
    onehot = (combo == combo_id).astype(jnp.bfloat16)
    lane = 128 if rows % 128 == 0 else rows
    earlier = (
        lax.broadcasted_iota(jnp.int32, (lane, lane), 0) < lax.broadcasted_iota(jnp.int32, (lane, lane), 1)
    ).astype(jnp.bfloat16)
    parts = []
    count = jnp.zeros((combos, 1), jnp.float32)
    for start in range(0, rows, lane):
        part = onehot[:, start : start + lane]
        parts.append(jnp.dot(part, earlier, preferred_element_type=jnp.float32) + count)
        count = count + jnp.sum(part.astype(jnp.float32), axis=1, keepdims=True)
    seen = jnp.concatenate(parts, axis=1)
    row_id = lax.broadcasted_iota(jnp.int32, (combos, combos), 0)
    col_id = lax.broadcasted_iota(jnp.int32, (combos, combos), 1)
    same_owner_lower = (row_id // page_total == col_id // page_total) & (col_id % page_total < row_id % page_total)
    offset = jnp.dot(same_owner_lower.astype(jnp.bfloat16), count.astype(jnp.bfloat16),
                     preferred_element_type=jnp.float32)
    base = (lax.broadcasted_iota(jnp.int32, (combos, 1), 0) // page_total * capacity).astype(jnp.float32) + offset
    slot = jnp.sum(onehot.astype(jnp.float32) * (base + seen), axis=0, keepdims=True).astype(jnp.int32)
    count_rows = [
        lax.dot_general(
            jnp.ones((1, rows), jnp.bfloat16), onehot[group * 128 : (group + 1) * 128],
            (((1,), (1,)), ((), ())), preferred_element_type=jnp.float32,
        )
        for group in range(combos // 128)
    ]
    lane = lax.broadcasted_iota(jnp.int32, (1, 128), 1)
    query_count_row = jnp.zeros((1, 128), jnp.float32)
    for query in range(query_counts_ref.shape[0]):
        query_count_row = jnp.where(lane == query, query_counts_ref[query].astype(jnp.float32), query_count_row)
    block_rows = message_ref.shape[1] - block_at
    block = jnp.concatenate(
        count_rows
        + [query_count_row, jnp.zeros((block_rows - len(count_rows) - 1, 128), jnp.float32)],
        axis=0,
    ).astype(jnp.bfloat16)
    copy.wait()
    proj = jnp.dot(rows_ref[...], weight_ref[...], preferred_element_type=jnp.float32) + bias_ref[...]
    scale = lax.rsqrt(jnp.sum(proj * proj, axis=1, keepdims=True) + 1e-06)
    local = (proj * scale).astype(jnp.bfloat16)
    own_half = queries_ref[pl.ds(pl.multiple_of(lax.axis_index("inner") * query_rows, query_rows), query_rows), :]
    slot_id = lax.broadcasted_iota(jnp.int32, (capacity, rows), 0)
    for owner in range(owners):
        placed = (slot == slot_id + owner * capacity).astype(jnp.bfloat16)
        message_ref[owner, 0:query_rows, :] = own_half
        message_ref[owner, query_rows : query_rows + capacity, :] = jnp.dot(
            placed, local, preferred_element_type=jnp.float32
        ).astype(jnp.bfloat16)
        message_ref[owner, block_at:, :] = block


def send_message(patch_rows, owner_ids, page_ids, proj_weight, proj_bias, query_tokens, query_counts, owners, capacity,
                 halves):
    rows, features = patch_rows.shape
    per_block, token_slots, width = query_tokens.shape
    query_rows = per_block // halves * token_slots
    block_at = -(-(query_rows + capacity) // 16) * 16
    vmem = pl.BlockSpec(memory_space=pltpu.VMEM)
    return pl.pallas_call(
        functools.partial(send_kernel, PAGES_DEV, capacity, query_rows, block_at),
        out_shape=jax.ShapeDtypeStruct((owners, block_at + 16, width), jnp.bfloat16),
        in_specs=[pl.BlockSpec(memory_space=pltpu.SMEM), vmem, vmem, pl.BlockSpec(memory_space=pl.ANY)] + [vmem] * 3,
        out_specs=vmem,
        scratch_shapes=[pltpu.VMEM((rows, features), jnp.bfloat16), pltpu.SemaphoreType.DMA],
        cost_estimate=pl.CostEstimate(
            flops=2 * rows * width * (features + owners * capacity),
            bytes_accessed=2 * (rows * features + features * width + owners * (block_at + 16) * width),
            transcendentals=rows,
        ),
    )(
        query_counts, owner_ids.reshape(1, rows), page_ids, patch_rows, proj_weight, proj_bias.reshape(1, width),
        query_tokens.reshape(per_block * token_slots, width),
    )


def score_kernel(page_total, token_slots, query_rows, token_block, table_ref, received_ref, partner_ref, out_ref,
                 ordered_ref, sims_ref, rows_ref, tokens_ref):
    owners = received_ref.shape[0]
    ordered_rows, width = ordered_ref.shape
    capacity = (ordered_rows - 16 * page_total - 16) // owners
    total_queries = out_ref.shape[1]
    totals = [sum(table_ref[chunk * page_total + page] for chunk in range(owners)) for page in range(page_total)]
    firsts = []
    at = 0
    for page in range(page_total):
        firsts.append(at)
        at = at + (totals[page] + 15) // 16 * 16
    slot = lax.broadcasted_iota(jnp.int32, (1, capacity), 1)
    before = [0] * page_total
    positions = []
    for chunk in range(owners):
        position = jnp.full((1, capacity), -1, jnp.int32)
        low = 0
        for page in range(page_total):
            high = low + table_ref[chunk * page_total + page]
            inside = (slot >= low) & (slot < high)
            position = jnp.where(inside, slot + (firsts[page] + before[page] - low), position)
            before[page] = before[page] + (high - low)
            low = high
        positions.append(position)
        rows_ref[chunk * capacity : (chunk + 1) * capacity, :] = received_ref[chunk, query_rows : query_rows + capacity, :]
    position = jnp.concatenate(positions, axis=1)
    place = (position == lax.broadcasted_iota(jnp.int32, (ordered_rows, owners * capacity), 0)).astype(jnp.bfloat16)
    ordered_ref[...] = jnp.dot(place, rows_ref[...], preferred_element_type=jnp.float32).astype(jnp.bfloat16)
    inner = lax.axis_index("inner")
    tokens_ref[:, pl.ds(pl.multiple_of(inner * query_rows, query_rows), query_rows), :] = (
        received_ref[:, 0:query_rows, :]
    )
    tokens_ref[:, pl.ds(pl.multiple_of((1 - inner) * query_rows, query_rows), query_rows), :] = partner_ref[...]
    sources = token_block // tokens_ref.shape[1]
    sub = lax.broadcasted_iota(jnp.int32, (8, token_block), 0)
    query_lane = lax.broadcasted_iota(jnp.int32, (1, total_queries), 1)
    live_count = jnp.zeros((1, total_queries), jnp.int32)
    for query in range(total_queries):
        live_count = jnp.where(query_lane == query, table_ref[owners * page_total + query], live_count)
    token_id = lax.broadcasted_iota(jnp.int32, (token_block, total_queries), 0)
    query_id = lax.broadcasted_iota(jnp.int32, (token_block, total_queries), 1)

    def block_scores(block, total):
        tokens = tokens_ref[pl.ds(block * sources, sources)].reshape(token_block, width)
        sims_ref[...] = lax.dot_general(
            ordered_ref[...], tokens, (((1,), (1,)), ((), ())), preferred_element_type=jnp.float32
        )
        best_rows = []
        for page in range(page_total):
            first = firsts[page]
            whole = totals[page] // 16
            rest = totals[page] % 16

            def step(i, carry):
                start = pl.multiple_of(first + i * 16, 16)
                return (
                    jnp.maximum(carry[0], sims_ref[pl.ds(start, 8), :]),
                    jnp.maximum(carry[1], sims_ref[pl.ds(start + 8, 8), :]),
                )

            floor = jnp.full((8, token_block), -2.0, jnp.float32)
            low, high = lax.fori_loop(0, whole, step, (floor, floor))
            start = pl.multiple_of(first + whole * 16, 16)
            low = jnp.maximum(low, jnp.where(sub < rest, sims_ref[pl.ds(start, 8), :], jnp.float32(-2.0)))
            high = jnp.maximum(high, jnp.where(sub + 8 < rest, sims_ref[pl.ds(start + 8, 8), :], jnp.float32(-2.0)))
            best_rows.append(jnp.max(jnp.maximum(low, high), axis=0, keepdims=True))
        best = jnp.concatenate(best_rows, axis=0)
        token = token_id + block * token_block
        live = ((token // token_slots) == query_id) & ((token % token_slots) < live_count)
        return total + jnp.dot(
            best, live.astype(jnp.float32), precision=lax.Precision.HIGHEST, preferred_element_type=jnp.float32
        )

    blocks = tokens_ref.shape[0] * tokens_ref.shape[1] // token_block
    out_ref[...] = lax.fori_loop(
        0, blocks, block_scores, jnp.zeros((page_total, total_queries), jnp.float32)
    )


def page_scores(received, tokens, table, total_queries, page_total, token_slots, query_rows, capacity):
    owners = received.shape[0]
    width = received.shape[2]
    ordered_rows = owners * capacity + 16 * page_total + 16
    token_total = 2 * tokens.shape[0] * tokens.shape[1]
    token_block = min(token_total, 1024)
    vmem = pl.BlockSpec(memory_space=pltpu.VMEM)
    return pl.pallas_call(
        functools.partial(score_kernel, page_total, token_slots, query_rows, token_block),
        out_shape=jax.ShapeDtypeStruct((page_total, total_queries), jnp.float32),
        in_specs=[pl.BlockSpec(memory_space=pltpu.SMEM), vmem, vmem],
        out_specs=vmem,
        scratch_shapes=[
            pltpu.VMEM((ordered_rows, width), jnp.bfloat16),
            pltpu.VMEM((ordered_rows, token_block), jnp.float32),
            pltpu.VMEM((owners * capacity, width), jnp.bfloat16),
            pltpu.VMEM((owners, 2 * query_rows, width), jnp.bfloat16),
        ],
        cost_estimate=pl.CostEstimate(
            flops=2 * ordered_rows * width * (owners * capacity + token_total),
            bytes_accessed=2 * received.size + 2 * tokens.size + 4 * page_total * total_queries,
            transcendentals=0,
        ),
    )(table, received, tokens)


def shards(patch_rows, owner_ids, page_ids, proj_weight, proj_bias, query_tokens, query_counts):
    owners = lax.axis_size("blk")
    halves = lax.axis_size("inner")
    rows = patch_rows.shape[0]
    capacity = 2 * rows // owners
    per_block = query_tokens.shape[0]
    token_slots = query_tokens.shape[1]
    width = query_tokens.shape[2]
    total_queries = per_block * owners
    half_queries = per_block // halves
    query_rows = half_queries * token_slots
    message = send_message(
        patch_rows, owner_ids, page_ids, proj_weight, proj_bias, query_tokens, query_counts, owners, capacity, halves
    )
    received = lax.all_to_all(message, "blk", split_axis=0, concat_axis=0, tiled=True)
    partner = lax.ppermute(received[:, :query_rows], "inner", [(0, 1), (1, 0)])
    block_at = -(-(query_rows + capacity) // 16) * 16
    combos = -(-owners * PAGES_DEV // 128) * 128
    count_rows = combos // 128
    page_counts = received[:, block_at : block_at + count_rows].reshape(owners, combos)
    page_counts = lax.dynamic_slice_in_dim(page_counts, lax.axis_index("blk") * PAGES_DEV, PAGES_DEV, axis=1)
    counts = received[:, block_at + count_rows, :per_block]
    table = jnp.concatenate([page_counts.reshape(owners * PAGES_DEV), counts.reshape(total_queries)]).astype(jnp.int32)
    return page_scores(received, partner, table, total_queries, PAGES_DEV, token_slots, query_rows, capacity)


def solution(mesh):
    in_specs = (
        P(("groups", "blk", "inner"), None),
        P(("groups", "blk", "inner"), None),
        P(("groups", "blk", "inner")),
        P(),
        P(),
        P(("groups", "blk"), None, None),
        P(("groups", "blk")),
    )
    out_specs = P(("groups", "blk", "inner"), None)
    return jax.shard_map(shards, mesh=mesh, in_specs=in_specs, out_specs=out_specs, check_vma=False)
```

```python
import functools
import math

import jax
import jax.numpy as jnp
from jax import lax
from jax.experimental import pallas as pl
from jax.experimental.pallas import tpu as pltpu
from jax.sharding import PartitionSpec as P

PAGES_DEV = 8


def send_kernel(page_total, capacity, query_rows, block_at, query_counts_ref, owner_ref, page_ref, rows_ref, weight_ref,
                bias_ref, queries_ref, message_ref):
    owners = message_ref.shape[0]
    rows = rows_ref.shape[0]
    proj = jnp.dot(rows_ref[...], weight_ref[...], preferred_element_type=jnp.float32) + bias_ref[...]
    scale = lax.rsqrt(jnp.sum(proj * proj, axis=1, keepdims=True) + 1e-06)
    local = (proj * scale).astype(jnp.bfloat16)
    combo = owner_ref[...].reshape(1, rows) * page_total + page_ref[...].reshape(1, rows)
    combos = -(-owners * page_total // 128) * 128
    combo_id = lax.broadcasted_iota(jnp.int32, (combos, rows), 0)
    onehot = (combo == combo_id).astype(jnp.bfloat16)
    lane = 128 if rows % 128 == 0 else rows
    earlier = (
        lax.broadcasted_iota(jnp.int32, (lane, lane), 0) < lax.broadcasted_iota(jnp.int32, (lane, lane), 1)
    ).astype(jnp.bfloat16)
    parts = []
    count = jnp.zeros((combos, 1), jnp.float32)
    for start in range(0, rows, lane):
        part = onehot[:, start : start + lane]
        parts.append(jnp.dot(part, earlier, preferred_element_type=jnp.float32) + count)
        count = count + jnp.sum(part.astype(jnp.float32), axis=1, keepdims=True)
    seen = jnp.concatenate(parts, axis=1)
    row_id = lax.broadcasted_iota(jnp.int32, (combos, combos), 0)
    col_id = lax.broadcasted_iota(jnp.int32, (combos, combos), 1)
    same_owner_lower = (row_id // page_total == col_id // page_total) & (col_id % page_total < row_id % page_total)
    offset = jnp.dot(same_owner_lower.astype(jnp.bfloat16), count.astype(jnp.bfloat16),
                     preferred_element_type=jnp.float32)
    base = (lax.broadcasted_iota(jnp.int32, (combos, 1), 0) // page_total * capacity).astype(jnp.float32) + offset
    slot = jnp.sum(onehot.astype(jnp.float32) * (base + seen), axis=0, keepdims=True).astype(jnp.int32)
    count_rows = [
        lax.dot_general(
            jnp.ones((1, rows), jnp.bfloat16), onehot[group * 128 : (group + 1) * 128],
            (((1,), (1,)), ((), ())), preferred_element_type=jnp.float32,
        )
        for group in range(combos // 128)
    ]
    lane = lax.broadcasted_iota(jnp.int32, (1, 128), 1)
    query_count_row = jnp.zeros((1, 128), jnp.float32)
    for query in range(query_counts_ref.shape[0]):
        query_count_row = jnp.where(lane == query, query_counts_ref[query].astype(jnp.float32), query_count_row)
    block_rows = message_ref.shape[1] - block_at
    block = jnp.concatenate(
        count_rows
        + [query_count_row, jnp.zeros((block_rows - len(count_rows) - 1, 128), jnp.float32)],
        axis=0,
    ).astype(jnp.bfloat16)
    own_half = queries_ref[pl.ds(pl.multiple_of(lax.axis_index("inner") * query_rows, query_rows), query_rows), :]
    slot_id = lax.broadcasted_iota(jnp.int32, (capacity, rows), 0).astype(jnp.bfloat16)
    for owner in range(owners):
        offset = (slot - owner * capacity).astype(jnp.bfloat16)
        placed = (offset == slot_id).astype(jnp.bfloat16)
        message_ref[owner, 0:query_rows, :] = own_half
        message_ref[owner, query_rows : query_rows + capacity, :] = jnp.dot(
            placed, local, preferred_element_type=jnp.float32
        ).astype(jnp.bfloat16)
        message_ref[owner, block_at:, :] = block


def send_message(patch_rows, owner_ids, page_ids, proj_weight, proj_bias, query_tokens, query_counts, owners, capacity,
                 halves):
    rows, features = patch_rows.shape
    per_block, token_slots, width = query_tokens.shape
    query_rows = per_block // halves * token_slots
    block_at = -(-(query_rows + capacity) // 16) * 16
    vmem = pl.BlockSpec(memory_space=pltpu.VMEM)
    return pl.pallas_call(
        functools.partial(send_kernel, PAGES_DEV, capacity, query_rows, block_at),
        out_shape=jax.ShapeDtypeStruct((owners, block_at + 16, width), jnp.bfloat16),
        in_specs=[pl.BlockSpec(memory_space=pltpu.SMEM)] + [vmem] * 6,
        out_specs=vmem,
        cost_estimate=pl.CostEstimate(
            flops=2 * rows * width * (features + owners * capacity),
            bytes_accessed=2 * (rows * features + features * width + owners * (block_at + 16) * width),
            transcendentals=rows,
        ),
    )(
        query_counts, owner_ids.reshape(1, rows), page_ids, patch_rows, proj_weight, proj_bias.reshape(1, width),
        query_tokens.reshape(per_block * token_slots, width),
    )


def score_kernel(page_total, token_slots, query_rows, token_block, table_ref, received_ref, partner_ref, out_ref,
                 ordered_ref, sims_ref, rows_ref, tokens_ref):
    owners = received_ref.shape[0]
    ordered_rows, width = ordered_ref.shape
    capacity = (ordered_rows - 16 * page_total - 16) // owners
    total_queries = out_ref.shape[1]
    totals = [sum(table_ref[chunk * page_total + page] for chunk in range(owners)) for page in range(page_total)]
    firsts = []
    at = 0
    for page in range(page_total):
        firsts.append(at)
        at = at + (totals[page] + 15) // 16 * 16
    slot = lax.broadcasted_iota(jnp.int32, (1, capacity), 1)
    before = [0] * page_total
    positions = []
    for chunk in range(owners):
        position = jnp.full((1, capacity), -1, jnp.int32)
        low = 0
        for page in range(page_total):
            high = low + table_ref[chunk * page_total + page]
            inside = (slot >= low) & (slot < high)
            position = jnp.where(inside, slot + (firsts[page] + before[page] - low), position)
            before[page] = before[page] + (high - low)
            low = high
        positions.append(position)
        rows_ref[chunk * capacity : (chunk + 1) * capacity, :] = received_ref[chunk, query_rows : query_rows + capacity, :]
    position = jnp.concatenate(positions, axis=1)
    place = (position == lax.broadcasted_iota(jnp.int32, (ordered_rows, owners * capacity), 0)).astype(jnp.bfloat16)
    ordered_ref[...] = jnp.dot(place, rows_ref[...], preferred_element_type=jnp.float32).astype(jnp.bfloat16)
    inner = lax.axis_index("inner")
    tokens_ref[:, pl.ds(pl.multiple_of(inner * query_rows, query_rows), query_rows), :] = (
        received_ref[:, 0:query_rows, :]
    )
    tokens_ref[:, pl.ds(pl.multiple_of((1 - inner) * query_rows, query_rows), query_rows), :] = partner_ref[...]
    sources = token_block // tokens_ref.shape[1]
    sub = lax.broadcasted_iota(jnp.int32, (8, token_block), 0)
    query_lane = lax.broadcasted_iota(jnp.int32, (1, total_queries), 1)
    live_count = jnp.zeros((1, total_queries), jnp.int32)
    for query in range(total_queries):
        live_count = jnp.where(query_lane == query, table_ref[owners * page_total + query], live_count)
    token_id = lax.broadcasted_iota(jnp.int32, (token_block, total_queries), 0)
    query_id = lax.broadcasted_iota(jnp.int32, (token_block, total_queries), 1)

    def block_scores(block, total):
        tokens = tokens_ref[pl.ds(block * sources, sources)].reshape(token_block, width)
        sims_ref[...] = lax.dot_general(
            ordered_ref[...], tokens, (((1,), (1,)), ((), ())), preferred_element_type=jnp.float32
        )
        best_rows = []
        for page in range(page_total):
            first = firsts[page]
            whole = totals[page] // 16
            rest = totals[page] % 16

            def step(i, carry):
                start = pl.multiple_of(first + i * 16, 16)
                return (
                    jnp.maximum(carry[0], sims_ref[pl.ds(start, 8), :]),
                    jnp.maximum(carry[1], sims_ref[pl.ds(start + 8, 8), :]),
                )

            floor = jnp.full((8, token_block), -2.0, jnp.float32)
            low, high = lax.fori_loop(0, whole, step, (floor, floor))
            start = pl.multiple_of(first + whole * 16, 16)
            low = jnp.maximum(low, jnp.where(sub < rest, sims_ref[pl.ds(start, 8), :], jnp.float32(-2.0)))
            high = jnp.maximum(high, jnp.where(sub + 8 < rest, sims_ref[pl.ds(start + 8, 8), :], jnp.float32(-2.0)))
            best_rows.append(jnp.max(jnp.maximum(low, high), axis=0, keepdims=True))
        best = jnp.concatenate(best_rows, axis=0)
        token = token_id + block * token_block
        live = ((token // token_slots) == query_id) & ((token % token_slots) < live_count)
        return total + jnp.dot(
            best, live.astype(jnp.float32), precision=lax.Precision.HIGHEST, preferred_element_type=jnp.float32
        )

    blocks = tokens_ref.shape[0] * tokens_ref.shape[1] // token_block
    out_ref[...] = lax.fori_loop(
        0, blocks, block_scores, jnp.zeros((page_total, total_queries), jnp.float32)
    )


def page_scores(received, tokens, table, total_queries, page_total, token_slots, query_rows, capacity):
    owners = received.shape[0]
    width = received.shape[2]
    ordered_rows = owners * capacity + 16 * page_total + 16
    token_total = 2 * tokens.shape[0] * tokens.shape[1]
    token_block = min(token_total, 1024)
    vmem = pl.BlockSpec(memory_space=pltpu.VMEM)
    return pl.pallas_call(
        functools.partial(score_kernel, page_total, token_slots, query_rows, token_block),
        out_shape=jax.ShapeDtypeStruct((page_total, total_queries), jnp.float32),
        in_specs=[pl.BlockSpec(memory_space=pltpu.SMEM), vmem, vmem],
        out_specs=vmem,
        scratch_shapes=[
            pltpu.VMEM((ordered_rows, width), jnp.bfloat16),
            pltpu.VMEM((ordered_rows, token_block), jnp.float32),
            pltpu.VMEM((owners * capacity, width), jnp.bfloat16),
            pltpu.VMEM((owners, 2 * query_rows, width), jnp.bfloat16),
        ],
        cost_estimate=pl.CostEstimate(
            flops=2 * ordered_rows * width * (owners * capacity + token_total),
            bytes_accessed=2 * received.size + 2 * tokens.size + 4 * page_total * total_queries,
            transcendentals=0,
        ),
    )(table, received, tokens)


def shards(patch_rows, owner_ids, page_ids, proj_weight, proj_bias, query_tokens, query_counts):
    owners = lax.axis_size("blk")
    halves = lax.axis_size("inner")
    rows = patch_rows.shape[0]
    capacity = 2 * rows // owners
    per_block = query_tokens.shape[0]
    token_slots = query_tokens.shape[1]
    width = query_tokens.shape[2]
    total_queries = per_block * owners
    half_queries = per_block // halves
    query_rows = half_queries * token_slots
    message = send_message(
        patch_rows, owner_ids, page_ids, proj_weight, proj_bias, query_tokens, query_counts, owners, capacity, halves
    )
    received = lax.all_to_all(message, "blk", split_axis=0, concat_axis=0, tiled=True)
    partner = lax.ppermute(received[:, :query_rows], "inner", [(0, 1), (1, 0)])
    block_at = -(-(query_rows + capacity) // 16) * 16
    combos = -(-owners * PAGES_DEV // 128) * 128
    count_rows = combos // 128
    page_counts = received[:, block_at : block_at + count_rows].reshape(owners, combos)
    page_counts = lax.dynamic_slice_in_dim(page_counts, lax.axis_index("blk") * PAGES_DEV, PAGES_DEV, axis=1)
    counts = received[:, block_at + count_rows, :per_block]
    table = jnp.concatenate([page_counts.reshape(owners * PAGES_DEV), counts.reshape(total_queries)]).astype(jnp.int32)
    return page_scores(received, partner, table, total_queries, PAGES_DEV, token_slots, query_rows, capacity)


def solution(mesh):
    in_specs = (
        P(("groups", "blk", "inner"), None),
        P(("groups", "blk", "inner"), None),
        P(("groups", "blk", "inner")),
        P(),
        P(),
        P(("groups", "blk"), None, None),
        P(("groups", "blk")),
    )
    out_specs = P(("groups", "blk", "inner"), None)
    return jax.shard_map(shards, mesh=mesh, in_specs=in_specs, out_specs=out_specs, check_vma=False)
```

```python
import functools
import math

import jax
import jax.numpy as jnp
from jax import lax
from jax.experimental import pallas as pl
from jax.experimental.pallas import tpu as pltpu
from jax.sharding import PartitionSpec as P

PAGES_DEV = 8


def send_kernel(page_total, capacity, query_rows, block_at, query_counts_ref, owner_ref, page_ref, rows_ref, weight_ref,
                bias_ref, queries_ref, message_ref):
    owners = message_ref.shape[0]
    rows = rows_ref.shape[0]
    proj = jnp.dot(rows_ref[...], weight_ref[...], preferred_element_type=jnp.float32) + bias_ref[...]
    scale = lax.rsqrt(jnp.sum(proj * proj, axis=1, keepdims=True) + 1e-06)
    local = (proj * scale).astype(jnp.bfloat16)
    combo = owner_ref[...].reshape(1, rows) * page_total + page_ref[...].reshape(1, rows)
    combos = -(-owners * page_total // 128) * 128
    combo_id = lax.broadcasted_iota(jnp.int32, (combos, rows), 0)
    onehot = (combo == combo_id).astype(jnp.bfloat16)
    lane = 128 if rows % 128 == 0 else rows
    earlier = (
        lax.broadcasted_iota(jnp.int32, (lane, lane), 0) < lax.broadcasted_iota(jnp.int32, (lane, lane), 1)
    ).astype(jnp.bfloat16)
    parts = []
    count = jnp.zeros((combos, 1), jnp.float32)
    for start in range(0, rows, lane):
        part = onehot[:, start : start + lane]
        parts.append(jnp.dot(part, earlier, preferred_element_type=jnp.float32) + count)
        count = count + jnp.sum(part.astype(jnp.float32), axis=1, keepdims=True)
    seen = jnp.concatenate(parts, axis=1)
    row_id = lax.broadcasted_iota(jnp.int32, (combos, combos), 0)
    col_id = lax.broadcasted_iota(jnp.int32, (combos, combos), 1)
    same_owner_lower = (row_id // page_total == col_id // page_total) & (col_id % page_total < row_id % page_total)
    offset = jnp.dot(same_owner_lower.astype(jnp.bfloat16), count.astype(jnp.bfloat16),
                     preferred_element_type=jnp.float32)
    base = (lax.broadcasted_iota(jnp.int32, (combos, 1), 0) // page_total * capacity).astype(jnp.float32) + offset
    slot = jnp.sum(onehot.astype(jnp.float32) * (base + seen), axis=0, keepdims=True).astype(jnp.int32)
    count_rows = [
        lax.dot_general(
            jnp.ones((1, rows), jnp.bfloat16), onehot[group * 128 : (group + 1) * 128],
            (((1,), (1,)), ((), ())), preferred_element_type=jnp.float32,
        )
        for group in range(combos // 128)
    ]
    lane = lax.broadcasted_iota(jnp.int32, (1, 128), 1)
    query_count_row = jnp.zeros((1, 128), jnp.float32)
    for query in range(query_counts_ref.shape[0]):
        query_count_row = jnp.where(lane == query, query_counts_ref[query].astype(jnp.float32), query_count_row)
    block_rows = message_ref.shape[1] - block_at
    block = jnp.concatenate(
        count_rows
        + [query_count_row, jnp.zeros((block_rows - len(count_rows) - 1, 128), jnp.float32)],
        axis=0,
    ).astype(jnp.bfloat16)
    own_half = queries_ref[pl.ds(pl.multiple_of(lax.axis_index("inner") * query_rows, query_rows), query_rows), :]
    slot_id = lax.broadcasted_iota(jnp.int32, (capacity, rows), 0)
    for owner in range(owners):
        placed = (slot == slot_id + owner * capacity).astype(jnp.bfloat16)
        message_ref[owner, 0:query_rows, :] = own_half
        message_ref[owner, query_rows : query_rows + capacity, :] = jnp.dot(
            placed, local, preferred_element_type=jnp.float32
        ).astype(jnp.bfloat16)
        message_ref[owner, block_at:, :] = block


def send_message(patch_rows, owner_ids, page_ids, proj_weight, proj_bias, query_tokens, query_counts, owners, capacity,
                 halves):
    rows, features = patch_rows.shape
    per_block, token_slots, width = query_tokens.shape
    query_rows = per_block // halves * token_slots
    block_at = -(-(query_rows + capacity) // 16) * 16
    vmem = pl.BlockSpec(memory_space=pltpu.VMEM)
    return pl.pallas_call(
        functools.partial(send_kernel, PAGES_DEV, capacity, query_rows, block_at),
        out_shape=jax.ShapeDtypeStruct((owners, block_at + 16, width), jnp.bfloat16),
        in_specs=[pl.BlockSpec(memory_space=pltpu.SMEM)] + [vmem] * 6,
        out_specs=vmem,
        cost_estimate=pl.CostEstimate(
            flops=2 * rows * width * (features + owners * capacity),
            bytes_accessed=2 * (rows * features + features * width + owners * (block_at + 16) * width),
            transcendentals=rows,
        ),
    )(
        query_counts, owner_ids.reshape(1, rows), page_ids, patch_rows, proj_weight, proj_bias.reshape(1, width),
        query_tokens.reshape(per_block * token_slots, width),
    )


def score_kernel(page_total, token_slots, query_rows, token_block, table_ref, received_ref, partner_ref, out_ref,
                 ordered_ref, sims_ref, rows_ref, tokens_ref):
    owners = received_ref.shape[0]
    ordered_rows, width = ordered_ref.shape
    capacity = (ordered_rows - 16 * page_total - 16) // owners
    total_queries = out_ref.shape[1]
    totals = [sum(table_ref[chunk * page_total + page] for chunk in range(owners)) for page in range(page_total)]
    firsts = []
    at = 0
    for page in range(page_total):
        firsts.append(at)
        at = at + (totals[page] + 15) // 16 * 16
    slot = lax.broadcasted_iota(jnp.int32, (1, capacity), 1)
    before = [0] * page_total
    positions = []
    for chunk in range(owners):
        position = jnp.full((1, capacity), -1, jnp.int32)
        low = 0
        for page in range(page_total):
            high = low + table_ref[chunk * page_total + page]
            inside = (slot >= low) & (slot < high)
            position = jnp.where(inside, slot + (firsts[page] + before[page] - low), position)
            before[page] = before[page] + (high - low)
            low = high
        positions.append(position)
        rows_ref[chunk * capacity : (chunk + 1) * capacity, :] = received_ref[chunk, query_rows : query_rows + capacity, :]
    position = jnp.concatenate(positions, axis=1)
    place = (position == lax.broadcasted_iota(jnp.int32, (ordered_rows, owners * capacity), 0)).astype(jnp.bfloat16)
    ordered_ref[...] = jnp.dot(place, rows_ref[...], preferred_element_type=jnp.float32).astype(jnp.bfloat16)
    inner = lax.axis_index("inner")
    tokens_ref[:, pl.ds(pl.multiple_of(inner * query_rows, query_rows), query_rows), :] = (
        received_ref[:, 0:query_rows, :]
    )
    tokens_ref[:, pl.ds(pl.multiple_of((1 - inner) * query_rows, query_rows), query_rows), :] = partner_ref[...]
    sources = token_block // tokens_ref.shape[1]
    sub = lax.broadcasted_iota(jnp.int32, (8, token_block), 0)
    query_lane = lax.broadcasted_iota(jnp.int32, (1, total_queries), 1)
    live_count = jnp.zeros((1, total_queries), jnp.int32)
    for query in range(total_queries):
        live_count = jnp.where(query_lane == query, table_ref[owners * page_total + query], live_count)
    token_id = lax.broadcasted_iota(jnp.int32, (token_block, total_queries), 0)
    query_id = lax.broadcasted_iota(jnp.int32, (token_block, total_queries), 1)
    query_gap = query_id - token_id // token_slots
    slot_live = (token_id % token_slots) < live_count

    def block_scores(block, total):
        tokens = tokens_ref[pl.ds(block * sources, sources)].reshape(token_block, width)
        sims_ref[...] = lax.dot_general(
            ordered_ref[...], tokens, (((1,), (1,)), ((), ())), preferred_element_type=jnp.float32
        )
        best_rows = []
        for page in range(page_total):
            first = firsts[page]
            whole = totals[page] // 16
            rest = totals[page] % 16

            def step(i, carry):
                start = pl.multiple_of(first + i * 16, 16)
                return (
                    jnp.maximum(carry[0], sims_ref[pl.ds(start, 8), :]),
                    jnp.maximum(carry[1], sims_ref[pl.ds(start + 8, 8), :]),
                )

            floor = jnp.full((8, token_block), -2.0, jnp.float32)
            low, high = lax.fori_loop(0, whole, step, (floor, floor))
            start = pl.multiple_of(first + whole * 16, 16)
            low = jnp.maximum(low, jnp.where(sub < rest, sims_ref[pl.ds(start, 8), :], jnp.float32(-2.0)))
            high = jnp.maximum(high, jnp.where(sub + 8 < rest, sims_ref[pl.ds(start + 8, 8), :], jnp.float32(-2.0)))
            best_rows.append(jnp.max(jnp.maximum(low, high), axis=0, keepdims=True))
        best = jnp.concatenate(best_rows, axis=0)
        live = (query_gap == block * (token_block // token_slots)) & slot_live
        return total + jnp.dot(
            best, live.astype(jnp.float32), precision=lax.Precision.HIGHEST, preferred_element_type=jnp.float32
        )

    blocks = tokens_ref.shape[0] * tokens_ref.shape[1] // token_block
    out_ref[...] = lax.fori_loop(
        0, blocks, block_scores, jnp.zeros((page_total, total_queries), jnp.float32)
    )


def page_scores(received, tokens, table, total_queries, page_total, token_slots, query_rows, capacity):
    owners = received.shape[0]
    width = received.shape[2]
    ordered_rows = owners * capacity + 16 * page_total + 16
    token_total = 2 * tokens.shape[0] * tokens.shape[1]
    token_block = min(token_total, 1024)
    vmem = pl.BlockSpec(memory_space=pltpu.VMEM)
    return pl.pallas_call(
        functools.partial(score_kernel, page_total, token_slots, query_rows, token_block),
        out_shape=jax.ShapeDtypeStruct((page_total, total_queries), jnp.float32),
        in_specs=[pl.BlockSpec(memory_space=pltpu.SMEM), vmem, vmem],
        out_specs=vmem,
        scratch_shapes=[
            pltpu.VMEM((ordered_rows, width), jnp.bfloat16),
            pltpu.VMEM((ordered_rows, token_block), jnp.float32),
            pltpu.VMEM((owners * capacity, width), jnp.bfloat16),
            pltpu.VMEM((owners, 2 * query_rows, width), jnp.bfloat16),
        ],
        cost_estimate=pl.CostEstimate(
            flops=2 * ordered_rows * width * (owners * capacity + token_total),
            bytes_accessed=2 * received.size + 2 * tokens.size + 4 * page_total * total_queries,
            transcendentals=0,
        ),
    )(table, received, tokens)


def shards(patch_rows, owner_ids, page_ids, proj_weight, proj_bias, query_tokens, query_counts):
    owners = lax.axis_size("blk")
    halves = lax.axis_size("inner")
    rows = patch_rows.shape[0]
    capacity = 2 * rows // owners
    per_block = query_tokens.shape[0]
    token_slots = query_tokens.shape[1]
    width = query_tokens.shape[2]
    total_queries = per_block * owners
    half_queries = per_block // halves
    query_rows = half_queries * token_slots
    message = send_message(
        patch_rows, owner_ids, page_ids, proj_weight, proj_bias, query_tokens, query_counts, owners, capacity, halves
    )
    received = lax.all_to_all(message, "blk", split_axis=0, concat_axis=0, tiled=True)
    partner = lax.ppermute(received[:, :query_rows], "inner", [(0, 1), (1, 0)])
    block_at = -(-(query_rows + capacity) // 16) * 16
    combos = -(-owners * PAGES_DEV // 128) * 128
    count_rows = combos // 128
    page_counts = received[:, block_at : block_at + count_rows].reshape(owners, combos)
    page_counts = lax.dynamic_slice_in_dim(page_counts, lax.axis_index("blk") * PAGES_DEV, PAGES_DEV, axis=1)
    counts = received[:, block_at + count_rows, :per_block]
    table = jnp.concatenate([page_counts.reshape(owners * PAGES_DEV), counts.reshape(total_queries)]).astype(jnp.int32)
    return page_scores(received, partner, table, total_queries, PAGES_DEV, token_slots, query_rows, capacity)


def solution(mesh):
    in_specs = (
        P(("groups", "blk", "inner"), None),
        P(("groups", "blk", "inner"), None),
        P(("groups", "blk", "inner")),
        P(),
        P(),
        P(("groups", "blk"), None, None),
        P(("groups", "blk")),
    )
    out_specs = P(("groups", "blk", "inner"), None)
    return jax.shard_map(shards, mesh=mesh, in_specs=in_specs, out_specs=out_specs, check_vma=False)
```

```python
import functools
import math

import jax
import jax.numpy as jnp
from jax import lax
from jax.experimental import pallas as pl
from jax.experimental.pallas import tpu as pltpu
from jax.sharding import PartitionSpec as P

PAGES_DEV = 8


def send_kernel(page_total, capacity, query_rows, block_at, query_counts_ref, owner_ref, page_ref, rows_ref, weight_ref,
                bias_ref, queries_ref, message_ref):
    owners = message_ref.shape[0]
    rows = rows_ref.shape[0]
    proj = jnp.dot(rows_ref[...], weight_ref[...], preferred_element_type=jnp.float32) + bias_ref[...]
    scale = lax.rsqrt(jnp.sum(proj * proj, axis=1, keepdims=True) + 1e-06)
    local = (proj * scale).astype(jnp.bfloat16)
    combo = owner_ref[...].reshape(1, rows) * page_total + page_ref[...].reshape(1, rows)
    combos = -(-owners * page_total // 128) * 128
    combo_id = lax.broadcasted_iota(jnp.int32, (combos, rows), 0)
    onehot = (combo == combo_id).astype(jnp.bfloat16)
    lane = 128 if rows % 128 == 0 else rows
    earlier = (
        lax.broadcasted_iota(jnp.int32, (lane, lane), 0) < lax.broadcasted_iota(jnp.int32, (lane, lane), 1)
    ).astype(jnp.bfloat16)
    parts = []
    count = jnp.zeros((combos, 1), jnp.float32)
    for start in range(0, rows, lane):
        part = onehot[:, start : start + lane]
        parts.append(jnp.dot(part, earlier, preferred_element_type=jnp.float32) + count)
        count = count + jnp.sum(part.astype(jnp.float32), axis=1, keepdims=True)
    seen = jnp.concatenate(parts, axis=1)
    row_id = lax.broadcasted_iota(jnp.int32, (combos, combos), 0)
    col_id = lax.broadcasted_iota(jnp.int32, (combos, combos), 1)
    same_owner_lower = (row_id // page_total == col_id // page_total) & (col_id % page_total < row_id % page_total)
    offset = jnp.dot(same_owner_lower.astype(jnp.bfloat16), count.astype(jnp.bfloat16),
                     preferred_element_type=jnp.float32)
    base = (lax.broadcasted_iota(jnp.int32, (combos, 1), 0) // page_total * capacity).astype(jnp.float32) + offset
    slot = jnp.sum(onehot.astype(jnp.float32) * (base + seen), axis=0, keepdims=True).astype(jnp.int32)
    count_rows = [
        lax.dot_general(
            jnp.ones((1, rows), jnp.bfloat16), onehot[group * 128 : (group + 1) * 128],
            (((1,), (1,)), ((), ())), preferred_element_type=jnp.float32,
        )
        for group in range(combos // 128)
    ]
    lane = lax.broadcasted_iota(jnp.int32, (1, 128), 1)
    query_count_row = jnp.zeros((1, 128), jnp.float32)
    for query in range(query_counts_ref.shape[0]):
        query_count_row = jnp.where(lane == query, query_counts_ref[query].astype(jnp.float32), query_count_row)
    block_rows = message_ref.shape[1] - block_at
    block = jnp.concatenate(
        count_rows
        + [query_count_row, jnp.zeros((block_rows - len(count_rows) - 1, 128), jnp.float32)],
        axis=0,
    ).astype(jnp.bfloat16)
    own_half = queries_ref[pl.ds(pl.multiple_of(lax.axis_index("inner") * query_rows, query_rows), query_rows), :]
    slot_id = lax.broadcasted_iota(jnp.int32, (capacity, rows), 0)
    for owner in range(owners):
        placed = (slot == slot_id + owner * capacity).astype(jnp.bfloat16)
        message_ref[owner, 0:query_rows, :] = own_half
        message_ref[owner, query_rows : query_rows + capacity, :] = jnp.dot(
            placed, local, preferred_element_type=jnp.float32
        ).astype(jnp.bfloat16)
        message_ref[owner, block_at:, :] = block


def send_message(patch_rows, owner_ids, page_ids, proj_weight, proj_bias, query_tokens, query_counts, owners, capacity,
                 halves):
    rows, features = patch_rows.shape
    per_block, token_slots, width = query_tokens.shape
    query_rows = per_block // halves * token_slots
    block_at = -(-(query_rows + capacity) // 16) * 16
    vmem = pl.BlockSpec(memory_space=pltpu.VMEM)
    return pl.pallas_call(
        functools.partial(send_kernel, PAGES_DEV, capacity, query_rows, block_at),
        out_shape=jax.ShapeDtypeStruct((owners, block_at + 16, width), jnp.bfloat16),
        in_specs=[pl.BlockSpec(memory_space=pltpu.SMEM)] + [vmem] * 6,
        out_specs=vmem,
        cost_estimate=pl.CostEstimate(
            flops=2 * rows * width * (features + owners * capacity),
            bytes_accessed=2 * (rows * features + features * width + owners * (block_at + 16) * width),
            transcendentals=rows,
        ),
    )(
        query_counts, owner_ids.reshape(1, rows), page_ids, patch_rows, proj_weight, proj_bias.reshape(1, width),
        query_tokens.reshape(per_block * token_slots, width),
    )


def score_kernel(page_total, token_slots, query_rows, token_block, table_ref, received_ref, partner_ref, out_ref,
                 ordered_ref, sims_ref, rows_ref, tokens_ref):
    owners = received_ref.shape[0]
    ordered_rows, width = ordered_ref.shape
    capacity = (ordered_rows - 16 * page_total - 16) // owners
    total_queries = out_ref.shape[1]
    totals = [sum(table_ref[chunk * page_total + page] for chunk in range(owners)) for page in range(page_total)]
    firsts = []
    at = 0
    for page in range(page_total):
        firsts.append(at)
        at = at + (totals[page] + 15) // 16 * 16
    slot = lax.broadcasted_iota(jnp.int32, (1, capacity), 1)
    before = [0] * page_total
    positions = []
    for chunk in range(owners):
        position = jnp.full((1, capacity), -1, jnp.int32)
        low = 0
        for page in range(page_total):
            high = low + table_ref[chunk * page_total + page]
            inside = (slot >= low) & (slot < high)
            position = jnp.where(inside, slot + (firsts[page] + before[page] - low), position)
            before[page] = before[page] + (high - low)
            low = high
        positions.append(position)
        rows_ref[chunk * capacity : (chunk + 1) * capacity, :] = received_ref[chunk, query_rows : query_rows + capacity, :]
    position = jnp.concatenate(positions, axis=1)
    place = (position == lax.broadcasted_iota(jnp.int32, (ordered_rows, owners * capacity), 0)).astype(jnp.bfloat16)
    ordered_ref[...] = jnp.dot(place, rows_ref[...], preferred_element_type=jnp.float32).astype(jnp.bfloat16)
    inner = lax.axis_index("inner")
    tokens_ref[:, pl.ds(pl.multiple_of(inner * query_rows, query_rows), query_rows), :] = (
        received_ref[:, 0:query_rows, :]
    )
    tokens_ref[:, pl.ds(pl.multiple_of((1 - inner) * query_rows, query_rows), query_rows), :] = partner_ref[...]
    sources = token_block // tokens_ref.shape[1]
    sub = lax.broadcasted_iota(jnp.int32, (8, token_block), 0)
    query_lane = lax.broadcasted_iota(jnp.int32, (1, total_queries), 1)
    live_count = jnp.zeros((1, total_queries), jnp.int32)
    for query in range(total_queries):
        live_count = jnp.where(query_lane == query, table_ref[owners * page_total + query], live_count)
    token_id = lax.broadcasted_iota(jnp.int32, (token_block, total_queries), 0)
    query_id = lax.broadcasted_iota(jnp.int32, (token_block, total_queries), 1)
    query_gap = query_id - token_id // token_slots
    slot_live = (token_id % token_slots) < live_count

    def block_scores(block, total):
        tokens = tokens_ref[pl.ds(block * sources, sources)].reshape(token_block, width)
        sims_ref[...] = lax.dot_general(
            ordered_ref[...], tokens, (((1,), (1,)), ((), ())), preferred_element_type=jnp.float32
        )
        best_rows = []
        for page in range(page_total):
            first = firsts[page]
            whole = totals[page] // 16
            rest = totals[page] % 16

            def step(i, carry):
                start = pl.multiple_of(first + i * 16, 16)
                return (
                    jnp.maximum(carry[0], sims_ref[pl.ds(start, 8), :]),
                    jnp.maximum(carry[1], sims_ref[pl.ds(start + 8, 8), :]),
                )

            floor = jnp.full((8, token_block), -2.0, jnp.float32)
            low, high = lax.fori_loop(0, whole, step, (floor, floor))
            start = pl.multiple_of(first + whole * 16, 16)
            low = jnp.maximum(low, jnp.where(sub < rest, sims_ref[pl.ds(start, 8), :], jnp.float32(-2.0)))
            high = jnp.maximum(high, jnp.where(sub + 8 < rest, sims_ref[pl.ds(start + 8, 8), :], jnp.float32(-2.0)))
            best_rows.append(jnp.max(jnp.maximum(low, high), axis=0, keepdims=True))
        best = jnp.concatenate(best_rows, axis=0)
        live = (query_gap == block * (token_block // token_slots)) & slot_live
        return total + jnp.dot(
            best, live.astype(jnp.float32), precision=lax.Precision.HIGHEST, preferred_element_type=jnp.float32
        )

    blocks = tokens_ref.shape[0] * tokens_ref.shape[1] // token_block
    out_ref[...] = lax.fori_loop(
        0, blocks, block_scores, jnp.zeros((page_total, total_queries), jnp.float32), unroll=blocks <= 4
    )


def page_scores(received, tokens, table, total_queries, page_total, token_slots, query_rows, capacity):
    owners = received.shape[0]
    width = received.shape[2]
    ordered_rows = owners * capacity + 16 * page_total + 16
    token_total = 2 * tokens.shape[0] * tokens.shape[1]
    token_block = min(token_total, 1024)
    vmem = pl.BlockSpec(memory_space=pltpu.VMEM)
    return pl.pallas_call(
        functools.partial(score_kernel, page_total, token_slots, query_rows, token_block),
        out_shape=jax.ShapeDtypeStruct((page_total, total_queries), jnp.float32),
        in_specs=[pl.BlockSpec(memory_space=pltpu.SMEM), vmem, vmem],
        out_specs=vmem,
        scratch_shapes=[
            pltpu.VMEM((ordered_rows, width), jnp.bfloat16),
            pltpu.VMEM((ordered_rows, token_block), jnp.float32),
            pltpu.VMEM((owners * capacity, width), jnp.bfloat16),
            pltpu.VMEM((owners, 2 * query_rows, width), jnp.bfloat16),
        ],
        cost_estimate=pl.CostEstimate(
            flops=2 * ordered_rows * width * (owners * capacity + token_total),
            bytes_accessed=2 * received.size + 2 * tokens.size + 4 * page_total * total_queries,
            transcendentals=0,
        ),
    )(table, received, tokens)


def shards(patch_rows, owner_ids, page_ids, proj_weight, proj_bias, query_tokens, query_counts):
    owners = lax.axis_size("blk")
    halves = lax.axis_size("inner")
    rows = patch_rows.shape[0]
    capacity = 2 * rows // owners
    per_block = query_tokens.shape[0]
    token_slots = query_tokens.shape[1]
    width = query_tokens.shape[2]
    total_queries = per_block * owners
    half_queries = per_block // halves
    query_rows = half_queries * token_slots
    message = send_message(
        patch_rows, owner_ids, page_ids, proj_weight, proj_bias, query_tokens, query_counts, owners, capacity, halves
    )
    received = lax.all_to_all(message, "blk", split_axis=0, concat_axis=0, tiled=True)
    partner = lax.ppermute(received[:, :query_rows], "inner", [(0, 1), (1, 0)])
    block_at = -(-(query_rows + capacity) // 16) * 16
    combos = -(-owners * PAGES_DEV // 128) * 128
    count_rows = combos // 128
    page_counts = received[:, block_at : block_at + count_rows].reshape(owners, combos)
    page_counts = lax.dynamic_slice_in_dim(page_counts, lax.axis_index("blk") * PAGES_DEV, PAGES_DEV, axis=1)
    counts = received[:, block_at + count_rows, :per_block]
    table = jnp.concatenate([page_counts.reshape(owners * PAGES_DEV), counts.reshape(total_queries)]).astype(jnp.int32)
    return page_scores(received, partner, table, total_queries, PAGES_DEV, token_slots, query_rows, capacity)


def solution(mesh):
    in_specs = (
        P(("groups", "blk", "inner"), None),
        P(("groups", "blk", "inner"), None),
        P(("groups", "blk", "inner")),
        P(),
        P(),
        P(("groups", "blk"), None, None),
        P(("groups", "blk")),
    )
    out_specs = P(("groups", "blk", "inner"), None)
    return jax.shard_map(shards, mesh=mesh, in_specs=in_specs, out_specs=out_specs, check_vma=False)
```

```python
import functools
import math

import jax
import jax.numpy as jnp
from jax import lax
from jax.experimental import pallas as pl
from jax.experimental.pallas import tpu as pltpu
from jax.sharding import PartitionSpec as P

PAGES_DEV = 8


def send_kernel(page_total, capacity, query_rows, block_at, query_counts_ref, owner_ref, page_ref, rows_ref, weight_ref,
                bias_ref, queries_ref, message_ref):
    owners = message_ref.shape[0]
    rows = rows_ref.shape[0]
    proj = jnp.dot(rows_ref[...], weight_ref[...], preferred_element_type=jnp.float32) + bias_ref[...]
    scale = lax.rsqrt(jnp.sum(proj * proj, axis=1, keepdims=True) + 1e-06)
    local = (proj * scale).astype(jnp.bfloat16)
    combo = owner_ref[...].reshape(1, rows) * page_total + page_ref[...].reshape(1, rows)
    combos = -(-owners * page_total // 128) * 128
    combo_id = lax.broadcasted_iota(jnp.int32, (combos, rows), 0)
    onehot = (combo == combo_id).astype(jnp.bfloat16)
    lane = 128 if rows % 128 == 0 else rows
    earlier = (
        lax.broadcasted_iota(jnp.int32, (lane, lane), 0) < lax.broadcasted_iota(jnp.int32, (lane, lane), 1)
    ).astype(jnp.bfloat16)
    parts = []
    count = jnp.zeros((combos, 1), jnp.float32)
    for start in range(0, rows, lane):
        part = onehot[:, start : start + lane]
        parts.append(jnp.dot(part, earlier, preferred_element_type=jnp.float32) + count)
        count = count + jnp.sum(part.astype(jnp.float32), axis=1, keepdims=True)
    seen = jnp.concatenate(parts, axis=1)
    row_id = lax.broadcasted_iota(jnp.int32, (combos, combos), 0)
    col_id = lax.broadcasted_iota(jnp.int32, (combos, combos), 1)
    same_owner_lower = (row_id // page_total == col_id // page_total) & (col_id % page_total < row_id % page_total)
    offset = jnp.dot(same_owner_lower.astype(jnp.bfloat16), count.astype(jnp.bfloat16),
                     preferred_element_type=jnp.float32)
    base = (lax.broadcasted_iota(jnp.int32, (combos, 1), 0) // page_total * capacity).astype(jnp.float32) + offset
    slot = jnp.sum(onehot.astype(jnp.float32) * (base + seen), axis=0, keepdims=True).astype(jnp.int32)
    count_rows = [
        lax.dot_general(
            jnp.ones((1, rows), jnp.bfloat16), onehot[group * 128 : (group + 1) * 128],
            (((1,), (1,)), ((), ())), preferred_element_type=jnp.float32,
        )
        for group in range(combos // 128)
    ]
    lane = lax.broadcasted_iota(jnp.int32, (1, 128), 1)
    query_count_row = jnp.zeros((1, 128), jnp.float32)
    for query in range(query_counts_ref.shape[0]):
        query_count_row = jnp.where(lane == query, query_counts_ref[query].astype(jnp.float32), query_count_row)
    block_rows = message_ref.shape[1] - block_at
    block = jnp.concatenate(
        count_rows
        + [query_count_row, jnp.zeros((block_rows - len(count_rows) - 1, 128), jnp.float32)],
        axis=0,
    ).astype(jnp.bfloat16)
    own_half = queries_ref[pl.ds(pl.multiple_of(lax.axis_index("inner") * query_rows, query_rows), query_rows), :]
    slot_id = lax.broadcasted_iota(jnp.int32, (capacity, rows), 0)
    for owner in range(owners):
        placed = (slot == slot_id + owner * capacity).astype(jnp.bfloat16)
        message_ref[owner, 0:query_rows, :] = own_half
        message_ref[owner, query_rows : query_rows + capacity, :] = jnp.dot(
            placed, local, preferred_element_type=jnp.float32
        ).astype(jnp.bfloat16)
        message_ref[owner, block_at:, :] = block


def send_message(patch_rows, owner_ids, page_ids, proj_weight, proj_bias, query_tokens, query_counts, owners, capacity,
                 halves):
    rows, features = patch_rows.shape
    per_block, token_slots, width = query_tokens.shape
    query_rows = per_block // halves * token_slots
    block_at = -(-(query_rows + capacity) // 16) * 16
    vmem = pl.BlockSpec(memory_space=pltpu.VMEM)
    return pl.pallas_call(
        functools.partial(send_kernel, PAGES_DEV, capacity, query_rows, block_at),
        out_shape=jax.ShapeDtypeStruct((owners, block_at + 16, width), jnp.bfloat16),
        in_specs=[pl.BlockSpec(memory_space=pltpu.SMEM)] + [vmem] * 6,
        out_specs=vmem,
        cost_estimate=pl.CostEstimate(
            flops=2 * rows * width * (features + owners * capacity),
            bytes_accessed=2 * (rows * features + features * width + owners * (block_at + 16) * width),
            transcendentals=rows,
        ),
    )(
        query_counts, owner_ids.reshape(1, rows), page_ids, patch_rows, proj_weight, proj_bias.reshape(1, width),
        query_tokens.reshape(per_block * token_slots, width),
    )


def score_kernel(page_total, token_slots, query_rows, token_block, table_ref, received_ref, partner_ref, out_ref,
                 ordered_ref, sims_ref, rows_ref, tokens_ref):
    owners = received_ref.shape[0]
    ordered_rows, width = ordered_ref.shape
    capacity = (ordered_rows - 16 * page_total - 16) // owners
    total_queries = out_ref.shape[1]
    totals = [sum(table_ref[chunk * page_total + page] for chunk in range(owners)) for page in range(page_total)]
    firsts = []
    at = 0
    for page in range(page_total):
        firsts.append(at)
        at = at + (totals[page] + 15) // 16 * 16
    slot = lax.broadcasted_iota(jnp.int32, (1, capacity), 1)
    before = [0] * page_total
    positions = []
    for chunk in range(owners):
        position = jnp.full((1, capacity), -1, jnp.int32)
        low = 0
        for page in range(page_total):
            high = low + table_ref[chunk * page_total + page]
            inside = (slot >= low) & (slot < high)
            position = jnp.where(inside, slot + (firsts[page] + before[page] - low), position)
            before[page] = before[page] + (high - low)
            low = high
        positions.append(position)
        rows_ref[chunk * capacity : (chunk + 1) * capacity, :] = received_ref[chunk, query_rows : query_rows + capacity, :]
    position = jnp.concatenate(positions, axis=1)
    place = (position == lax.broadcasted_iota(jnp.int32, (ordered_rows, owners * capacity), 0)).astype(jnp.bfloat16)
    ordered_ref[...] = jnp.dot(place, rows_ref[...], preferred_element_type=jnp.float32).astype(jnp.bfloat16)
    inner = lax.axis_index("inner")
    tokens_ref[:, pl.ds(pl.multiple_of(inner * query_rows, query_rows), query_rows), :] = (
        received_ref[:, 0:query_rows, :]
    )
    tokens_ref[:, pl.ds(pl.multiple_of((1 - inner) * query_rows, query_rows), query_rows), :] = partner_ref[...]
    sources = token_block // tokens_ref.shape[1]
    sub = lax.broadcasted_iota(jnp.int32, (8, token_block), 0)
    query_lane = lax.broadcasted_iota(jnp.int32, (1, total_queries), 1)
    live_count = jnp.zeros((1, total_queries), jnp.int32)
    for query in range(total_queries):
        live_count = jnp.where(query_lane == query, table_ref[owners * page_total + query], live_count)
    token_id = lax.broadcasted_iota(jnp.int32, (token_block, total_queries), 0)
    query_id = lax.broadcasted_iota(jnp.int32, (token_block, total_queries), 1)
    query_gap = query_id - token_id // token_slots
    slot_live = (token_id % token_slots) < live_count

    def block_scores(block, total):
        tokens = tokens_ref[pl.ds(block * sources, sources)].reshape(token_block, width)
        sims_ref[...] = lax.dot_general(
            ordered_ref[...], tokens, (((1,), (1,)), ((), ())), preferred_element_type=jnp.float32
        )
        best_rows = []
        for page in range(page_total):
            first = firsts[page]
            whole = totals[page] // 16
            rest = totals[page] % 16

            def step(i, carry):
                start = pl.multiple_of(first + i * 16, 16)
                return (
                    jnp.maximum(carry[0], sims_ref[pl.ds(start, 8), :]),
                    jnp.maximum(carry[1], sims_ref[pl.ds(start + 8, 8), :]),
                )

            floor = jnp.full((8, token_block), -2.0, jnp.float32)
            low, high = lax.fori_loop(0, whole, step, (floor, floor))
            start = pl.multiple_of(first + whole * 16, 16)
            low = jnp.maximum(low, jnp.where(sub < rest, sims_ref[pl.ds(start, 8), :], jnp.float32(-2.0)))
            high = jnp.maximum(high, jnp.where(sub + 8 < rest, sims_ref[pl.ds(start + 8, 8), :], jnp.float32(-2.0)))
            best_rows.append(jnp.max(jnp.maximum(low, high), axis=0, keepdims=True))
        best = jnp.concatenate(best_rows, axis=0)
        live = (query_gap == block * (token_block // token_slots)) & slot_live
        return total + jnp.dot(
            best, live.astype(jnp.float32), precision=lax.Precision.HIGH, preferred_element_type=jnp.float32
        )

    blocks = tokens_ref.shape[0] * tokens_ref.shape[1] // token_block
    out_ref[...] = lax.fori_loop(
        0, blocks, block_scores, jnp.zeros((page_total, total_queries), jnp.float32)
    )


def page_scores(received, tokens, table, total_queries, page_total, token_slots, query_rows, capacity):
    owners = received.shape[0]
    width = received.shape[2]
    ordered_rows = owners * capacity + 16 * page_total + 16
    token_total = 2 * tokens.shape[0] * tokens.shape[1]
    token_block = min(token_total, 1024)
    vmem = pl.BlockSpec(memory_space=pltpu.VMEM)
    return pl.pallas_call(
        functools.partial(score_kernel, page_total, token_slots, query_rows, token_block),
        out_shape=jax.ShapeDtypeStruct((page_total, total_queries), jnp.float32),
        in_specs=[pl.BlockSpec(memory_space=pltpu.SMEM), vmem, vmem],
        out_specs=vmem,
        scratch_shapes=[
            pltpu.VMEM((ordered_rows, width), jnp.bfloat16),
            pltpu.VMEM((ordered_rows, token_block), jnp.float32),
            pltpu.VMEM((owners * capacity, width), jnp.bfloat16),
            pltpu.VMEM((owners, 2 * query_rows, width), jnp.bfloat16),
        ],
        cost_estimate=pl.CostEstimate(
            flops=2 * ordered_rows * width * (owners * capacity + token_total),
            bytes_accessed=2 * received.size + 2 * tokens.size + 4 * page_total * total_queries,
            transcendentals=0,
        ),
    )(table, received, tokens)


def shards(patch_rows, owner_ids, page_ids, proj_weight, proj_bias, query_tokens, query_counts):
    owners = lax.axis_size("blk")
    halves = lax.axis_size("inner")
    rows = patch_rows.shape[0]
    capacity = 2 * rows // owners
    per_block = query_tokens.shape[0]
    token_slots = query_tokens.shape[1]
    width = query_tokens.shape[2]
    total_queries = per_block * owners
    half_queries = per_block // halves
    query_rows = half_queries * token_slots
    message = send_message(
        patch_rows, owner_ids, page_ids, proj_weight, proj_bias, query_tokens, query_counts, owners, capacity, halves
    )
    received = lax.all_to_all(message, "blk", split_axis=0, concat_axis=0, tiled=True)
    partner = lax.ppermute(received[:, :query_rows], "inner", [(0, 1), (1, 0)])
    block_at = -(-(query_rows + capacity) // 16) * 16
    combos = -(-owners * PAGES_DEV // 128) * 128
    count_rows = combos // 128
    page_counts = received[:, block_at : block_at + count_rows].reshape(owners, combos)
    page_counts = lax.dynamic_slice_in_dim(page_counts, lax.axis_index("blk") * PAGES_DEV, PAGES_DEV, axis=1)
    counts = received[:, block_at + count_rows, :per_block]
    table = jnp.concatenate([page_counts.reshape(owners * PAGES_DEV), counts.reshape(total_queries)]).astype(jnp.int32)
    return page_scores(received, partner, table, total_queries, PAGES_DEV, token_slots, query_rows, capacity)


def solution(mesh):
    in_specs = (
        P(("groups", "blk", "inner"), None),
        P(("groups", "blk", "inner"), None),
        P(("groups", "blk", "inner")),
        P(),
        P(),
        P(("groups", "blk"), None, None),
        P(("groups", "blk")),
    )
    out_specs = P(("groups", "blk", "inner"), None)
    return jax.shard_map(shards, mesh=mesh, in_specs=in_specs, out_specs=out_specs, check_vma=False)
```
